128 devices in a mesh: seq: 16 (over x_hi, y, core), head: 8 (over x_lo, z).
Axes of the slice: x: 4 (x_hi: 2, x_lo: 2; x = x_hi * 2 + x_lo), y: 4, z: 4, core: 2. Of those that a mesh axis runs over, the one named last changes fastest.
Arguments:
- tokens: bfloat16 [4096, 2048], P('seq'), may hold values from -6 to 6
- norm_gain: float32 [2048], replicated, may hold values from 0.1 to 1.9
- w_query: bfloat16 [2048, 4096], P(None, 'head')
- w_key: bfloat16 [2048, 512], replicated
- w_value: bfloat16 [2048, 512], replicated, may hold values from -0.125 to 0.125
- query_gain: float32 [128], replicated, may hold values from 0.5 to 5.5
- key_gain: float32 [128], replicated, may hold values from 0.5 to 5.5
- w_out: bfloat16 [4096, 2048], P('head'), may hold values from -0.5 to 0.5
- post_gain: float32 [2048], replicated, may hold values from 0.1 to 1.9
- doc_lengths: int32 [6], replicated, may hold values from 1 to 2560, 4096 in all
- expert_ids: int32 [4096, 8], P(('seq', 'head')), may hold values from 0 to 127, all different within a row; in each aligned block of 32 rows (0 to 31, 32 to 63, ...) at most 4 rows name the same one
- route_weights: float32 [4096, 8], P(('seq', 'head')), may hold values from 0.15 to 1
- w_gate: bfloat16 [128, 2048, 768], P(('seq', 'head')), may hold values from -0.125 to 0.125
- w_up: bfloat16 [128, 2048, 768], P(('seq', 'head')), may hold values from -0.125 to 0.125
- w_down: bfloat16 [128, 768, 2048], P(('seq', 'head')), may hold values from -0.21875 to 0.21875
Outputs:
- layer_out: bfloat16 [4096, 2048], P(('seq', 'head'))
The draws below stay inside these ranges and needn't reach their ends.
Inputs may be any that keep to these rules, and one draw needn't show every extreme that they name: `doc_lengths`: 6 document lengths that sum to 4096; the largest is exactly 2560. `expert_ids`: each row names 8 different experts. Among the 32 rows of one device no expert is named more than 4 times; in some devices' rows some expert is named exactly 4 times.
All inputs are finite; a program needn't handle non-finite values.
Results may differ from the reference program's by a relative error of at most 0.015.
The reference program's roundings to bfloat16 on the way count: a program that leaves them out, or rounds other values in their place, can miss the bound.
Values may be sent and summed in bfloat16 or wider, within the bound.
No kernel may reach another device: no remote copies, remote signals or barrier semaphores. Data moves between devices by JAX's collectives and lax.ppermute only.
A program may use at most 128 MiB of HBM per device.

```python
import math
import jax
import jax.numpy as jnp
import numpy as np
from jax import lax

D = 2048
HEADS = 32
KV_HEADS = 4
HEAD_DIM = 128
FF = 768
TOP = 8
NDOCS = 6
SEQLEN = 4096
MOST = 2560
EXPERTS = 128
HEAD_GROUP = 4
ROWS = 32
CAP = 4
N_HEAD = 8
DEVICES = 128


def query_matrix(key):
    raw = jax.random.normal(jax.random.fold_in(key, 11), (D, HEADS * HEAD_DIM), jnp.float32)
    return jnp.clip(raw, -4.0, 4.0) * D ** (-0.5)


def draw_w_query(key, part):
    return query_matrix(key).astype(jnp.bfloat16)


def draw_w_key(key, part):
    raw = jax.random.normal(jax.random.fold_in(key, 12), (D, KV_HEADS * HEAD_DIM), jnp.float32)
    own = jnp.clip(raw, -4.0, 4.0) * D ** (-0.5)
    return own.astype(jnp.bfloat16)


def draw_query_gain(key, part):
    return jax.random.uniform(jax.random.fold_in(key, 13), (HEAD_DIM,), jnp.float32, 1.2, 2.6)


def draw_key_gain(key, part):
    return jax.random.uniform(jax.random.fold_in(key, 14), (HEAD_DIM,), jnp.float32, 1.2, 2.6)


def levels(key, dims, split, low, high):
    factor_of, own = 1.0, jax.random.fold_in(key, 6)
    for dim, blocks in split:
        steps = jnp.exp(jax.random.uniform(jax.random.fold_in(own, dim), (blocks,), jnp.float32, low / len(split), high / len(split)))
        factor_of = factor_of * jnp.repeat(steps, dims[dim] // blocks).reshape([-1 if axis == dim else 1 for axis in range(len(dims))])
    return factor_of


def length_profile(number_of, total, limit, skew):
    portions = [(1 << 20) // math.isqrt(rank ** skew) + 1 for rank in range(2, number_of + 1)]
    rest, given = total - limit - (number_of - 1), [1] * (number_of - 1)
    while rest > 0:
        candidates = [i for i in range(number_of - 1) if given[i] < limit]
        whole, left = sum([portions[i] for i in candidates]), rest
        for i in candidates:
            extra = min(limit - given[i], max(1, left * portions[i] // whole), rest)
            given[i] = given[i] + extra
            rest = rest - extra
    return np.array([limit] + given)


def uneven(rng, number_of, total, limit, lean):
    if number_of == 2:
        one = jax.random.randint(rng, (), max(1, total - limit), min(limit, total - 1) + 1)
        return jnp.stack([one, total - one])
    tallies = jnp.asarray(length_profile(number_of, total, limit, lean), jnp.int32)
    couples = (number_of - 1) // 2
    donor, receiver = tallies[1:1 + 2 * couples:2], tallies[2:2 + 2 * couples:2]
    margin = jnp.minimum(donor - 1, limit - receiver)
    moved = jax.random.randint(jax.random.fold_in(rng, 1), (couples,), 0, 1 << 20) % (margin + 1)
    tallies = tallies.at[1:1 + 2 * couples:2].set(donor - moved).at[2:2 + 2 * couples:2].set(receiver + moved)
    return tallies[jax.random.permutation(jax.random.fold_in(rng, 2), number_of)]


def shared_out(key, own, number, rows, amount, top, bound, slope):
    sequence = jax.random.permutation(key, amount)
    heavy_load, ordinary = portions_of(amount, rows * top, bound, slope, True), portions_of(amount, rows * top, bound, slope, False)
    places = jnp.arange(amount)

    def named(sizes, offset_by):
        used = int((sizes > 0).sum())
        fixed = max(1, used // 4)
        shifted = fixed + (places - fixed + offset_by * (used - fixed)) % max(1, amount - fixed)
        return jnp.zeros((amount,), jnp.int32).at[sequence[jnp.where(places < fixed, places, shifted)]].set(jnp.asarray(sizes, jnp.int32))

    sizes = jnp.where(number % 4 == 0, named(heavy_load, number // 4), named(ordinary, number - number // 4 - 1))
    mixed = jax.random.permutation(jax.random.fold_in(own, 3), amount)
    source_of, sink = mixed[0:amount // 2 * 2:2], mixed[1:amount // 2 * 2:2]
    slack = jnp.minimum(sizes[source_of] - 1, bound - sizes[sink]) // 2
    slack = jnp.where((source_of == sequence[0]) | (sink == sequence[0]) | (sizes[sink] == 0), 0, jnp.maximum(slack, 0))
    shifted = jax.random.randint(jax.random.fold_in(own, 4), (amount // 2,), 0, 1 << 20) % (slack + 1)
    sizes = sizes.at[source_of].add(-shifted).at[sink].add(shifted)
    items = jnp.searchsorted(jnp.cumsum(sizes), jnp.arange(rows * top), side="right").astype(jnp.int32)
    table = items.reshape(top, rows).T
    table = table[jax.random.permutation(jax.random.fold_in(own, 1), rows)]
    offset_by = jax.random.randint(jax.random.fold_in(own, 2), (rows, 1), 0, top)
    return jnp.take_along_axis(table, (jnp.arange(top)[None, :] + offset_by) % top, axis=1)


def portions_of(amount, total, reach, skew, full):
    loads = [(1 << 20) // math.isqrt(rank ** skew) + 1 for rank in range(1, amount + 1)]
    largest = reach if full else min(reach, max(-(-total // amount), total * loads[0] // sum(loads)))
    least = 1 if total - largest >= amount - 1 else 0
    holding, rest = [largest] + [least] * (amount - 1), total - largest - least * (amount - 1)
    while rest > 0:
        free = [i for i in range(1, amount) if holding[i] < largest] or [i for i in range(1, amount) if holding[i] < reach]
        pool, left = sum([loads[i] for i in free]), rest
        for i in free:
            more = min(reach - holding[i], max(1, left * loads[i] // pool), rest)
            holding[i] = holding[i] + more
            rest = rest - more
    return np.array(holding)


def centred(rng, dims, width, bound, cuts=(), kind=jnp.bfloat16):
    values = jax.random.normal(rng, dims, jnp.float32) * width
    if len(cuts) > 0:
        values = levels(rng, dims, cuts, -0.22, 0.18) * values
    return jnp.clip(values, min=-bound, max=bound).astype(kind)


def setup_inputs(seed: int = 0) -> dict:
    streams_of = jax.random.split(jax.random.key(seed), 16)
    tokens = centred(streams_of[0], (SEQLEN, D), 1.0, 6.0, ((0, 16),))
    norm_gain = jnp.clip(1.0 + 0.18 * jax.random.normal(streams_of[1], (D,), jnp.float32), 0.1, 1.9)
    w_query = draw_w_query(jax.random.fold_in(streams_of[15], 71), 0)
    w_key = draw_w_key(jax.random.fold_in(streams_of[15], 71), 0)
    w_value = centred(streams_of[4], (D, KV_HEADS * HEAD_DIM), D ** -0.5, 0.125)
    query_gain = draw_query_gain(jax.random.fold_in(streams_of[15], 71), 0)
    key_gain = draw_key_gain(jax.random.fold_in(streams_of[15], 71), 0)
    w_out = centred(streams_of[7], (HEADS * HEAD_DIM, D), HEAD_DIM ** -0.5, 0.5, ((0, 8),))
    post_gain = jnp.clip(1.0 + 0.18 * jax.random.normal(streams_of[8], (D,), jnp.float32), 0.1, 1.9)
    doc_lengths = uneven(streams_of[9], NDOCS, SEQLEN, MOST, 2).astype(jnp.int32)
    expert_ids_keys = jax.random.split(jax.random.fold_in(streams_of[10], 1), SEQLEN // ROWS)
    expert_ids_turns = jax.random.permutation(jax.random.fold_in(streams_of[10], 3), SEQLEN // ROWS)
    expert_ids = jax.vmap(lambda own, number: shared_out(jax.random.fold_in(streams_of[10], 2), own, number, ROWS, EXPERTS, TOP, CAP, 2))(expert_ids_keys, expert_ids_turns).reshape((SEQLEN, TOP))
    route_weights = jnp.clip(0.15 + 0.85 * jax.random.uniform(streams_of[11], (SEQLEN, TOP), jnp.float32) ** levels(streams_of[11], (SEQLEN, TOP), ((0, 128),), -0.2, 0.2), 0.15, 1.0)
    w_gate = centred(streams_of[12], (EXPERTS, D, FF), D ** -0.5, 0.125, ((0, 128),))
    w_up = centred(streams_of[13], (EXPERTS, D, FF), D ** -0.5, 0.125, ((0, 128),))
    w_down = centred(streams_of[14], (EXPERTS, FF, D), FF ** -0.5, 0.21875, ((0, 128),))
    return dict(tokens=tokens, norm_gain=norm_gain, w_query=w_query, w_key=w_key, w_value=w_value, query_gain=query_gain, key_gain=key_gain, w_out=w_out, post_gain=post_gain, doc_lengths=doc_lengths, expert_ids=expert_ids, route_weights=route_weights, w_gate=w_gate, w_up=w_up, w_down=w_down)


EPSILON = 1e-06
THETA = 1000000.0
FLOOR = -1e+30

def rms_scale(values, gain):
    return values * lax.rsqrt(lax.optimization_barrier(jnp.mean(values * values, axis=-1, keepdims=True)) + EPSILON) * gain

def rotate(values, cosine, sine):
    half = values.shape[-1] // 2
    first = values[..., :half]
    second = values[..., half:]
    return jnp.concatenate([first * cosine - second * sine, second * cosine + first * sine], axis=-1)

def doc_index(positions, ends):
    return lax.optimization_barrier(jnp.sum((positions[:, None] >= ends[None, :]).astype(jnp.int32), axis=1))

def reference(tokens, norm_gain, w_query, w_key, w_value, query_gain, key_gain, w_out, post_gain, doc_lengths, expert_ids, route_weights, w_gate, w_up, w_down):
    inputs = tokens.astype(jnp.float32)
    normed = rms_scale(inputs, norm_gain).astype(jnp.bfloat16)
    ends = jnp.cumsum(doc_lengths).astype(jnp.int32)
    starts = ends - doc_lengths
    positions = jnp.arange(SEQLEN, dtype=jnp.int32)
    query_doc = doc_index(positions, ends)
    offset = (positions - starts[query_doc]).astype(jnp.float32)
    half = HEAD_DIM // 2
    inverse = THETA ** (-2.0 * jnp.arange(half, dtype=jnp.float32) / HEAD_DIM)
    angles = offset[:, None] * inverse[None, :]
    cosine = jnp.cos(angles)[:, None, :]
    sine = jnp.sin(angles)[:, None, :]
    queries = jnp.dot(normed, w_query, preferred_element_type=jnp.float32).reshape(SEQLEN, HEADS, HEAD_DIM)
    queries = rotate(rms_scale(queries, query_gain), cosine, sine).astype(jnp.bfloat16)
    keys = jnp.dot(normed, w_key, preferred_element_type=jnp.float32).reshape(SEQLEN, KV_HEADS, HEAD_DIM)
    keys = rotate(rms_scale(keys, key_gain), cosine, sine).astype(jnp.bfloat16)
    values = jnp.dot(normed, w_value, preferred_element_type=jnp.float32).astype(jnp.bfloat16).reshape(SEQLEN, KV_HEADS, HEAD_DIM)
    block = math.gcd(512, SEQLEN)
    nblocks = SEQLEN // block
    scale = HEAD_DIM ** (-0.5)
    group = HEADS // KV_HEADS

    def one_head(head):
        q_head = lax.dynamic_index_in_dim(queries, head, 1, keepdims=False)
        k_head = lax.dynamic_index_in_dim(keys, head // group, 1, keepdims=False)
        v_head = lax.dynamic_index_in_dim(values, head // group, 1, keepdims=False)

        def one_block(index):
            begin = (index * block).astype(jnp.int32)
            q_block = lax.dynamic_slice_in_dim(q_head, begin, block, 0)
            q_pos = begin + jnp.arange(block, dtype=jnp.int32)
            q_doc = lax.dynamic_slice_in_dim(query_doc, begin, block, 0)
            scores = jnp.dot(q_block, k_head.T, preferred_element_type=jnp.float32) * scale
            allowed = (query_doc[None, :] == q_doc[:, None]) & (positions[None, :] <= q_pos[:, None])
            scores = jnp.where(allowed, scores, FLOOR)
            high = lax.optimization_barrier(jnp.max(scores, axis=1, keepdims=True))
            weights = jnp.where(allowed, jnp.exp(scores - high), 0.0)
            total = lax.optimization_barrier(jnp.sum(weights, axis=1, keepdims=True))
            return jnp.dot(weights.astype(jnp.bfloat16), v_head, preferred_element_type=jnp.float32) / total
        result = lax.map(one_block, jnp.arange(nblocks, dtype=jnp.int32))
        return result.reshape(SEQLEN, HEAD_DIM).astype(jnp.bfloat16)
    heads_out = lax.map(one_head, jnp.arange(HEADS, dtype=jnp.int32))
    attended = jnp.transpose(heads_out, (1, 0, 2)).reshape(SEQLEN, HEADS * HEAD_DIM)
    group_width = HEAD_GROUP * HEAD_DIM

    def add_group(total, index):
        begin = (index * group_width).astype(jnp.int32)
        left = lax.dynamic_slice_in_dim(attended, begin, group_width, 1)
        right = lax.dynamic_slice_in_dim(w_out, begin, group_width, 0)
        term = jnp.dot(left, right, preferred_element_type=jnp.float32)
        term = lax.optimization_barrier(term.astype(jnp.bfloat16)).astype(jnp.float32)
        return (total + term, None)
    attn = lax.scan(add_group, jnp.zeros((SEQLEN, D), jnp.float32), jnp.arange(N_HEAD, dtype=jnp.int32))[0]
    resid = inputs + attn
    routed = rms_scale(resid, post_gain).astype(jnp.bfloat16)
    assigned = ROWS * TOP
    chosen = expert_ids.reshape(DEVICES, assigned)
    hits = (chosen[:, :, None] == jnp.arange(EXPERTS, dtype=jnp.int32)[None, None, :]).astype(jnp.int32)
    rank = lax.optimization_barrier(jnp.sum((jnp.cumsum(hits, axis=1) - hits) * hits, axis=2))
    owner = (jnp.arange(DEVICES * assigned, dtype=jnp.int32) // TOP).reshape(DEVICES, assigned)
    slot_col = jnp.arange(DEVICES, dtype=jnp.int32)[:, None] * CAP + rank
    table = jnp.full((EXPERTS, DEVICES * CAP), SEQLEN, jnp.int32).at[chosen, slot_col].set(owner)
    weight_table = jnp.zeros((EXPERTS, DEVICES * CAP), jnp.float32).at[chosen, slot_col].set(route_weights.reshape(DEVICES, assigned))
    padded = jnp.concatenate([routed, jnp.zeros((1, D), jnp.bfloat16)], axis=0)

    def per_expert(total, expert):
        index = table[expert]
        rows = padded[index]
        gate = jnp.dot(rows, w_gate[expert], preferred_element_type=jnp.float32)
        up = jnp.dot(rows, w_up[expert], preferred_element_type=jnp.float32)
        hidden = (jax.nn.silu(gate) * up).astype(jnp.bfloat16)
        result = jnp.dot(hidden, w_down[expert], preferred_element_type=jnp.float32).astype(jnp.bfloat16)
        return (total.at[index].add(weight_table[expert][:, None] * result.astype(jnp.float32)), None)
    mixture = lax.scan(per_expert, jnp.zeros((SEQLEN + 1, D), jnp.float32), jnp.arange(EXPERTS, dtype=jnp.int32))[0][:SEQLEN]
    return (resid + mixture).astype(jnp.bfloat16)
```

```python
import math

import jax
import jax.numpy as jnp
from jax import lax
from jax.sharding import PartitionSpec as P

HEADS = 32
KV_HEADS = 4
TOP = 8


EPSILON = 1e-06
THETA = 1000000.0
FLOOR = -1e30


def rms_scale(values, gain):
    return values * lax.rsqrt(jnp.mean(values * values, axis=-1, keepdims=True) + EPSILON) * gain


def rotate(values, cosine, sine):
    half = values.shape[-1] // 2
    first = values[..., :half]
    second = values[..., half:]
    return jnp.concatenate(
        [first * cosine - second * sine, second * cosine + first * sine], axis=-1
    )


def doc_index(positions, ends):
    return jnp.sum((positions[:, None] >= ends[None, :]).astype(jnp.int32), axis=1)


def local(
    tokens,
    norm_gain,
    w_query,
    w_key,
    w_value,
    query_gain,
    key_gain,
    w_out,
    post_gain,
    doc_lengths,
    expert_ids,
    route_weights,
    w_gate,
    w_up,
    w_down,
):
    tok_dev, width = tokens.shape
    head_dim = query_gain.shape[0]
    per_dev = w_query.shape[1] // head_dim
    n_seq = lax.axis_size("seq")
    n_head = lax.axis_size("head")
    seq_index = lax.axis_index("seq")
    head_index = lax.axis_index("head")
    ndocs = doc_lengths.shape[0]
    ends = jnp.cumsum(doc_lengths)
    starts = ends - doc_lengths
    positions = seq_index * tok_dev + jnp.arange(tok_dev, dtype=jnp.int32)
    query_doc = doc_index(positions, ends)
    matches = query_doc[:, None] == jnp.arange(ndocs, dtype=jnp.int32)[None, :]
    own_start = jnp.sum(jnp.where(matches, starts[None, :], 0), axis=1)
    offset = (positions - own_start).astype(jnp.float32)
    half = head_dim // 2
    inverse = THETA ** (-2.0 * jnp.arange(half, dtype=jnp.float32) / head_dim)
    angles = offset[:, None] * inverse[None, :]
    cosine = jnp.cos(angles)
    sine = jnp.sin(angles)
    inputs = tokens.astype(jnp.float32)
    normed = rms_scale(inputs, norm_gain).astype(jnp.bfloat16)
    queries = jnp.dot(normed, w_query, preferred_element_type=jnp.float32).reshape(
        tok_dev, per_dev, head_dim
    )
    queries = rotate(rms_scale(queries, query_gain), cosine[:, None, :], sine[:, None, :]).astype(
        jnp.bfloat16
    )
    column = head_index * per_dev // (HEADS // KV_HEADS) * head_dim
    key_cols = lax.dynamic_slice_in_dim(w_key, column, head_dim, 1)
    value_cols = lax.dynamic_slice_in_dim(w_value, column, head_dim, 1)
    keys = rotate(
        rms_scale(jnp.dot(normed, key_cols, preferred_element_type=jnp.float32), key_gain),
        cosine,
        sine,
    ).astype(jnp.bfloat16)
    values = jnp.dot(normed, value_cols, preferred_element_type=jnp.float32).astype(jnp.bfloat16)
    stacked = jnp.stack([keys, values])
    scale = head_dim ** (-0.5)
    last_query = positions[-1]
    first_start = own_start[0]

    def attend(state, block, key_start):
        count = block.shape[1]
        key_pos = key_start + jnp.arange(count, dtype=jnp.int32)

        def update(carry):
            high, total, accum = carry
            key_doc = doc_index(key_pos, ends)
            allowed = (
                (key_doc[None, :] == query_doc[:, None])
                & (key_pos[None, :] <= positions[:, None])
                & (key_pos[None, :] >= 0)
            )
            scores = (
                jnp.einsum("qhd,kd->hqk", queries, block[0], preferred_element_type=jnp.float32)
                * scale
            )
            scores = jnp.where(allowed[None], scores, FLOOR)
            new_high = jnp.maximum(high, jnp.max(scores, axis=2))
            weights = jnp.where(allowed[None], jnp.exp(scores - new_high[:, :, None]), 0.0)
            factor = jnp.exp(high - new_high)
            total = total * factor + jnp.sum(weights, axis=2)
            accum = accum * jnp.transpose(factor)[:, :, None] + jnp.einsum(
                "hqk,kd->qhd",
                weights.astype(jnp.bfloat16),
                block[1],
                preferred_element_type=jnp.float32,
            )
            return (new_high, total, accum)

        needed = (key_start <= last_query) & (key_start + count - 1 >= first_start)
        return lax.cond(needed, update, lambda carry: carry, state)

    initial = (
        jnp.full((per_dev, tok_dev), FLOOR, jnp.float32),
        jnp.zeros((per_dev, tok_dev), jnp.float32),
        jnp.zeros((tok_dev, per_dev, head_dim), jnp.float32),
    )
    spread = jnp.broadcast_to(stacked[:, None], (2, n_seq) + stacked.shape[1:])
    piece = lax.all_to_all(spread, "seq", 1, 1, tiled=True).reshape(2, n_seq * tok_dev, head_dim)
    count = piece.shape[1]
    step = math.gcd(count, tok_dev * max(1, 512 // tok_dev))

    def inner(index, carry):
        block = lax.dynamic_slice_in_dim(piece, index * step, step, 1)
        return attend(carry, block, index * step)

    state = lax.fori_loop(0, count // step, inner, initial)
    high, total, accum = state
    attended = (
        (accum / jnp.transpose(total)[:, :, None])
        .astype(jnp.bfloat16)
        .reshape(tok_dev, per_dev * head_dim)
    )
    rows = tok_dev // n_head
    terms = jnp.dot(attended, w_out, preferred_element_type=jnp.float32).astype(jnp.bfloat16)
    terms = lax.all_to_all(terms.reshape(n_head, rows, width), "head", 0, 0, tiled=True)
    attn_rows = jnp.sum(terms.astype(jnp.float32), axis=0)
    resid = lax.dynamic_slice_in_dim(inputs, head_index * rows, rows, 0) + attn_rows
    routed = rms_scale(resid, post_gain).astype(jnp.bfloat16)
    experts = n_seq * n_head * w_gate.shape[0]
    capacity = 2 * TOP * rows // experts
    chosen = expert_ids.reshape(-1)
    hits = (chosen[:, None] == jnp.arange(experts, dtype=jnp.int32)[None, :]).astype(jnp.int32)
    rank = jnp.sum((jnp.cumsum(hits, axis=0) - hits) * hits, axis=1)
    target = chosen * capacity + rank
    outgoing = (
        jnp.zeros((experts * capacity, width), jnp.bfloat16)
        .at[target]
        .set(jnp.repeat(routed, TOP, axis=0))
    )
    flat = lax.all_to_all(outgoing, ("seq", "head"), split_axis=0, concat_axis=0, tiled=True)
    gate = jnp.dot(flat, w_gate[0], preferred_element_type=jnp.float32)
    up = jnp.dot(flat, w_up[0], preferred_element_type=jnp.float32)
    hidden = (jax.nn.silu(gate) * up).astype(jnp.bfloat16)
    returned = lax.all_to_all(
        jnp.dot(hidden, w_down[0], preferred_element_type=jnp.float32)
        .astype(jnp.bfloat16),
        ("seq", "head"),
        split_axis=0,
        concat_axis=0,
        tiled=True,
    )
    picked = returned.reshape(experts * capacity, width)[target].reshape(rows, TOP, width)
    combined = jnp.sum(picked.astype(jnp.float32) * route_weights[:, :, None], axis=1)
    return (resid + combined).astype(jnp.bfloat16)


def solution(mesh):
    placed = (
        P("seq", None),
        P(),
        P(None, "head"),
        P(),
        P(),
        P(),
        P(),
        P("head", None),
        P(),
        P(),
        P(("seq", "head"), None),
        P(("seq", "head"), None),
        P(("seq", "head"), None, None),
        P(("seq", "head"), None, None),
        P(("seq", "head"), None, None),
    )
    return jax.shard_map(
        local, mesh=mesh, in_specs=placed, out_specs=P(("seq", "head"), None), check_vma=False
    )
```

```python
import functools
import math

import jax
import jax.numpy as jnp
from jax import lax
from jax.experimental import pallas as pl
from jax.experimental.pallas import tpu as pltpu
from jax.sharding import PartitionSpec as P

HEADS = 32
KV_HEADS = 4
TOP = 8


EPSILON = 1e-06
THETA = 1000000.0
FLOOR = -1e30


def rms_scale(values, gain):
    return values * lax.rsqrt(jnp.mean(values * values, axis=-1, keepdims=True) + EPSILON) * gain


def rotate(values, cosine, sine):
    half = values.shape[-1] // 2
    first = values[..., :half]
    second = values[..., half:]
    return jnp.concatenate(
        [first * cosine - second * sine, second * cosine + first * sine], axis=-1
    )


def doc_index(positions, ends):
    return jnp.sum((positions[:, None] >= ends[None, :]).astype(jnp.int32), axis=1)


def _attend_kernel(bounds_ref, q_ref, kv_ref, qpos_ref, qstart_ref, o_ref, *, block, scale):
    q = q_ref[...]
    qpos = qpos_ref[...]
    qstart = qstart_ref[...]
    rows, width = q.shape

    def body(j, carry):
        high, total, accum = carry
        base = pl.multiple_of((bounds_ref[0] + j) * block, block)
        keys = kv_ref[0, pl.ds(base, block), :]
        values = kv_ref[1, pl.ds(base, block), :]
        scores = lax.dot_general(q, keys, (((1,), (1,)), ((), ())), preferred_element_type=jnp.float32) * scale
        key_pos = base + lax.broadcasted_iota(jnp.int32, (1, block), 1)
        allowed = (key_pos >= qstart) & (key_pos <= qpos)
        scores = jnp.where(allowed, scores, FLOOR)
        new_high = jnp.maximum(high, jnp.max(scores, axis=1, keepdims=True))
        weights = jnp.where(allowed, jnp.exp(scores - new_high), 0.0)
        factor = jnp.exp(high - new_high)
        total = total * factor + jnp.sum(weights, axis=1, keepdims=True)
        accum = accum * factor + jnp.dot(weights.astype(jnp.bfloat16), values, preferred_element_type=jnp.float32)
        return new_high, total, accum

    initial = (
        jnp.full((rows, 1), FLOOR, jnp.float32),
        jnp.zeros((rows, 1), jnp.float32),
        jnp.zeros((rows, width), jnp.float32),
    )
    high, total, accum = lax.fori_loop(0, bounds_ref[1], body, initial)
    o_ref[...] = (accum / total).astype(o_ref.dtype)

def attend(bounds, queries, kv, qpos, qstart, block):
    tok, heads, dim = queries.shape
    kernel = functools.partial(_attend_kernel, block=block, scale=dim ** (-0.5))
    spec = pltpu.PrefetchScalarGridSpec(
        num_scalar_prefetch=1,
        grid=(heads,),
        in_specs=[
            pl.BlockSpec((tok, dim), lambda h, b: (0, h)),
            pl.BlockSpec(kv.shape, lambda h, b: (0, 0, 0)),
            pl.BlockSpec((tok, 1), lambda h, b: (0, 0)),
            pl.BlockSpec((tok, 1), lambda h, b: (0, 0)),
        ],
        out_specs=pl.BlockSpec((tok, dim), lambda h, b: (0, h)),
    )
    return pl.pallas_call(
        kernel, grid_spec=spec, out_shape=jax.ShapeDtypeStruct((tok, heads * dim), jnp.bfloat16),
    )(bounds, queries.reshape(tok, heads * dim), kv, qpos, qstart)


def local(
    tokens,
    norm_gain,
    w_query,
    w_key,
    w_value,
    query_gain,
    key_gain,
    w_out,
    post_gain,
    doc_lengths,
    expert_ids,
    route_weights,
    w_gate,
    w_up,
    w_down,
):
    tok_dev, width = tokens.shape
    head_dim = query_gain.shape[0]
    per_dev = w_query.shape[1] // head_dim
    n_seq = lax.axis_size("seq")
    n_head = lax.axis_size("head")
    seq_index = lax.axis_index("seq")
    head_index = lax.axis_index("head")
    ndocs = doc_lengths.shape[0]
    ends = jnp.cumsum(doc_lengths)
    starts = ends - doc_lengths
    positions = seq_index * tok_dev + jnp.arange(tok_dev, dtype=jnp.int32)
    query_doc = doc_index(positions, ends)
    matches = query_doc[:, None] == jnp.arange(ndocs, dtype=jnp.int32)[None, :]
    own_start = jnp.sum(jnp.where(matches, starts[None, :], 0), axis=1)
    offset = (positions - own_start).astype(jnp.float32)
    half = head_dim // 2
    inverse = THETA ** (-2.0 * jnp.arange(half, dtype=jnp.float32) / head_dim)
    angles = offset[:, None] * inverse[None, :]
    cosine = jnp.cos(angles)
    sine = jnp.sin(angles)
    inputs = tokens.astype(jnp.float32)
    normed = rms_scale(inputs, norm_gain).astype(jnp.bfloat16)
    queries = jnp.dot(normed, w_query, preferred_element_type=jnp.float32).reshape(
        tok_dev, per_dev, head_dim
    )
    queries = rotate(rms_scale(queries, query_gain), cosine[:, None, :], sine[:, None, :]).astype(
        jnp.bfloat16
    )
    column = head_index * per_dev // (HEADS // KV_HEADS) * head_dim
    key_cols = lax.dynamic_slice_in_dim(w_key, column, head_dim, 1)
    value_cols = lax.dynamic_slice_in_dim(w_value, column, head_dim, 1)
    keys = rotate(
        rms_scale(jnp.dot(normed, key_cols, preferred_element_type=jnp.float32), key_gain),
        cosine,
        sine,
    ).astype(jnp.bfloat16)
    values = jnp.dot(normed, value_cols, preferred_element_type=jnp.float32).astype(jnp.bfloat16)
    stacked = jnp.stack([keys, values])
    spread = jnp.broadcast_to(stacked[:, None], (2, n_seq) + stacked.shape[1:])
    piece = lax.all_to_all(spread, "seq", 1, 1, tiled=True).reshape(2, n_seq * tok_dev, head_dim)
    block = tok_dev
    low = own_start[0] // block
    bounds = jnp.stack([low, positions[-1] // block - low + 1]).astype(jnp.int32)
    attended = attend(bounds, queries, piece, positions[:, None], own_start[:, None], block)
    rows = tok_dev // n_head
    terms = jnp.dot(attended, w_out, preferred_element_type=jnp.float32).astype(jnp.bfloat16)
    terms = lax.all_to_all(terms.reshape(n_head, rows, width), "head", 0, 0, tiled=True)
    attn_rows = jnp.sum(terms.astype(jnp.float32), axis=0)
    resid = lax.dynamic_slice_in_dim(inputs, head_index * rows, rows, 0) + attn_rows
    routed = rms_scale(resid, post_gain).astype(jnp.bfloat16)
    experts = n_seq * n_head * w_gate.shape[0]
    capacity = 2 * TOP * rows // experts
    chosen = expert_ids.reshape(-1)
    hits = (chosen[:, None] == jnp.arange(experts, dtype=jnp.int32)[None, :]).astype(jnp.int32)
    rank = jnp.sum((jnp.cumsum(hits, axis=0) - hits) * hits, axis=1)
    target = chosen * capacity + rank
    outgoing = (
        jnp.zeros((experts * capacity, width), jnp.bfloat16)
        .at[target]
        .set(jnp.repeat(routed, TOP, axis=0))
    )
    flat = lax.all_to_all(outgoing, ("seq", "head"), split_axis=0, concat_axis=0, tiled=True)
    gate = jnp.dot(flat, w_gate[0], preferred_element_type=jnp.float32)
    up = jnp.dot(flat, w_up[0], preferred_element_type=jnp.float32)
    hidden = (jax.nn.silu(gate) * up).astype(jnp.bfloat16)
    returned = lax.all_to_all(
        jnp.dot(hidden, w_down[0], preferred_element_type=jnp.float32)
        .astype(jnp.bfloat16),
        ("seq", "head"),
        split_axis=0,
        concat_axis=0,
        tiled=True,
    )
    picked = returned.reshape(experts * capacity, width)[target].reshape(rows, TOP, width)
    combined = jnp.sum(picked.astype(jnp.float32) * route_weights[:, :, None], axis=1)
    return (resid + combined).astype(jnp.bfloat16)


def solution(mesh):
    placed = (
        P("seq", None),
        P(),
        P(None, "head"),
        P(),
        P(),
        P(),
        P(),
        P("head", None),
        P(),
        P(),
        P(("seq", "head"), None),
        P(("seq", "head"), None),
        P(("seq", "head"), None, None),
        P(("seq", "head"), None, None),
        P(("seq", "head"), None, None),
    )
    return jax.shard_map(
        local, mesh=mesh, in_specs=placed, out_specs=P(("seq", "head"), None), check_vma=False
    )
```

```python
import functools
import math

import jax
import jax.numpy as jnp
from jax import lax
from jax.experimental import pallas as pl
from jax.experimental.pallas import tpu as pltpu
from jax.sharding import PartitionSpec as P

HEADS = 32
KV_HEADS = 4
TOP = 8


EPSILON = 1e-06
THETA = 1000000.0
FLOOR = -1e30


def rms_scale(values, gain):
    return values * lax.rsqrt(jnp.mean(values * values, axis=-1, keepdims=True) + EPSILON) * gain


def rotate(values, cosine, sine):
    half = values.shape[-1] // 2
    first = values[..., :half]
    second = values[..., half:]
    return jnp.concatenate(
        [first * cosine - second * sine, second * cosine + first * sine], axis=-1
    )


def doc_index(positions, ends):
    return jnp.sum((positions[:, None] >= ends[None, :]).astype(jnp.int32), axis=1)


def _attend_kernel(bounds_ref, q_ref, kv_ref, qpos_ref, qstart_ref, o_ref, *, block, scale):
    q = q_ref[...]
    qpos = qpos_ref[...]
    qstart = qstart_ref[...]
    rows, width = q.shape

    def body(j, carry):
        high, total, accum = carry
        base = pl.multiple_of((bounds_ref[0] + j) * block, block)
        keys = kv_ref[0, pl.ds(base, block), :]
        values = kv_ref[1, pl.ds(base, block), :]
        scores = lax.dot_general(q, keys, (((1,), (1,)), ((), ())), preferred_element_type=jnp.float32) * scale
        key_pos = base + lax.broadcasted_iota(jnp.int32, (1, block), 1)
        allowed = (key_pos >= qstart) & (key_pos <= qpos)
        scores = jnp.where(allowed, scores, FLOOR)
        new_high = jnp.maximum(high, jnp.max(scores, axis=1, keepdims=True))
        weights = jnp.where(allowed, jnp.exp(scores - new_high), 0.0)
        factor = jnp.exp(high - new_high)
        total = total * factor + jnp.sum(weights, axis=1, keepdims=True)
        accum = accum * factor + jnp.dot(weights.astype(jnp.bfloat16), values, preferred_element_type=jnp.float32)
        return new_high, total, accum

    initial = (
        jnp.full((rows, 1), FLOOR, jnp.float32),
        jnp.zeros((rows, 1), jnp.float32),
        jnp.zeros((rows, width), jnp.float32),
    )
    high, total, accum = lax.fori_loop(0, bounds_ref[1], body, initial)
    o_ref[...] = (accum / total).astype(o_ref.dtype)

def attend(bounds, queries, kv, qpos, qstart, block):
    tok, heads, dim = queries.shape
    kernel = functools.partial(_attend_kernel, block=block, scale=dim ** (-0.5))
    spec = pltpu.PrefetchScalarGridSpec(
        num_scalar_prefetch=1,
        grid=(heads,),
        in_specs=[
            pl.BlockSpec((tok, dim), lambda h, b: (0, h)),
            pl.BlockSpec(kv.shape, lambda h, b: (0, 0, 0)),
            pl.BlockSpec((tok, 1), lambda h, b: (0, 0)),
            pl.BlockSpec((tok, 1), lambda h, b: (0, 0)),
        ],
        out_specs=pl.BlockSpec((tok, dim), lambda h, b: (0, h)),
    )
    return pl.pallas_call(
        kernel, grid_spec=spec, out_shape=jax.ShapeDtypeStruct((tok, heads * dim), jnp.bfloat16),
    )(bounds, queries.reshape(tok, heads * dim), kv, qpos, qstart)


def local(
    tokens,
    norm_gain,
    w_query,
    w_key,
    w_value,
    query_gain,
    key_gain,
    w_out,
    post_gain,
    doc_lengths,
    expert_ids,
    route_weights,
    w_gate,
    w_up,
    w_down,
):
    tok_dev, width = tokens.shape
    head_dim = query_gain.shape[0]
    per_dev = w_query.shape[1] // head_dim
    n_seq = lax.axis_size("seq")
    n_head = lax.axis_size("head")
    seq_index = lax.axis_index("seq")
    head_index = lax.axis_index("head")
    ndocs = doc_lengths.shape[0]
    ends = jnp.cumsum(doc_lengths)
    starts = ends - doc_lengths
    positions = seq_index * tok_dev + jnp.arange(tok_dev, dtype=jnp.int32)
    query_doc = doc_index(positions, ends)
    matches = query_doc[:, None] == jnp.arange(ndocs, dtype=jnp.int32)[None, :]
    own_start = jnp.sum(jnp.where(matches, starts[None, :], 0), axis=1)
    offset = (positions - own_start).astype(jnp.float32)
    half = head_dim // 2
    inverse = THETA ** (-2.0 * jnp.arange(half, dtype=jnp.float32) / head_dim)
    angles = offset[:, None] * inverse[None, :]
    cosine = jnp.cos(angles)
    sine = jnp.sin(angles)
    inputs = tokens.astype(jnp.float32)
    normed = rms_scale(inputs, norm_gain).astype(jnp.bfloat16)
    queries = jnp.dot(normed, w_query, preferred_element_type=jnp.float32).reshape(
        tok_dev, per_dev, head_dim
    )
    queries = rotate(rms_scale(queries, query_gain), cosine[:, None, :], sine[:, None, :]).astype(
        jnp.bfloat16
    )
    column = head_index * per_dev // (HEADS // KV_HEADS) * head_dim
    key_cols = lax.dynamic_slice_in_dim(w_key, column, head_dim, 1)
    value_cols = lax.dynamic_slice_in_dim(w_value, column, head_dim, 1)
    keys = rotate(
        rms_scale(jnp.dot(normed, key_cols, preferred_element_type=jnp.float32), key_gain),
        cosine,
        sine,
    ).astype(jnp.bfloat16)
    values = jnp.dot(normed, value_cols, preferred_element_type=jnp.float32).astype(jnp.bfloat16)
    stacked = jnp.stack([keys, values])
    spread = jnp.broadcast_to(stacked[:, None], (2, n_seq) + stacked.shape[1:])
    piece = lax.all_to_all(spread, "seq", 1, 1, tiled=True).reshape(2, n_seq * tok_dev, head_dim)
    block = tok_dev
    low = own_start[0] // block
    bounds = jnp.stack([low, positions[-1] // block - low + 1]).astype(jnp.int32)
    attended = attend(bounds, queries, piece, positions[:, None], own_start[:, None], block)
    rows = tok_dev // n_head
    terms = jnp.dot(attended, w_out, preferred_element_type=jnp.float32).astype(jnp.bfloat16)
    terms = lax.all_to_all(terms.reshape(n_head, rows, width), "head", 0, 0, tiled=True)
    attn_rows = jnp.sum(terms.astype(jnp.float32), axis=0)
    resid = lax.dynamic_slice_in_dim(tokens, head_index * rows, rows, 0).astype(jnp.float32) + attn_rows
    routed = rms_scale(resid, post_gain).astype(jnp.bfloat16)
    experts = n_seq * n_head * w_gate.shape[0]
    capacity = 2 * TOP * rows // experts
    chosen = expert_ids.reshape(-1)
    hits = (chosen[:, None] == jnp.arange(experts, dtype=jnp.int32)[None, :]).astype(jnp.int32)
    rank = jnp.sum((jnp.cumsum(hits, axis=0) - hits) * hits, axis=1)
    slot = rank * experts + chosen
    select = (slot[:, None] == jnp.arange(capacity * experts, dtype=jnp.int32)[None, :]).reshape(
        rows, TOP, capacity * experts
    )
    sources = jnp.transpose(jnp.any(select, axis=1)).astype(jnp.bfloat16)
    outgoing = jnp.dot(sources, routed, preferred_element_type=jnp.float32).astype(jnp.bfloat16)
    outgoing = outgoing.reshape(capacity, experts, width)
    block = lax.all_to_all(outgoing, ("seq", "head"), split_axis=1, concat_axis=1, tiled=True)
    flat = block.reshape(-1, width)
    gate = jnp.dot(flat, w_gate[0], preferred_element_type=jnp.float32)
    up = jnp.dot(flat, w_up[0], preferred_element_type=jnp.float32)
    hidden = (jax.nn.silu(gate) * up).astype(jnp.bfloat16)
    returned = lax.all_to_all(
        jnp.dot(hidden, w_down[0], preferred_element_type=jnp.float32)
        .astype(jnp.bfloat16)
        .reshape(block.shape),
        ("seq", "head"),
        split_axis=1,
        concat_axis=1,
        tiled=True,
    ).reshape(-1, width)
    mixing = jnp.sum(jnp.where(select, route_weights[:, :, None], 0.0), axis=1)
    combined = jnp.dot(
        mixing, returned.astype(jnp.float32), precision=lax.Precision.HIGHEST,
        preferred_element_type=jnp.float32,
    )
    return (resid + combined).astype(jnp.bfloat16)


def solution(mesh):
    placed = (
        P("seq", None),
        P(),
        P(None, "head"),
        P(),
        P(),
        P(),
        P(),
        P("head", None),
        P(),
        P(),
        P(("seq", "head"), None),
        P(("seq", "head"), None),
        P(("seq", "head"), None, None),
        P(("seq", "head"), None, None),
        P(("seq", "head"), None, None),
    )
    return jax.shard_map(
        local, mesh=mesh, in_specs=placed, out_specs=P(("seq", "head"), None), check_vma=False
    )
```

```python
import functools
import math

import jax
import jax.numpy as jnp
from jax import lax
from jax.experimental import pallas as pl
from jax.experimental.pallas import tpu as pltpu
from jax.sharding import PartitionSpec as P

HEADS = 32
KV_HEADS = 4
TOP = 8


EPSILON = 1e-06
THETA = 1000000.0
FLOOR = -1e30


def rms_scale(values, gain):
    return values * lax.rsqrt(jnp.mean(values * values, axis=-1, keepdims=True) + EPSILON) * gain


def rotate(values, cosine, sine):
    half = values.shape[-1] // 2
    first = values[..., :half]
    second = values[..., half:]
    return jnp.concatenate(
        [first * cosine - second * sine, second * cosine + first * sine], axis=-1
    )


def doc_index(positions, ends):
    return jnp.sum((positions[:, None] >= ends[None, :]).astype(jnp.int32), axis=1)


def _attend_kernel(bounds_ref, q_ref, kv_ref, qpos_ref, qstart_ref, o_ref, *, block, scale):
    q = q_ref[...]
    qpos = qpos_ref[...]
    qstart = qstart_ref[...]
    rows, width = q.shape

    def body(j, carry):
        high, total, accum = carry
        base = pl.multiple_of((bounds_ref[0] + j) * block, block)
        keys = kv_ref[0, pl.ds(base, block), :]
        values = kv_ref[1, pl.ds(base, block), :]
        scores = lax.dot_general(q, keys, (((1,), (1,)), ((), ())), preferred_element_type=jnp.float32) * scale
        key_pos = base + lax.broadcasted_iota(jnp.int32, (1, block), 1)
        allowed = (key_pos >= qstart) & (key_pos <= qpos)
        scores = jnp.where(allowed, scores, FLOOR)
        new_high = jnp.maximum(high, jnp.max(scores, axis=1, keepdims=True))
        weights = jnp.where(allowed, jnp.exp(scores - new_high), 0.0)
        factor = jnp.exp(high - new_high)
        total = total * factor + jnp.sum(weights, axis=1, keepdims=True)
        accum = accum * factor + jnp.dot(weights.astype(jnp.bfloat16), values, preferred_element_type=jnp.float32)
        return new_high, total, accum

    initial = (
        jnp.full((rows, 1), FLOOR, jnp.float32),
        jnp.zeros((rows, 1), jnp.float32),
        jnp.zeros((rows, width), jnp.float32),
    )
    high, total, accum = lax.fori_loop(0, bounds_ref[1], body, initial)
    o_ref[...] = (accum / total).astype(o_ref.dtype)

def attend(bounds, queries, kv, qpos, qstart, block):
    tok, heads, dim = queries.shape
    kernel = functools.partial(_attend_kernel, block=block, scale=dim ** (-0.5))
    spec = pltpu.PrefetchScalarGridSpec(
        num_scalar_prefetch=1,
        grid=(heads,),
        in_specs=[
            pl.BlockSpec((tok, dim), lambda h, b: (0, h)),
            pl.BlockSpec(kv.shape, lambda h, b: (0, 0, 0)),
            pl.BlockSpec((tok, 1), lambda h, b: (0, 0)),
            pl.BlockSpec((tok, 1), lambda h, b: (0, 0)),
        ],
        out_specs=pl.BlockSpec((tok, dim), lambda h, b: (0, h)),
    )
    return pl.pallas_call(
        kernel, grid_spec=spec, out_shape=jax.ShapeDtypeStruct((tok, heads * dim), jnp.bfloat16),
    )(bounds, queries.reshape(tok, heads * dim), kv, qpos, qstart)


def local(
    tokens,
    norm_gain,
    w_query,
    w_key,
    w_value,
    query_gain,
    key_gain,
    w_out,
    post_gain,
    doc_lengths,
    expert_ids,
    route_weights,
    w_gate,
    w_up,
    w_down,
):
    tok_dev, width = tokens.shape
    head_dim = query_gain.shape[0]
    per_dev = w_query.shape[1] // head_dim
    n_seq = lax.axis_size("seq")
    n_head = lax.axis_size("head")
    seq_index = lax.axis_index("seq")
    head_index = lax.axis_index("head")
    ndocs = doc_lengths.shape[0]
    ends = jnp.cumsum(doc_lengths)
    starts = ends - doc_lengths
    positions = seq_index * tok_dev + jnp.arange(tok_dev, dtype=jnp.int32)
    query_doc = doc_index(positions, ends)
    matches = query_doc[:, None] == jnp.arange(ndocs, dtype=jnp.int32)[None, :]
    own_start = jnp.sum(jnp.where(matches, starts[None, :], 0), axis=1)
    offset = (positions - own_start).astype(jnp.float32)
    half = head_dim // 2
    inverse = THETA ** (-2.0 * jnp.arange(half, dtype=jnp.float32) / head_dim)
    angles = offset[:, None] * inverse[None, :]
    cosine = jnp.cos(angles)
    sine = jnp.sin(angles)
    inputs = tokens.astype(jnp.float32)
    normed = rms_scale(inputs, norm_gain).astype(jnp.bfloat16)
    queries = jnp.dot(normed, w_query, preferred_element_type=jnp.float32).reshape(
        tok_dev, per_dev, head_dim
    )
    queries = rotate(rms_scale(queries, query_gain), cosine[:, None, :], sine[:, None, :]).astype(
        jnp.bfloat16
    )
    column = head_index * per_dev // (HEADS // KV_HEADS) * head_dim
    key_cols = lax.dynamic_slice_in_dim(w_key, column, head_dim, 1)
    value_cols = lax.dynamic_slice_in_dim(w_value, column, head_dim, 1)
    keys = rotate(
        rms_scale(jnp.dot(normed, key_cols, preferred_element_type=jnp.float32), key_gain),
        cosine,
        sine,
    ).astype(jnp.bfloat16)
    values = jnp.dot(normed, value_cols, preferred_element_type=jnp.float32).astype(jnp.bfloat16)
    stacked = jnp.stack([keys, values])
    spread = jnp.broadcast_to(stacked[:, None], (2, n_seq) + stacked.shape[1:])
    piece = lax.all_to_all(spread, "seq", 1, 1, tiled=True).reshape(2, n_seq * tok_dev, head_dim)
    block = tok_dev
    low = own_start[0] // block
    bounds = jnp.stack([low, positions[-1] // block - low + 1]).astype(jnp.int32)
    attended = attend(bounds, queries, piece, positions[:, None], own_start[:, None], block)
    rows = tok_dev // n_head
    terms = jnp.dot(attended, w_out, preferred_element_type=jnp.float32).astype(jnp.bfloat16)
    terms = lax.all_to_all(terms.reshape(n_head, rows, width), "head", 0, 0, tiled=True)
    attn_rows = jnp.sum(terms.astype(jnp.float32), axis=0)
    resid = lax.dynamic_slice_in_dim(tokens, head_index * rows, rows, 0).astype(jnp.float32) + attn_rows
    routed = rms_scale(resid, post_gain).astype(jnp.bfloat16)
    experts = n_seq * n_head * w_gate.shape[0]
    capacity = 2 * TOP * rows // experts
    chosen = expert_ids.reshape(-1)
    hits = (chosen[:, None] == jnp.arange(experts, dtype=jnp.int32)[None, :]).astype(jnp.int32)
    rank = jnp.sum((jnp.cumsum(hits, axis=0) - hits) * hits, axis=1)
    slot = rank * experts + chosen
    select = (slot[:, None] == jnp.arange(capacity * experts, dtype=jnp.int32)[None, :]).reshape(
        rows, TOP, capacity * experts
    )
    sources = jnp.transpose(jnp.any(select, axis=1)).astype(jnp.bfloat16)
    outgoing = jnp.dot(sources, routed, preferred_element_type=jnp.float32).astype(jnp.bfloat16)
    outgoing = outgoing.reshape(capacity, experts, width)
    half = capacity // 2
    results = []
    for part in (outgoing[:half], outgoing[half:]):
        block = lax.all_to_all(part, ("seq", "head"), split_axis=1, concat_axis=1, tiled=True)
        flat = block.reshape(-1, width)
        gate = jnp.dot(flat, w_gate[0], preferred_element_type=jnp.float32)
        up = jnp.dot(flat, w_up[0], preferred_element_type=jnp.float32)
        hidden = (jax.nn.silu(gate) * up).astype(jnp.bfloat16)
        down = jnp.dot(hidden, w_down[0], preferred_element_type=jnp.float32).astype(jnp.bfloat16)
        results.append(
            lax.all_to_all(
                down.reshape(block.shape), ("seq", "head"), split_axis=1, concat_axis=1, tiled=True
            )
        )
    returned = jnp.concatenate(results, axis=0).reshape(-1, width)
    mixing = jnp.sum(jnp.where(select, route_weights[:, :, None], 0.0), axis=1)
    combined = jnp.dot(
        mixing, returned.astype(jnp.float32), precision=lax.Precision.HIGHEST,
        preferred_element_type=jnp.float32,
    )
    return (resid + combined).astype(jnp.bfloat16)


def solution(mesh):
    placed = (
        P("seq", None),
        P(),
        P(None, "head"),
        P(),
        P(),
        P(),
        P(),
        P("head", None),
        P(),
        P(),
        P(("seq", "head"), None),
        P(("seq", "head"), None),
        P(("seq", "head"), None, None),
        P(("seq", "head"), None, None),
        P(("seq", "head"), None, None),
    )
    return jax.shard_map(
        local, mesh=mesh, in_specs=placed, out_specs=P(("seq", "head"), None), check_vma=False
    )
```

```python
import functools
import math

import jax
import jax.numpy as jnp
from jax import lax
from jax.experimental import pallas as pl
from jax.experimental.pallas import tpu as pltpu
from jax.sharding import PartitionSpec as P

HEADS = 32
KV_HEADS = 4
TOP = 8


EPSILON = 1e-06
THETA = 1000000.0
FLOOR = -1e30


def rms_scale(values, gain):
    return values * lax.rsqrt(jnp.mean(values * values, axis=-1, keepdims=True) + EPSILON) * gain


def rotate(values, cosine, sine):
    half = values.shape[-1] // 2
    first = values[..., :half]
    second = values[..., half:]
    return jnp.concatenate(
        [first * cosine - second * sine, second * cosine + first * sine], axis=-1
    )


def doc_index(positions, ends):
    return jnp.sum((positions[:, None] >= ends[None, :]).astype(jnp.int32), axis=1)


def _attend_kernel(bounds_ref, q_ref, kv_ref, qpos_ref, qstart_ref, o_ref, *, dim):
    heads = q_ref.shape[1] // dim
    tok = q_ref.shape[0]
    block = kv_ref.shape[2]
    q = jnp.concatenate([q_ref[:, h * dim : (h + 1) * dim] for h in range(heads)], axis=0)
    qpos = qpos_ref[...]
    qstart = qstart_ref[...]
    scale = dim ** (-0.5)

    def step(j, carry, masked):
        high, total, accum = carry
        keys = kv_ref[j, 0]
        values = kv_ref[j, 1]
        scores = lax.dot_general(q, keys, (((1,), (1,)), ((), ())), preferred_element_type=jnp.float32) * scale
        if masked:
            key_pos = j * block + lax.broadcasted_iota(jnp.int32, (1, block), 1)
            allowed = (key_pos >= qstart) & (key_pos <= qpos)
            scores = jnp.where(allowed, scores, FLOOR)
        new_high = jnp.maximum(high, jnp.max(scores, axis=1, keepdims=True))
        weights = jnp.exp(scores - new_high)
        if masked:
            weights = jnp.where(allowed, weights, 0.0)
        factor = jnp.exp(high - new_high)
        total = total * factor + jnp.sum(weights, axis=1, keepdims=True)
        accum = accum * factor + jnp.dot(
            weights.astype(jnp.bfloat16), values, preferred_element_type=jnp.float32
        )
        return new_high, total, accum

    carry = (
        jnp.full((heads * tok, 1), FLOOR, jnp.float32),
        jnp.zeros((heads * tok, 1), jnp.float32),
        jnp.zeros((heads * tok, dim), jnp.float32),
    )
    carry = lax.fori_loop(bounds_ref[0], bounds_ref[1], lambda j, c: step(j, c, True), carry)
    carry = lax.fori_loop(bounds_ref[1], bounds_ref[2], lambda j, c: step(j, c, False), carry)
    carry = lax.fori_loop(bounds_ref[2], bounds_ref[3], lambda j, c: step(j, c, True), carry)
    high, total, accum = carry
    out = (accum / total).astype(o_ref.dtype)
    for h in range(heads):
        o_ref[:, h * dim : (h + 1) * dim] = out[h * tok : (h + 1) * tok]


def attend(bounds, queries, kv, qpos, qstart):
    tok, heads, dim = queries.shape
    kernel = functools.partial(_attend_kernel, dim=dim)
    spec = pltpu.PrefetchScalarGridSpec(
        num_scalar_prefetch=1,
        grid=(1,),
        in_specs=[
            pl.BlockSpec((tok, heads * dim), lambda i, b: (0, 0)),
            pl.BlockSpec(kv.shape, lambda i, b: (0, 0, 0, 0)),
            pl.BlockSpec((heads * tok, 1), lambda i, b: (0, 0)),
            pl.BlockSpec((heads * tok, 1), lambda i, b: (0, 0)),
        ],
        out_specs=pl.BlockSpec((tok, heads * dim), lambda i, b: (0, 0)),
    )
    return pl.pallas_call(
        kernel, grid_spec=spec, out_shape=jax.ShapeDtypeStruct((tok, heads * dim), jnp.bfloat16)
    )(bounds, queries.reshape(tok, heads * dim), kv, jnp.tile(qpos, (heads, 1)), jnp.tile(qstart, (heads, 1)))


def local(
    tokens,
    norm_gain,
    w_query,
    w_key,
    w_value,
    query_gain,
    key_gain,
    w_out,
    post_gain,
    doc_lengths,
    expert_ids,
    route_weights,
    w_gate,
    w_up,
    w_down,
):
    tok_dev, width = tokens.shape
    head_dim = query_gain.shape[0]
    per_dev = w_query.shape[1] // head_dim
    n_seq = lax.axis_size("seq")
    n_head = lax.axis_size("head")
    seq_index = lax.axis_index("seq")
    head_index = lax.axis_index("head")
    ndocs = doc_lengths.shape[0]
    ends = jnp.cumsum(doc_lengths)
    starts = ends - doc_lengths
    positions = seq_index * tok_dev + jnp.arange(tok_dev, dtype=jnp.int32)
    query_doc = doc_index(positions, ends)
    matches = query_doc[:, None] == jnp.arange(ndocs, dtype=jnp.int32)[None, :]
    own_start = jnp.sum(jnp.where(matches, starts[None, :], 0), axis=1)
    offset = (positions - own_start).astype(jnp.float32)
    half = head_dim // 2
    inverse = THETA ** (-2.0 * jnp.arange(half, dtype=jnp.float32) / head_dim)
    angles = offset[:, None] * inverse[None, :]
    cosine = jnp.cos(angles)
    sine = jnp.sin(angles)
    inputs = tokens.astype(jnp.float32)
    normed = rms_scale(inputs, norm_gain).astype(jnp.bfloat16)
    queries = jnp.dot(normed, w_query, preferred_element_type=jnp.float32).reshape(
        tok_dev, per_dev, head_dim
    )
    queries = rotate(rms_scale(queries, query_gain), cosine[:, None, :], sine[:, None, :]).astype(
        jnp.bfloat16
    )
    column = head_index * per_dev // (HEADS // KV_HEADS) * head_dim
    key_cols = lax.dynamic_slice_in_dim(w_key, column, head_dim, 1)
    value_cols = lax.dynamic_slice_in_dim(w_value, column, head_dim, 1)
    keys = rotate(
        rms_scale(jnp.dot(normed, key_cols, preferred_element_type=jnp.float32), key_gain),
        cosine,
        sine,
    ).astype(jnp.bfloat16)
    values = jnp.dot(normed, value_cols, preferred_element_type=jnp.float32).astype(jnp.bfloat16)
    stacked = jnp.stack([keys, values])
    spread = jnp.broadcast_to(stacked[None], (n_seq,) + stacked.shape)
    piece = lax.all_to_all(spread, "seq", 0, 0, tiled=True)
    block = tok_dev
    low = own_start[0] // block
    high = positions[-1] // block + 1
    inner_low = jnp.clip(-(-own_start[-1] // block), low, high)
    inner_high = jnp.clip((positions[0] + 1) // block, inner_low, high)
    bounds = jnp.stack([low, inner_low, inner_high, high]).astype(jnp.int32)
    attended = attend(bounds, queries, piece, positions[:, None], own_start[:, None])
    rows = tok_dev // n_head
    terms = jnp.dot(attended, w_out, preferred_element_type=jnp.float32).astype(jnp.bfloat16)
    terms = lax.all_to_all(terms.reshape(n_head, rows, width), "head", 0, 0, tiled=True)
    attn_rows = jnp.sum(terms.astype(jnp.float32), axis=0)
    resid = lax.dynamic_slice_in_dim(tokens, head_index * rows, rows, 0).astype(jnp.float32) + attn_rows
    routed = rms_scale(resid, post_gain).astype(jnp.bfloat16)
    experts = n_seq * n_head * w_gate.shape[0]
    capacity = 2 * TOP * rows // experts
    chosen = expert_ids.reshape(-1)
    hits = (chosen[:, None] == jnp.arange(experts, dtype=jnp.int32)[None, :]).astype(jnp.int32)
    rank = jnp.sum((jnp.cumsum(hits, axis=0) - hits) * hits, axis=1)
    slot = rank * experts + chosen
    select = (slot[:, None] == jnp.arange(capacity * experts, dtype=jnp.int32)[None, :]).reshape(
        rows, TOP, capacity * experts
    )
    sources = jnp.transpose(jnp.any(select, axis=1)).astype(jnp.bfloat16)
    outgoing = jnp.dot(sources, routed, preferred_element_type=jnp.float32).astype(jnp.bfloat16)
    outgoing = outgoing.reshape(capacity, experts, width)
    block = lax.all_to_all(outgoing, ("seq", "head"), split_axis=1, concat_axis=1, tiled=True)
    flat = block.reshape(-1, width)
    gate = jnp.dot(flat, w_gate[0], preferred_element_type=jnp.float32)
    up = jnp.dot(flat, w_up[0], preferred_element_type=jnp.float32)
    hidden = (jax.nn.silu(gate) * up).astype(jnp.bfloat16)
    returned = lax.all_to_all(
        jnp.dot(hidden, w_down[0], preferred_element_type=jnp.float32)
        .astype(jnp.bfloat16)
        .reshape(block.shape),
        ("seq", "head"),
        split_axis=1,
        concat_axis=1,
        tiled=True,
    ).reshape(-1, width)
    mixing = jnp.sum(jnp.where(select, route_weights[:, :, None], 0.0), axis=1)
    combined = jnp.dot(
        mixing, returned.astype(jnp.float32), precision=lax.Precision.HIGHEST,
        preferred_element_type=jnp.float32,
    )
    return (resid + combined).astype(jnp.bfloat16)


def solution(mesh):
    placed = (
        P("seq", None),
        P(),
        P(None, "head"),
        P(),
        P(),
        P(),
        P(),
        P("head", None),
        P(),
        P(),
        P(("seq", "head"), None),
        P(("seq", "head"), None),
        P(("seq", "head"), None, None),
        P(("seq", "head"), None, None),
        P(("seq", "head"), None, None),
    )
    return jax.shard_map(
        local, mesh=mesh, in_specs=placed, out_specs=P(("seq", "head"), None), check_vma=False
    )
```

```python
import functools
import math

import jax
import jax.numpy as jnp
from jax import lax
from jax.experimental import pallas as pl
from jax.experimental.pallas import tpu as pltpu
from jax.sharding import PartitionSpec as P

HEADS = 32
KV_HEADS = 4
TOP = 8


EPSILON = 1e-06
THETA = 1000000.0
FLOOR = -1e30


def rms_scale(values, gain):
    return values * lax.rsqrt(jnp.mean(values * values, axis=-1, keepdims=True) + EPSILON) * gain


def rotate(values, cosine, sine):
    half = values.shape[-1] // 2
    first = values[..., :half]
    second = values[..., half:]
    return jnp.concatenate(
        [first * cosine - second * sine, second * cosine + first * sine], axis=-1
    )


def doc_index(positions, ends):
    return jnp.sum((positions[:, None] >= ends[None, :]).astype(jnp.int32), axis=1)


def _attend_kernel(bounds_ref, q_ref, kv_ref, qpos_ref, qstart_ref, o_ref, *, dim):
    heads = q_ref.shape[1] // dim
    tok = q_ref.shape[0]
    block = kv_ref.shape[2]
    q = jnp.concatenate([q_ref[:, h * dim : (h + 1) * dim] for h in range(heads)], axis=0)
    qpos = qpos_ref[...]
    qstart = qstart_ref[...]
    scale = dim ** (-0.5)

    def step(j, carry, masked):
        high, total, accum = carry
        keys = kv_ref[j, 0]
        values = kv_ref[j, 1]
        scores = lax.dot_general(q, keys, (((1,), (1,)), ((), ())), preferred_element_type=jnp.float32) * scale
        if masked:
            key_pos = j * block + lax.broadcasted_iota(jnp.int32, (1, block), 1)
            allowed = (key_pos >= qstart) & (key_pos <= qpos)
            scores = jnp.where(allowed, scores, FLOOR)
        new_high = jnp.maximum(high, jnp.max(scores, axis=1, keepdims=True))
        weights = jnp.exp(scores - new_high)
        if masked:
            weights = jnp.where(allowed, weights, 0.0)
        factor = jnp.exp(high - new_high)
        total = total * factor + jnp.sum(weights, axis=1, keepdims=True)
        accum = accum * factor + jnp.dot(
            weights.astype(jnp.bfloat16), values, preferred_element_type=jnp.float32
        )
        return new_high, total, accum

    carry = (
        jnp.full((heads * tok, 1), FLOOR, jnp.float32),
        jnp.zeros((heads * tok, 1), jnp.float32),
        jnp.zeros((heads * tok, dim), jnp.float32),
    )
    carry = lax.fori_loop(bounds_ref[0], bounds_ref[1], lambda j, c: step(j, c, True), carry)
    carry = lax.fori_loop(bounds_ref[1], bounds_ref[2], lambda j, c: step(j, c, False), carry)
    carry = lax.fori_loop(bounds_ref[2], bounds_ref[3], lambda j, c: step(j, c, True), carry)
    high, total, accum = carry
    out = (accum / total).astype(o_ref.dtype)
    for h in range(heads):
        o_ref[:, h * dim : (h + 1) * dim] = out[h * tok : (h + 1) * tok]


def attend(bounds, queries, kv, qpos, qstart):
    tok, heads, dim = queries.shape
    kernel = functools.partial(_attend_kernel, dim=dim)
    spec = pltpu.PrefetchScalarGridSpec(
        num_scalar_prefetch=1,
        grid=(1,),
        in_specs=[
            pl.BlockSpec((tok, heads * dim), lambda i, b: (0, 0)),
            pl.BlockSpec(kv.shape, lambda i, b: (0, 0, 0, 0)),
            pl.BlockSpec((heads * tok, 1), lambda i, b: (0, 0)),
            pl.BlockSpec((heads * tok, 1), lambda i, b: (0, 0)),
        ],
        out_specs=pl.BlockSpec((tok, heads * dim), lambda i, b: (0, 0)),
    )
    return pl.pallas_call(
        kernel, grid_spec=spec, out_shape=jax.ShapeDtypeStruct((tok, heads * dim), jnp.bfloat16)
    )(bounds, queries.reshape(tok, heads * dim), kv, jnp.tile(qpos, (heads, 1)), jnp.tile(qstart, (heads, 1)))


def local(
    tokens,
    norm_gain,
    w_query,
    w_key,
    w_value,
    query_gain,
    key_gain,
    w_out,
    post_gain,
    doc_lengths,
    expert_ids,
    route_weights,
    w_gate,
    w_up,
    w_down,
):
    tok_dev, width = tokens.shape
    head_dim = query_gain.shape[0]
    per_dev = w_query.shape[1] // head_dim
    n_seq = lax.axis_size("seq")
    n_head = lax.axis_size("head")
    seq_index = lax.axis_index("seq")
    head_index = lax.axis_index("head")
    ndocs = doc_lengths.shape[0]
    ends = jnp.cumsum(doc_lengths)
    starts = ends - doc_lengths
    positions = seq_index * tok_dev + jnp.arange(tok_dev, dtype=jnp.int32)
    query_doc = doc_index(positions, ends)
    matches = query_doc[:, None] == jnp.arange(ndocs, dtype=jnp.int32)[None, :]
    own_start = jnp.sum(jnp.where(matches, starts[None, :], 0), axis=1)
    offset = (positions - own_start).astype(jnp.float32)
    half = head_dim // 2
    inverse = THETA ** (-2.0 * jnp.arange(half, dtype=jnp.float32) / head_dim)
    angles = offset[:, None] * inverse[None, :]
    cosine = jnp.cos(angles)
    sine = jnp.sin(angles)
    inputs = tokens.astype(jnp.float32)
    normed = rms_scale(inputs, norm_gain).astype(jnp.bfloat16)
    queries = jnp.dot(normed, w_query, preferred_element_type=jnp.float32).reshape(
        tok_dev, per_dev, head_dim
    )
    queries = rotate(rms_scale(queries, query_gain), cosine[:, None, :], sine[:, None, :]).astype(
        jnp.bfloat16
    )
    column = head_index * per_dev // (HEADS // KV_HEADS) * head_dim
    key_cols = lax.dynamic_slice_in_dim(w_key, column, head_dim, 1)
    value_cols = lax.dynamic_slice_in_dim(w_value, column, head_dim, 1)
    keys = rotate(
        rms_scale(jnp.dot(normed, key_cols, preferred_element_type=jnp.float32), key_gain),
        cosine,
        sine,
    ).astype(jnp.bfloat16)
    values = jnp.dot(normed, value_cols, preferred_element_type=jnp.float32).astype(jnp.bfloat16)
    stacked = jnp.stack([keys, values])
    spread = jnp.broadcast_to(stacked[None], (n_seq,) + stacked.shape)
    piece = lax.all_to_all(spread, "seq", 0, 0, tiled=True)
    block = tok_dev
    low = own_start[0] // block
    high = positions[-1] // block + 1
    inner_low = jnp.clip(-(-own_start[-1] // block), low, high)
    inner_high = jnp.clip((positions[0] + 1) // block, inner_low, high)
    bounds = jnp.stack([low, inner_low, inner_high, high]).astype(jnp.int32)
    attended = attend(bounds, queries, piece, positions[:, None], own_start[:, None])
    rows = tok_dev // n_head
    terms = jnp.dot(attended, w_out, preferred_element_type=jnp.float32).astype(jnp.bfloat16)
    terms = lax.all_to_all(terms.reshape(n_head, rows, width), "head", 0, 0, tiled=True)
    attn_rows = jnp.sum(terms.astype(jnp.float32), axis=0)
    resid = lax.dynamic_slice_in_dim(tokens, head_index * rows, rows, 0).astype(jnp.float32) + attn_rows
    routed = rms_scale(resid, post_gain).astype(jnp.bfloat16)
    experts = n_seq * n_head * w_gate.shape[0]
    capacity = 2 * TOP * rows // experts
    chosen = expert_ids.reshape(-1)
    hits = (chosen[:, None] == jnp.arange(experts, dtype=jnp.int32)[None, :]).astype(jnp.int32)
    rank = jnp.sum((jnp.cumsum(hits, axis=0) - hits) * hits, axis=1)
    slot = chosen * capacity + rank
    select = (slot[:, None] == jnp.arange(experts * capacity, dtype=jnp.int32)[None, :]).reshape(
        rows, TOP, experts, capacity
    )
    sources = jnp.any(select, axis=1).astype(jnp.bfloat16)
    outgoing = lax.dot_general(
        sources, routed, (((0,), (0,)), ((), ())), preferred_element_type=jnp.float32
    ).astype(jnp.bfloat16)
    block = lax.all_to_all(outgoing, ("seq", "head"), split_axis=0, concat_axis=0, tiled=True)
    gate = jnp.einsum("scd,df->scf", block, w_gate[0], preferred_element_type=jnp.float32)
    up = jnp.einsum("scd,df->scf", block, w_up[0], preferred_element_type=jnp.float32)
    hidden = (jax.nn.silu(gate) * up).astype(jnp.bfloat16)
    down = jnp.einsum("scf,fd->scd", hidden, w_down[0], preferred_element_type=jnp.float32)
    returned = lax.all_to_all(
        down.astype(jnp.bfloat16), ("seq", "head"), split_axis=0, concat_axis=0, tiled=True
    )
    mixing = jnp.sum(jnp.where(select, route_weights[:, :, None, None], 0.0), axis=1)
    combined = lax.dot_general(
        mixing,
        returned.astype(jnp.float32),
        (((1, 2), (0, 1)), ((), ())),
        precision=lax.Precision.HIGHEST,
        preferred_element_type=jnp.float32,
    )
    return (resid + combined).astype(jnp.bfloat16)


def solution(mesh):
    placed = (
        P("seq", None),
        P(),
        P(None, "head"),
        P(),
        P(),
        P(),
        P(),
        P("head", None),
        P(),
        P(),
        P(("seq", "head"), None),
        P(("seq", "head"), None),
        P(("seq", "head"), None, None),
        P(("seq", "head"), None, None),
        P(("seq", "head"), None, None),
    )
    return jax.shard_map(
        local, mesh=mesh, in_specs=placed, out_specs=P(("seq", "head"), None), check_vma=False
    )
```

```python
import functools
import math

import jax
import jax.numpy as jnp
from jax import lax
from jax.experimental import pallas as pl
from jax.experimental.pallas import tpu as pltpu
from jax.sharding import PartitionSpec as P

HEADS = 32
KV_HEADS = 4
TOP = 8


EPSILON = 1e-06
THETA = 1000000.0
FLOOR = -1e30


def rms_scale(values, gain):
    return values * lax.rsqrt(jnp.mean(values * values, axis=-1, keepdims=True) + EPSILON) * gain


def rotate(values, cosine, sine):
    half = values.shape[-1] // 2
    first = values[..., :half]
    second = values[..., half:]
    return jnp.concatenate(
        [first * cosine - second * sine, second * cosine + first * sine], axis=-1
    )


def doc_index(positions, ends):
    return jnp.sum((positions[:, None] >= ends[None, :]).astype(jnp.int32), axis=1)


def _attend_kernel(bounds_ref, q_ref, own_ref, other_ref, qpos_ref, qstart_ref, o_ref, *, dim):
    heads = q_ref.shape[1] // dim
    tok = q_ref.shape[0]
    block = own_ref.shape[2]
    q = jnp.concatenate([q_ref[:, h * dim : (h + 1) * dim] for h in range(heads)], axis=0)
    qpos = qpos_ref[...]
    qstart = qstart_ref[...]
    scale = dim ** (-0.5)

    def step(j, carry, masked):
        high, total, accum = carry
        mine = j % 2 == bounds_ref[4]
        keys = jnp.where(mine, own_ref[j // 2, 0], other_ref[j // 2, 0])
        values = jnp.where(mine, own_ref[j // 2, 1], other_ref[j // 2, 1])
        scores = lax.dot_general(q, keys, (((1,), (1,)), ((), ())), preferred_element_type=jnp.float32) * scale
        if masked:
            key_pos = j * block + lax.broadcasted_iota(jnp.int32, (1, block), 1)
            allowed = (key_pos >= qstart) & (key_pos <= qpos)
            scores = jnp.where(allowed, scores, FLOOR)
        new_high = jnp.maximum(high, jnp.max(scores, axis=1, keepdims=True))
        weights = jnp.exp(scores - new_high)
        if masked:
            weights = jnp.where(allowed, weights, 0.0)
        factor = jnp.exp(high - new_high)
        total = total * factor + jnp.sum(weights, axis=1, keepdims=True)
        accum = accum * factor + jnp.dot(
            weights.astype(jnp.bfloat16), values, preferred_element_type=jnp.float32
        )
        return new_high, total, accum

    carry = (
        jnp.full((heads * tok, 1), FLOOR, jnp.float32),
        jnp.zeros((heads * tok, 1), jnp.float32),
        jnp.zeros((heads * tok, dim), jnp.float32),
    )
    carry = lax.fori_loop(bounds_ref[0], bounds_ref[1], lambda j, c: step(j, c, True), carry)
    carry = lax.fori_loop(bounds_ref[1], bounds_ref[2], lambda j, c: step(j, c, False), carry)
    carry = lax.fori_loop(bounds_ref[2], bounds_ref[3], lambda j, c: step(j, c, True), carry)
    high, total, accum = carry
    out = (accum / total).astype(o_ref.dtype)
    for h in range(heads):
        o_ref[:, h * dim : (h + 1) * dim] = out[h * tok : (h + 1) * tok]


def attend(bounds, queries, own, other, qpos, qstart):
    tok, heads, dim = queries.shape
    kernel = functools.partial(_attend_kernel, dim=dim)
    spec = pltpu.PrefetchScalarGridSpec(
        num_scalar_prefetch=1,
        grid=(1,),
        in_specs=[
            pl.BlockSpec((tok, heads * dim), lambda i, b: (0, 0)),
            pl.BlockSpec(own.shape, lambda i, b: (0, 0, 0, 0)),
            pl.BlockSpec(other.shape, lambda i, b: (0, 0, 0, 0)),
            pl.BlockSpec((heads * tok, 1), lambda i, b: (0, 0)),
            pl.BlockSpec((heads * tok, 1), lambda i, b: (0, 0)),
        ],
        out_specs=pl.BlockSpec((tok, heads * dim), lambda i, b: (0, 0)),
    )
    return pl.pallas_call(
        kernel, grid_spec=spec, out_shape=jax.ShapeDtypeStruct((tok, heads * dim), jnp.bfloat16)
    )(bounds, queries.reshape(tok, heads * dim), own, other, jnp.tile(qpos, (heads, 1)), jnp.tile(qstart, (heads, 1)))


def local(
    tokens,
    norm_gain,
    w_query,
    w_key,
    w_value,
    query_gain,
    key_gain,
    w_out,
    post_gain,
    doc_lengths,
    expert_ids,
    route_weights,
    w_gate,
    w_up,
    w_down,
):
    tok_dev, width = tokens.shape
    head_dim = query_gain.shape[0]
    per_dev = w_query.shape[1] // head_dim
    n_seq = lax.axis_size("seq")
    n_head = lax.axis_size("head")
    seq_index = lax.axis_index("seq")
    head_index = lax.axis_index("head")
    ndocs = doc_lengths.shape[0]
    ends = jnp.cumsum(doc_lengths)
    starts = ends - doc_lengths
    positions = seq_index * tok_dev + jnp.arange(tok_dev, dtype=jnp.int32)
    query_doc = doc_index(positions, ends)
    matches = query_doc[:, None] == jnp.arange(ndocs, dtype=jnp.int32)[None, :]
    own_start = jnp.sum(jnp.where(matches, starts[None, :], 0), axis=1)
    offset = (positions - own_start).astype(jnp.float32)
    half = head_dim // 2
    inverse = THETA ** (-2.0 * jnp.arange(half, dtype=jnp.float32) / head_dim)
    angles = offset[:, None] * inverse[None, :]
    cosine = jnp.cos(angles)
    sine = jnp.sin(angles)
    inputs = tokens.astype(jnp.float32)
    normed = rms_scale(inputs, norm_gain).astype(jnp.bfloat16)
    queries = jnp.dot(normed, w_query, preferred_element_type=jnp.float32).reshape(
        tok_dev, per_dev, head_dim
    )
    queries = rotate(rms_scale(queries, query_gain), cosine[:, None, :], sine[:, None, :]).astype(
        jnp.bfloat16
    )
    column = head_index * per_dev // (HEADS // KV_HEADS) * head_dim
    key_cols = lax.dynamic_slice_in_dim(w_key, column, head_dim, 1)
    value_cols = lax.dynamic_slice_in_dim(w_value, column, head_dim, 1)
    keys = rotate(
        rms_scale(jnp.dot(normed, key_cols, preferred_element_type=jnp.float32), key_gain),
        cosine,
        sine,
    ).astype(jnp.bfloat16)
    values = jnp.dot(normed, value_cols, preferred_element_type=jnp.float32).astype(jnp.bfloat16)
    stacked = jnp.stack([keys, values])
    pairs = n_seq // 2
    groups = [[2 * i + c for i in range(pairs)] for c in range(2)]
    spread = jnp.broadcast_to(stacked[None], (pairs,) + stacked.shape)
    same_core = lax.all_to_all(spread, "seq", 0, 0, tiled=True, axis_index_groups=groups)
    other_core = lax.ppermute(same_core, "seq", [(i, i ^ 1) for i in range(n_seq)])
    block = tok_dev
    low = own_start[0] // block
    high = positions[-1] // block + 1
    inner_low = jnp.clip(-(-own_start[-1] // block), low, high)
    inner_high = jnp.clip((positions[0] + 1) // block, inner_low, high)
    bounds = jnp.stack([low, inner_low, inner_high, high, seq_index % 2]).astype(jnp.int32)
    attended = attend(bounds, queries, same_core, other_core, positions[:, None], own_start[:, None])
    rows = tok_dev // n_head
    terms = jnp.dot(attended, w_out, preferred_element_type=jnp.float32).astype(jnp.bfloat16)
    terms = lax.all_to_all(terms.reshape(n_head, rows, width), "head", 0, 0, tiled=True)
    attn_rows = jnp.sum(terms.astype(jnp.float32), axis=0)
    resid = lax.dynamic_slice_in_dim(tokens, head_index * rows, rows, 0).astype(jnp.float32) + attn_rows
    routed = rms_scale(resid, post_gain).astype(jnp.bfloat16)
    experts = n_seq * n_head * w_gate.shape[0]
    capacity = 2 * TOP * rows // experts
    chosen = expert_ids.reshape(-1)
    hits = (chosen[:, None] == jnp.arange(experts, dtype=jnp.int32)[None, :]).astype(jnp.int32)
    rank = jnp.sum((jnp.cumsum(hits, axis=0) - hits) * hits, axis=1)
    slot = rank * experts + chosen
    select = (slot[:, None] == jnp.arange(capacity * experts, dtype=jnp.int32)[None, :]).reshape(
        rows, TOP, capacity * experts
    )
    sources = jnp.transpose(jnp.any(select, axis=1)).astype(jnp.bfloat16)
    outgoing = jnp.dot(sources, routed, preferred_element_type=jnp.float32).astype(jnp.bfloat16)
    outgoing = outgoing.reshape(capacity, experts, width)
    block = lax.all_to_all(outgoing, ("seq", "head"), split_axis=1, concat_axis=1, tiled=True)
    flat = block.reshape(-1, width)
    gate = jnp.dot(flat, w_gate[0], preferred_element_type=jnp.float32)
    up = jnp.dot(flat, w_up[0], preferred_element_type=jnp.float32)
    hidden = (jax.nn.silu(gate) * up).astype(jnp.bfloat16)
    returned = lax.all_to_all(
        jnp.dot(hidden, w_down[0], preferred_element_type=jnp.float32)
        .astype(jnp.bfloat16)
        .reshape(block.shape),
        ("seq", "head"),
        split_axis=1,
        concat_axis=1,
        tiled=True,
    ).reshape(-1, width)
    mixing = jnp.sum(jnp.where(select, route_weights[:, :, None], 0.0), axis=1)
    combined = jnp.dot(
        mixing, returned.astype(jnp.float32), precision=lax.Precision.HIGHEST,
        preferred_element_type=jnp.float32,
    )
    return (resid + combined).astype(jnp.bfloat16)


def solution(mesh):
    placed = (
        P("seq", None),
        P(),
        P(None, "head"),
        P(),
        P(),
        P(),
        P(),
        P("head", None),
        P(),
        P(),
        P(("seq", "head"), None),
        P(("seq", "head"), None),
        P(("seq", "head"), None, None),
        P(("seq", "head"), None, None),
        P(("seq", "head"), None, None),
    )
    return jax.shard_map(
        local, mesh=mesh, in_specs=placed, out_specs=P(("seq", "head"), None), check_vma=False
    )
```

```python
import functools
import math

import jax
import jax.numpy as jnp
from jax import lax
from jax.experimental import pallas as pl
from jax.experimental.pallas import tpu as pltpu
from jax.sharding import PartitionSpec as P

HEADS = 32
KV_HEADS = 4
TOP = 8


EPSILON = 1e-06
THETA = 1000000.0
FLOOR = -1e30


def rms_scale(values, gain):
    return values * lax.rsqrt(jnp.mean(values * values, axis=-1, keepdims=True) + EPSILON) * gain


def rotate(values, cosine, sine):
    half = values.shape[-1] // 2
    first = values[..., :half]
    second = values[..., half:]
    return jnp.concatenate(
        [first * cosine - second * sine, second * cosine + first * sine], axis=-1
    )


def doc_index(positions, ends):
    return jnp.sum((positions[:, None] >= ends[None, :]).astype(jnp.int32), axis=1)


def _attend_kernel(bounds_ref, q_ref, own_ref, other_ref, qpos_ref, qstart_ref, o_ref, *, dim):
    heads = q_ref.shape[1] // dim
    tok = q_ref.shape[0]
    block = own_ref.shape[2]
    q = jnp.concatenate([q_ref[:, h * dim : (h + 1) * dim] for h in range(heads)], axis=0)
    qpos = qpos_ref[...]
    qstart = qstart_ref[...]
    scale = dim ** (-0.5)

    def step(j, carry, masked):
        high, total, accum = carry
        mine = j % 2 == bounds_ref[4]
        keys = jnp.where(mine, own_ref[j // 2, 0], other_ref[j // 2, 0])
        values = jnp.where(mine, own_ref[j // 2, 1], other_ref[j // 2, 1])
        scores = lax.dot_general(q, keys, (((1,), (1,)), ((), ())), preferred_element_type=jnp.float32) * scale
        if masked:
            key_pos = j * block + lax.broadcasted_iota(jnp.int32, (1, block), 1)
            allowed = (key_pos >= qstart) & (key_pos <= qpos)
            scores = jnp.where(allowed, scores, FLOOR)
        new_high = jnp.maximum(high, jnp.max(scores, axis=1, keepdims=True))
        weights = jnp.exp(scores - new_high)
        if masked:
            weights = jnp.where(allowed, weights, 0.0)
        factor = jnp.exp(high - new_high)
        total = total * factor + jnp.sum(weights, axis=1, keepdims=True)
        accum = accum * factor + jnp.dot(
            weights.astype(jnp.bfloat16), values, preferred_element_type=jnp.float32
        )
        return new_high, total, accum

    carry = (
        jnp.full((heads * tok, 1), FLOOR, jnp.float32),
        jnp.zeros((heads * tok, 1), jnp.float32),
        jnp.zeros((heads * tok, dim), jnp.float32),
    )
    carry = lax.fori_loop(bounds_ref[0], bounds_ref[1], lambda j, c: step(j, c, True), carry)
    carry = lax.fori_loop(bounds_ref[1], bounds_ref[2], lambda j, c: step(j, c, False), carry)
    carry = lax.fori_loop(bounds_ref[2], bounds_ref[3], lambda j, c: step(j, c, True), carry)
    high, total, accum = carry
    out = (accum / total).astype(o_ref.dtype)
    for h in range(heads):
        o_ref[:, h * dim : (h + 1) * dim] = out[h * tok : (h + 1) * tok]


def attend(bounds, queries, own, other, qpos, qstart):
    tok, heads, dim = queries.shape
    kernel = functools.partial(_attend_kernel, dim=dim)
    spec = pltpu.PrefetchScalarGridSpec(
        num_scalar_prefetch=1,
        grid=(1,),
        in_specs=[
            pl.BlockSpec((tok, heads * dim), lambda i, b: (0, 0)),
            pl.BlockSpec(own.shape, lambda i, b: (0, 0, 0, 0)),
            pl.BlockSpec(other.shape, lambda i, b: (0, 0, 0, 0)),
            pl.BlockSpec((heads * tok, 1), lambda i, b: (0, 0)),
            pl.BlockSpec((heads * tok, 1), lambda i, b: (0, 0)),
        ],
        out_specs=pl.BlockSpec((tok, heads * dim), lambda i, b: (0, 0)),
    )
    return pl.pallas_call(
        kernel, grid_spec=spec, out_shape=jax.ShapeDtypeStruct((tok, heads * dim), jnp.bfloat16)
    )(bounds, queries.reshape(tok, heads * dim), own, other, jnp.tile(qpos, (heads, 1)), jnp.tile(qstart, (heads, 1)))


def local(
    tokens,
    norm_gain,
    w_query,
    w_key,
    w_value,
    query_gain,
    key_gain,
    w_out,
    post_gain,
    doc_lengths,
    expert_ids,
    route_weights,
    w_gate,
    w_up,
    w_down,
):
    tok_dev, width = tokens.shape
    head_dim = query_gain.shape[0]
    per_dev = w_query.shape[1] // head_dim
    n_seq = lax.axis_size("seq")
    n_head = lax.axis_size("head")
    seq_index = lax.axis_index("seq")
    head_index = lax.axis_index("head")
    ndocs = doc_lengths.shape[0]
    ends = jnp.cumsum(doc_lengths)
    starts = ends - doc_lengths
    positions = seq_index * tok_dev + jnp.arange(tok_dev, dtype=jnp.int32)
    query_doc = doc_index(positions, ends)
    matches = query_doc[:, None] == jnp.arange(ndocs, dtype=jnp.int32)[None, :]
    own_start = jnp.sum(jnp.where(matches, starts[None, :], 0), axis=1)
    offset = (positions - own_start).astype(jnp.float32)
    half = head_dim // 2
    inverse = THETA ** (-2.0 * jnp.arange(half, dtype=jnp.float32) / head_dim)
    angles = offset[:, None] * inverse[None, :]
    cosine = jnp.cos(angles)
    sine = jnp.sin(angles)
    inputs = tokens.astype(jnp.float32)
    normed = rms_scale(inputs, norm_gain).astype(jnp.bfloat16)
    queries = jnp.dot(normed, w_query, preferred_element_type=jnp.float32).reshape(
        tok_dev, per_dev, head_dim
    )
    queries = rotate(rms_scale(queries, query_gain), cosine[:, None, :], sine[:, None, :]).astype(
        jnp.bfloat16
    )
    column = head_index * per_dev // (HEADS // KV_HEADS) * head_dim
    key_cols = lax.dynamic_slice_in_dim(w_key, column, head_dim, 1)
    value_cols = lax.dynamic_slice_in_dim(w_value, column, head_dim, 1)
    keys = rotate(
        rms_scale(jnp.dot(normed, key_cols, preferred_element_type=jnp.float32), key_gain),
        cosine,
        sine,
    ).astype(jnp.bfloat16)
    values = jnp.dot(normed, value_cols, preferred_element_type=jnp.float32).astype(jnp.bfloat16)
    stacked = jnp.stack([keys, values])
    pairs = n_seq // 2
    groups = [[2 * i + c for i in range(pairs)] for c in range(2)]
    spread = jnp.broadcast_to(stacked[None], (pairs,) + stacked.shape)
    same_core = lax.all_to_all(spread, "seq", 0, 0, tiled=True, axis_index_groups=groups)
    queries, same_core = lax.optimization_barrier((queries, same_core))
    other_core = lax.ppermute(same_core, "seq", [(i, i ^ 1) for i in range(n_seq)])
    block = tok_dev
    low = own_start[0] // block
    high = positions[-1] // block + 1
    inner_low = jnp.clip(-(-own_start[-1] // block), low, high)
    inner_high = jnp.clip((positions[0] + 1) // block, inner_low, high)
    bounds = jnp.stack([low, inner_low, inner_high, high, seq_index % 2]).astype(jnp.int32)
    attended = attend(bounds, queries, same_core, other_core, positions[:, None], own_start[:, None])
    rows = tok_dev // n_head
    terms = jnp.dot(attended, w_out, preferred_element_type=jnp.float32).astype(jnp.bfloat16)
    terms = lax.all_to_all(terms.reshape(n_head, rows, width), "head", 0, 0, tiled=True)
    attn_rows = jnp.sum(terms.astype(jnp.float32), axis=0)
    resid = lax.dynamic_slice_in_dim(tokens, head_index * rows, rows, 0).astype(jnp.float32) + attn_rows
    routed = rms_scale(resid, post_gain).astype(jnp.bfloat16)
    experts = n_seq * n_head * w_gate.shape[0]
    capacity = 2 * TOP * rows // experts
    chosen = expert_ids.reshape(-1)
    hits = (chosen[:, None] == jnp.arange(experts, dtype=jnp.int32)[None, :]).astype(jnp.int32)
    rank = jnp.sum((jnp.cumsum(hits, axis=0) - hits) * hits, axis=1)
    slot = rank * experts + chosen
    select = (slot[:, None] == jnp.arange(capacity * experts, dtype=jnp.int32)[None, :]).reshape(
        rows, TOP, capacity * experts
    )
    sources = jnp.transpose(jnp.any(select, axis=1)).astype(jnp.bfloat16)
    outgoing = jnp.dot(sources, routed, preferred_element_type=jnp.float32).astype(jnp.bfloat16)
    outgoing = outgoing.reshape(capacity, experts, width)
    block = lax.all_to_all(outgoing, ("seq", "head"), split_axis=1, concat_axis=1, tiled=True)
    flat = block.reshape(-1, width)
    gate = jnp.dot(flat, w_gate[0], preferred_element_type=jnp.float32)
    up = jnp.dot(flat, w_up[0], preferred_element_type=jnp.float32)
    hidden = (jax.nn.silu(gate) * up).astype(jnp.bfloat16)
    returned = lax.all_to_all(
        jnp.dot(hidden, w_down[0], preferred_element_type=jnp.float32)
        .astype(jnp.bfloat16)
        .reshape(block.shape),
        ("seq", "head"),
        split_axis=1,
        concat_axis=1,
        tiled=True,
    ).reshape(-1, width)
    mixing = jnp.sum(jnp.where(select, route_weights[:, :, None], 0.0), axis=1)
    combined = jnp.dot(
        mixing, returned.astype(jnp.float32), precision=lax.Precision.HIGHEST,
        preferred_element_type=jnp.float32,
    )
    return (resid + combined).astype(jnp.bfloat16)


def solution(mesh):
    placed = (
        P("seq", None),
        P(),
        P(None, "head"),
        P(),
        P(),
        P(),
        P(),
        P("head", None),
        P(),
        P(),
        P(("seq", "head"), None),
        P(("seq", "head"), None),
        P(("seq", "head"), None, None),
        P(("seq", "head"), None, None),
        P(("seq", "head"), None, None),
    )
    return jax.shard_map(
        local, mesh=mesh, in_specs=placed, out_specs=P(("seq", "head"), None), check_vma=False
    )
```

```python
import functools
import math

import jax
import jax.numpy as jnp
from jax import lax
from jax.experimental import pallas as pl
from jax.experimental.pallas import tpu as pltpu
from jax.sharding import PartitionSpec as P

HEADS = 32
KV_HEADS = 4
TOP = 8


EPSILON = 1e-06
THETA = 1000000.0
FLOOR = -1e30


def rms_scale(values, gain):
    return values * lax.rsqrt(jnp.mean(values * values, axis=-1, keepdims=True) + EPSILON) * gain


def rotate(values, cosine, sine):
    half = values.shape[-1] // 2
    first = values[..., :half]
    second = values[..., half:]
    return jnp.concatenate(
        [first * cosine - second * sine, second * cosine + first * sine], axis=-1
    )


def doc_index(positions, ends):
    return jnp.sum((positions[:, None] >= ends[None, :]).astype(jnp.int32), axis=1)


def _attend_kernel(bounds_ref, q_ref, own_ref, other_ref, qpos_ref, qstart_ref, o_ref, *, dim):
    heads = q_ref.shape[1] // dim
    tok = q_ref.shape[0]
    block = own_ref.shape[2]
    q = jnp.concatenate([q_ref[:, h * dim : (h + 1) * dim] for h in range(heads)], axis=0)
    qpos = qpos_ref[...]
    qstart = qstart_ref[...]
    scale = dim ** (-0.5)

    def step(j, carry, masked):
        high, total, accum = carry
        mine = j % 2 == bounds_ref[4]
        keys = jnp.where(mine, own_ref[j // 2, 0], other_ref[j // 2, 0])
        values = jnp.where(mine, own_ref[j // 2, 1], other_ref[j // 2, 1])
        scores = lax.dot_general(q, keys, (((1,), (1,)), ((), ())), preferred_element_type=jnp.float32) * scale
        if masked:
            key_pos = j * block + lax.broadcasted_iota(jnp.int32, (1, block), 1)
            allowed = (key_pos >= qstart) & (key_pos <= qpos)
            scores = jnp.where(allowed, scores, FLOOR)
        new_high = jnp.maximum(high, jnp.max(scores, axis=1, keepdims=True))
        weights = jnp.exp(scores - new_high)
        if masked:
            weights = jnp.where(allowed, weights, 0.0)
        factor = jnp.exp(high - new_high)
        total = total * factor + jnp.sum(weights, axis=1, keepdims=True)
        accum = accum * factor + jnp.dot(
            weights.astype(jnp.bfloat16), values, preferred_element_type=jnp.float32
        )
        return new_high, total, accum

    carry = (
        jnp.full((heads * tok, 1), FLOOR, jnp.float32),
        jnp.zeros((heads * tok, 1), jnp.float32),
        jnp.zeros((heads * tok, dim), jnp.float32),
    )
    carry = lax.fori_loop(bounds_ref[0], bounds_ref[1], lambda j, c: step(j, c, True), carry)
    carry = lax.fori_loop(bounds_ref[1], bounds_ref[2], lambda j, c: step(j, c, False), carry)
    carry = lax.fori_loop(bounds_ref[2], bounds_ref[3], lambda j, c: step(j, c, True), carry)
    high, total, accum = carry
    out = (accum / total).astype(o_ref.dtype)
    for h in range(heads):
        o_ref[:, h * dim : (h + 1) * dim] = out[h * tok : (h + 1) * tok]


def attend(bounds, queries, own, other, qpos, qstart):
    tok, width = queries.shape
    dim = own.shape[-1]
    kernel = functools.partial(_attend_kernel, dim=dim)
    spec = pltpu.PrefetchScalarGridSpec(
        num_scalar_prefetch=1,
        grid=(1,),
        in_specs=[
            pl.BlockSpec((tok, width), lambda i, b: (0, 0)),
            pl.BlockSpec(own.shape, lambda i, b: (0, 0, 0, 0)),
            pl.BlockSpec(other.shape, lambda i, b: (0, 0, 0, 0)),
            pl.BlockSpec(qpos.shape, lambda i, b: (0, 0)),
            pl.BlockSpec(qstart.shape, lambda i, b: (0, 0)),
        ],
        out_specs=pl.BlockSpec((tok, width), lambda i, b: (0, 0)),
    )
    return pl.pallas_call(
        kernel, grid_spec=spec, out_shape=jax.ShapeDtypeStruct((tok, width), jnp.bfloat16)
    )(bounds, queries, own, other, qpos, qstart)


def local(
    tokens,
    norm_gain,
    w_query,
    w_key,
    w_value,
    query_gain,
    key_gain,
    w_out,
    post_gain,
    doc_lengths,
    expert_ids,
    route_weights,
    w_gate,
    w_up,
    w_down,
):
    tok_dev, width = tokens.shape
    head_dim = query_gain.shape[0]
    per_dev = w_query.shape[1] // head_dim
    n_seq = lax.axis_size("seq")
    n_head = lax.axis_size("head")
    seq_index = lax.axis_index("seq")
    head_index = lax.axis_index("head")
    ndocs = doc_lengths.shape[0]
    ends = jnp.cumsum(doc_lengths)
    starts = ends - doc_lengths
    positions = seq_index * tok_dev + jnp.arange(tok_dev, dtype=jnp.int32)
    query_doc = doc_index(positions, ends)
    matches = query_doc[:, None] == jnp.arange(ndocs, dtype=jnp.int32)[None, :]
    own_start = jnp.sum(jnp.where(matches, starts[None, :], 0), axis=1)
    offset = (positions - own_start).astype(jnp.float32)
    half = head_dim // 2
    inverse = THETA ** (-2.0 * jnp.arange(half, dtype=jnp.float32) / head_dim)
    angles = offset[:, None] * inverse[None, :]
    cosine = jnp.cos(angles)
    sine = jnp.sin(angles)
    inputs = tokens.astype(jnp.float32)
    normed = rms_scale(inputs, norm_gain).astype(jnp.bfloat16)
    queries = jnp.dot(normed, w_query, preferred_element_type=jnp.float32).reshape(
        tok_dev, per_dev, head_dim
    )
    queries = rotate(rms_scale(queries, query_gain), cosine[:, None, :], sine[:, None, :]).astype(
        jnp.bfloat16
    )
    column = head_index * per_dev // (HEADS // KV_HEADS) * head_dim
    key_cols = lax.dynamic_slice_in_dim(w_key, column, head_dim, 1)
    value_cols = lax.dynamic_slice_in_dim(w_value, column, head_dim, 1)
    keys = rotate(
        rms_scale(jnp.dot(normed, key_cols, preferred_element_type=jnp.float32), key_gain),
        cosine,
        sine,
    ).astype(jnp.bfloat16)
    values = jnp.dot(normed, value_cols, preferred_element_type=jnp.float32).astype(jnp.bfloat16)
    stacked = jnp.stack([keys, values])
    pairs = n_seq // 2
    groups = [[2 * i + c for i in range(pairs)] for c in range(2)]
    spread = jnp.broadcast_to(stacked[None], (pairs,) + stacked.shape)
    same_core = lax.all_to_all(spread, "seq", 0, 0, tiled=True, axis_index_groups=groups)
    block = tok_dev
    low = own_start[0] // block
    high = positions[-1] // block + 1
    inner_low = jnp.clip(-(-own_start[-1] // block), low, high)
    inner_high = jnp.clip((positions[0] + 1) // block, inner_low, high)
    bounds = jnp.stack([low, inner_low, inner_high, high, seq_index % 2]).astype(jnp.int32)
    operands = (
        bounds,
        queries.reshape(tok_dev, per_dev * head_dim),
        jnp.tile(positions[:, None], (per_dev, 1)),
        jnp.tile(own_start[:, None], (per_dev, 1)),
    )
    operands, same_core = lax.optimization_barrier((operands, same_core))
    other_core = lax.ppermute(same_core, "seq", [(i, i ^ 1) for i in range(n_seq)])
    bounds, flat_queries, qpos, qstart = operands
    attended = attend(bounds, flat_queries, same_core, other_core, qpos, qstart)
    rows = tok_dev // n_head
    terms = jnp.dot(attended, w_out, preferred_element_type=jnp.float32).astype(jnp.bfloat16)
    terms = lax.all_to_all(terms.reshape(n_head, rows, width), "head", 0, 0, tiled=True)
    attn_rows = jnp.sum(terms.astype(jnp.float32), axis=0)
    resid = lax.dynamic_slice_in_dim(tokens, head_index * rows, rows, 0).astype(jnp.float32) + attn_rows
    routed = rms_scale(resid, post_gain).astype(jnp.bfloat16)
    experts = n_seq * n_head * w_gate.shape[0]
    capacity = 2 * TOP * rows // experts
    chosen = expert_ids.reshape(-1)
    hits = (chosen[:, None] == jnp.arange(experts, dtype=jnp.int32)[None, :]).astype(jnp.int32)
    rank = jnp.sum((jnp.cumsum(hits, axis=0) - hits) * hits, axis=1)
    slot = rank * experts + chosen
    select = (slot[:, None] == jnp.arange(capacity * experts, dtype=jnp.int32)[None, :]).reshape(
        rows, TOP, capacity * experts
    )
    sources = jnp.transpose(jnp.any(select, axis=1)).astype(jnp.bfloat16)
    outgoing = jnp.dot(sources, routed, preferred_element_type=jnp.float32).astype(jnp.bfloat16)
    outgoing = outgoing.reshape(capacity, experts, width)
    block = lax.all_to_all(outgoing, ("seq", "head"), split_axis=1, concat_axis=1, tiled=True)
    flat = block.reshape(-1, width)
    gate = jnp.dot(flat, w_gate[0], preferred_element_type=jnp.float32)
    up = jnp.dot(flat, w_up[0], preferred_element_type=jnp.float32)
    hidden = (jax.nn.silu(gate) * up).astype(jnp.bfloat16)
    returned = lax.all_to_all(
        jnp.dot(hidden, w_down[0], preferred_element_type=jnp.float32)
        .astype(jnp.bfloat16)
        .reshape(block.shape),
        ("seq", "head"),
        split_axis=1,
        concat_axis=1,
        tiled=True,
    ).reshape(-1, width)
    mixing = jnp.sum(jnp.where(select, route_weights[:, :, None], 0.0), axis=1)
    combined = jnp.dot(
        mixing, returned.astype(jnp.float32), precision=lax.Precision.HIGHEST,
        preferred_element_type=jnp.float32,
    )
    return (resid + combined).astype(jnp.bfloat16)


def solution(mesh):
    placed = (
        P("seq", None),
        P(),
        P(None, "head"),
        P(),
        P(),
        P(),
        P(),
        P("head", None),
        P(),
        P(),
        P(("seq", "head"), None),
        P(("seq", "head"), None),
        P(("seq", "head"), None, None),
        P(("seq", "head"), None, None),
        P(("seq", "head"), None, None),
    )
    return jax.shard_map(
        local, mesh=mesh, in_specs=placed, out_specs=P(("seq", "head"), None), check_vma=False
    )
```

```python
import functools
import math

import jax
import jax.numpy as jnp
from jax import lax
from jax.experimental import pallas as pl
from jax.experimental.pallas import tpu as pltpu
from jax.sharding import PartitionSpec as P

HEADS = 32
KV_HEADS = 4
TOP = 8


EPSILON = 1e-06
THETA = 1000000.0
FLOOR = -1e30


def rms_scale(values, gain):
    return values * lax.rsqrt(jnp.mean(values * values, axis=-1, keepdims=True) + EPSILON) * gain


def rotate(values, cosine, sine):
    half = values.shape[-1] // 2
    first = values[..., :half]
    second = values[..., half:]
    return jnp.concatenate(
        [first * cosine - second * sine, second * cosine + first * sine], axis=-1
    )


def doc_index(positions, ends):
    return jnp.sum((positions[:, None] >= ends[None, :]).astype(jnp.int32), axis=1)


def _attend_kernel(
    bounds_ref, q_ref, cos_ref, sin_ref, gain_ref, own_ref, other_ref, qpos_ref, qstart_ref, o_ref, *, dim
):
    heads = q_ref.shape[1] // dim
    tok = q_ref.shape[0]
    block = own_ref.shape[2]
    parts = []
    for h in range(heads):
        part = q_ref[:, h * dim : (h + 1) * dim]
        part = part * lax.rsqrt(jnp.mean(part * part, axis=1, keepdims=True) + EPSILON) * gain_ref[...]
        part = part * cos_ref[...] + pltpu.roll(part, dim // 2, 1) * sin_ref[...]
        parts.append(part.astype(jnp.bfloat16))
    q = jnp.concatenate(parts, axis=0)
    qpos = qpos_ref[...]
    qstart = qstart_ref[...]
    scale = dim ** (-0.5)

    def step(j, carry, masked):
        high, total, accum = carry
        mine = j % 2 == bounds_ref[4]
        keys = jnp.where(mine, own_ref[j // 2, 0], other_ref[j // 2, 0])
        values = jnp.where(mine, own_ref[j // 2, 1], other_ref[j // 2, 1])
        scores = lax.dot_general(q, keys, (((1,), (1,)), ((), ())), preferred_element_type=jnp.float32) * scale
        if masked:
            key_pos = j * block + lax.broadcasted_iota(jnp.int32, (1, block), 1)
            allowed = (key_pos >= qstart) & (key_pos <= qpos)
            scores = jnp.where(allowed, scores, FLOOR)
        new_high = jnp.maximum(high, jnp.max(scores, axis=1, keepdims=True))
        weights = jnp.exp(scores - new_high)
        if masked:
            weights = jnp.where(allowed, weights, 0.0)
        factor = jnp.exp(high - new_high)
        total = total * factor + jnp.sum(weights, axis=1, keepdims=True)
        accum = accum * factor + jnp.dot(
            weights.astype(jnp.bfloat16), values, preferred_element_type=jnp.float32
        )
        return new_high, total, accum

    carry = (
        jnp.full((heads * tok, 1), FLOOR, jnp.float32),
        jnp.zeros((heads * tok, 1), jnp.float32),
        jnp.zeros((heads * tok, dim), jnp.float32),
    )
    carry = lax.fori_loop(bounds_ref[0], bounds_ref[1], lambda j, c: step(j, c, True), carry)
    carry = lax.fori_loop(bounds_ref[1], bounds_ref[2], lambda j, c: step(j, c, False), carry)
    carry = lax.fori_loop(bounds_ref[2], bounds_ref[3], lambda j, c: step(j, c, True), carry)
    high, total, accum = carry
    out = (accum / total).astype(o_ref.dtype)
    for h in range(heads):
        o_ref[:, h * dim : (h + 1) * dim] = out[h * tok : (h + 1) * tok]


def attend(bounds, queries, cosine, sine, gain, own, other, qpos, qstart):
    tok, width = queries.shape
    dim = own.shape[-1]
    kernel = functools.partial(_attend_kernel, dim=dim)
    spec = pltpu.PrefetchScalarGridSpec(
        num_scalar_prefetch=1,
        grid=(1,),
        in_specs=[
            pl.BlockSpec((tok, width), lambda i, b: (0, 0)),
            pl.BlockSpec(cosine.shape, lambda i, b: (0, 0)),
            pl.BlockSpec(sine.shape, lambda i, b: (0, 0)),
            pl.BlockSpec(gain.shape, lambda i, b: (0, 0)),
            pl.BlockSpec(own.shape, lambda i, b: (0, 0, 0, 0)),
            pl.BlockSpec(other.shape, lambda i, b: (0, 0, 0, 0)),
            pl.BlockSpec(qpos.shape, lambda i, b: (0, 0)),
            pl.BlockSpec(qstart.shape, lambda i, b: (0, 0)),
        ],
        out_specs=pl.BlockSpec((tok, width), lambda i, b: (0, 0)),
    )
    return pl.pallas_call(
        kernel, grid_spec=spec, out_shape=jax.ShapeDtypeStruct((tok, width), jnp.bfloat16)
    )(bounds, queries, cosine, sine, gain, own, other, qpos, qstart)


def local(
    tokens,
    norm_gain,
    w_query,
    w_key,
    w_value,
    query_gain,
    key_gain,
    w_out,
    post_gain,
    doc_lengths,
    expert_ids,
    route_weights,
    w_gate,
    w_up,
    w_down,
):
    tok_dev, width = tokens.shape
    head_dim = query_gain.shape[0]
    per_dev = w_query.shape[1] // head_dim
    n_seq = lax.axis_size("seq")
    n_head = lax.axis_size("head")
    seq_index = lax.axis_index("seq")
    head_index = lax.axis_index("head")
    ndocs = doc_lengths.shape[0]
    ends = jnp.cumsum(doc_lengths)
    starts = ends - doc_lengths
    positions = seq_index * tok_dev + jnp.arange(tok_dev, dtype=jnp.int32)
    query_doc = doc_index(positions, ends)
    matches = query_doc[:, None] == jnp.arange(ndocs, dtype=jnp.int32)[None, :]
    own_start = jnp.sum(jnp.where(matches, starts[None, :], 0), axis=1)
    offset = (positions - own_start).astype(jnp.float32)
    half = head_dim // 2
    inverse = THETA ** (-2.0 * jnp.arange(half, dtype=jnp.float32) / head_dim)
    angles = offset[:, None] * inverse[None, :]
    cosine = jnp.cos(angles)
    sine = jnp.sin(angles)
    inputs = tokens.astype(jnp.float32)
    normed = rms_scale(inputs, norm_gain).astype(jnp.bfloat16)
    queries = jnp.dot(normed, w_query, preferred_element_type=jnp.float32)
    column = head_index * per_dev // (HEADS // KV_HEADS) * head_dim
    key_cols = lax.dynamic_slice_in_dim(w_key, column, head_dim, 1)
    value_cols = lax.dynamic_slice_in_dim(w_value, column, head_dim, 1)
    keys = rotate(
        rms_scale(jnp.dot(normed, key_cols, preferred_element_type=jnp.float32), key_gain),
        cosine,
        sine,
    ).astype(jnp.bfloat16)
    values = jnp.dot(normed, value_cols, preferred_element_type=jnp.float32).astype(jnp.bfloat16)
    stacked = jnp.stack([keys, values])
    pairs = n_seq // 2
    groups = [[2 * i + c for i in range(pairs)] for c in range(2)]
    spread = jnp.broadcast_to(stacked[None], (pairs,) + stacked.shape)
    same_core = lax.all_to_all(spread, "seq", 0, 0, tiled=True, axis_index_groups=groups)
    block = tok_dev
    low = own_start[0] // block
    high = positions[-1] // block + 1
    inner_low = jnp.clip(-(-own_start[-1] // block), low, high)
    inner_high = jnp.clip((positions[0] + 1) // block, inner_low, high)
    bounds = jnp.stack([low, inner_low, inner_high, high, seq_index % 2]).astype(jnp.int32)
    operands = (
        bounds,
        queries,
        jnp.concatenate([cosine, cosine], axis=-1),
        jnp.concatenate([-sine, sine], axis=-1),
        query_gain[None, :],
        jnp.tile(positions[:, None], (per_dev, 1)),
        jnp.tile(own_start[:, None], (per_dev, 1)),
    )
    operands, same_core = lax.optimization_barrier((operands, same_core))
    other_core = lax.ppermute(same_core, "seq", [(i, i ^ 1) for i in range(n_seq)])
    bounds, queries, cosine2, sine2, gain, qpos, qstart = operands
    attended = attend(bounds, queries, cosine2, sine2, gain, same_core, other_core, qpos, qstart)
    rows = tok_dev // n_head
    terms = jnp.dot(attended, w_out, preferred_element_type=jnp.float32).astype(jnp.bfloat16)
    terms = lax.all_to_all(terms.reshape(n_head, rows, width), "head", 0, 0, tiled=True)
    attn_rows = jnp.sum(terms.astype(jnp.float32), axis=0)
    resid = lax.dynamic_slice_in_dim(tokens, head_index * rows, rows, 0).astype(jnp.float32) + attn_rows
    routed = rms_scale(resid, post_gain).astype(jnp.bfloat16)
    experts = n_seq * n_head * w_gate.shape[0]
    capacity = 2 * TOP * rows // experts
    chosen = expert_ids.reshape(-1)
    hits = (chosen[:, None] == jnp.arange(experts, dtype=jnp.int32)[None, :]).astype(jnp.int32)
    rank = jnp.sum((jnp.cumsum(hits, axis=0) - hits) * hits, axis=1)
    slot = rank * experts + chosen
    select = (slot[:, None] == jnp.arange(capacity * experts, dtype=jnp.int32)[None, :]).reshape(
        rows, TOP, capacity * experts
    )
    sources = jnp.transpose(jnp.any(select, axis=1)).astype(jnp.bfloat16)
    outgoing = jnp.dot(sources, routed, preferred_element_type=jnp.float32).astype(jnp.bfloat16)
    outgoing = outgoing.reshape(capacity, experts, width)
    block = lax.all_to_all(outgoing, ("seq", "head"), split_axis=1, concat_axis=1, tiled=True)
    flat = block.reshape(-1, width)
    gate = jnp.dot(flat, w_gate[0], preferred_element_type=jnp.float32)
    up = jnp.dot(flat, w_up[0], preferred_element_type=jnp.float32)
    gate, up = lax.optimization_barrier((gate, up))
    hidden = (jax.nn.silu(gate) * up).astype(jnp.bfloat16)
    returned = lax.all_to_all(
        jnp.dot(hidden, w_down[0], preferred_element_type=jnp.float32)
        .astype(jnp.bfloat16)
        .reshape(block.shape),
        ("seq", "head"),
        split_axis=1,
        concat_axis=1,
        tiled=True,
    ).reshape(-1, width)
    mixing = jnp.sum(jnp.where(select, route_weights[:, :, None], 0.0), axis=1)
    combined = jnp.dot(
        mixing, returned.astype(jnp.float32), precision=lax.Precision.HIGHEST,
        preferred_element_type=jnp.float32,
    )
    return (resid + combined).astype(jnp.bfloat16)


def solution(mesh):
    placed = (
        P("seq", None),
        P(),
        P(None, "head"),
        P(),
        P(),
        P(),
        P(),
        P("head", None),
        P(),
        P(),
        P(("seq", "head"), None),
        P(("seq", "head"), None),
        P(("seq", "head"), None, None),
        P(("seq", "head"), None, None),
        P(("seq", "head"), None, None),
    )
    return jax.shard_map(
        local, mesh=mesh, in_specs=placed, out_specs=P(("seq", "head"), None), check_vma=False
    )
```

```python
import functools
import math

import jax
import jax.numpy as jnp
from jax import lax
from jax.experimental import pallas as pl
from jax.experimental.pallas import tpu as pltpu
from jax.sharding import PartitionSpec as P

HEADS = 32
KV_HEADS = 4
TOP = 8


EPSILON = 1e-06
THETA = 1000000.0
FLOOR = -1e30


def rms_scale(values, gain):
    return values * lax.rsqrt(jnp.mean(values * values, axis=-1, keepdims=True) + EPSILON) * gain


def rotate(values, cosine, sine):
    half = values.shape[-1] // 2
    first = values[..., :half]
    second = values[..., half:]
    return jnp.concatenate(
        [first * cosine - second * sine, second * cosine + first * sine], axis=-1
    )


def doc_index(positions, ends):
    return jnp.sum((positions[:, None] >= ends[None, :]).astype(jnp.int32), axis=1)


def _attend_kernel(
    bounds_ref, q_ref, cos_ref, sin_ref, gain_ref, own_ref, other_ref, qpos_ref, qstart_ref, w_ref, o_ref, *, dim
):
    heads = q_ref.shape[1] // dim
    tok = q_ref.shape[0]
    block = own_ref.shape[2]
    parts = []
    for h in range(heads):
        part = q_ref[:, h * dim : (h + 1) * dim]
        part = part * lax.rsqrt(jnp.mean(part * part, axis=1, keepdims=True) + EPSILON) * gain_ref[...]
        part = part * cos_ref[...] + pltpu.roll(part, dim // 2, 1) * sin_ref[...]
        parts.append(part.astype(jnp.bfloat16))
    q = jnp.concatenate(parts, axis=0)
    qpos = qpos_ref[...]
    qstart = qstart_ref[...]
    scale = dim ** (-0.5)

    def step(j, carry, masked):
        high, total, accum = carry
        mine = j % 2 == bounds_ref[4]
        keys = jnp.where(mine, own_ref[j // 2, 0], other_ref[j // 2, 0])
        values = jnp.where(mine, own_ref[j // 2, 1], other_ref[j // 2, 1])
        scores = lax.dot_general(q, keys, (((1,), (1,)), ((), ())), preferred_element_type=jnp.float32) * scale
        if masked:
            key_pos = j * block + lax.broadcasted_iota(jnp.int32, (1, block), 1)
            allowed = (key_pos >= qstart) & (key_pos <= qpos)
            scores = jnp.where(allowed, scores, FLOOR)
        new_high = jnp.maximum(high, jnp.max(scores, axis=1, keepdims=True))
        weights = jnp.exp(scores - new_high)
        if masked:
            weights = jnp.where(allowed, weights, 0.0)
        factor = jnp.exp(high - new_high)
        total = total * factor + jnp.sum(weights, axis=1, keepdims=True)
        accum = accum * factor + jnp.dot(
            weights.astype(jnp.bfloat16), values, preferred_element_type=jnp.float32
        )
        return new_high, total, accum

    carry = (
        jnp.full((heads * tok, 1), FLOOR, jnp.float32),
        jnp.zeros((heads * tok, 1), jnp.float32),
        jnp.zeros((heads * tok, dim), jnp.float32),
    )
    carry = lax.fori_loop(bounds_ref[0], bounds_ref[1], lambda j, c: step(j, c, True), carry)
    carry = lax.fori_loop(bounds_ref[1], bounds_ref[2], lambda j, c: step(j, c, False), carry)
    carry = lax.fori_loop(bounds_ref[2], bounds_ref[3], lambda j, c: step(j, c, True), carry)
    high, total, accum = carry
    out = (accum / total).astype(jnp.bfloat16)
    terms = jnp.dot(out[:tok], w_ref[:dim, :], preferred_element_type=jnp.float32)
    for h in range(1, heads):
        terms = terms + jnp.dot(
            out[h * tok : (h + 1) * tok], w_ref[h * dim : (h + 1) * dim, :], preferred_element_type=jnp.float32
        )
    o_ref[...] = terms.astype(o_ref.dtype)


def attend(bounds, queries, cosine, sine, gain, own, other, qpos, qstart, w_out):
    tok, width = queries.shape
    dim = own.shape[-1]
    kernel = functools.partial(_attend_kernel, dim=dim)
    spec = pltpu.PrefetchScalarGridSpec(
        num_scalar_prefetch=1,
        grid=(1,),
        in_specs=[
            pl.BlockSpec((tok, width), lambda i, b: (0, 0)),
            pl.BlockSpec(cosine.shape, lambda i, b: (0, 0)),
            pl.BlockSpec(sine.shape, lambda i, b: (0, 0)),
            pl.BlockSpec(gain.shape, lambda i, b: (0, 0)),
            pl.BlockSpec(own.shape, lambda i, b: (0, 0, 0, 0)),
            pl.BlockSpec(other.shape, lambda i, b: (0, 0, 0, 0)),
            pl.BlockSpec(qpos.shape, lambda i, b: (0, 0)),
            pl.BlockSpec(qstart.shape, lambda i, b: (0, 0)),
            pl.BlockSpec(w_out.shape, lambda i, b: (0, 0)),
        ],
        out_specs=pl.BlockSpec((tok, w_out.shape[1]), lambda i, b: (0, 0)),
    )
    return pl.pallas_call(
        kernel, grid_spec=spec, out_shape=jax.ShapeDtypeStruct((tok, w_out.shape[1]), jnp.bfloat16)
    )(bounds, queries, cosine, sine, gain, own, other, qpos, qstart, w_out)


def local(
    tokens,
    norm_gain,
    w_query,
    w_key,
    w_value,
    query_gain,
    key_gain,
    w_out,
    post_gain,
    doc_lengths,
    expert_ids,
    route_weights,
    w_gate,
    w_up,
    w_down,
):
    tok_dev, width = tokens.shape
    head_dim = query_gain.shape[0]
    per_dev = w_query.shape[1] // head_dim
    n_seq = lax.axis_size("seq")
    n_head = lax.axis_size("head")
    seq_index = lax.axis_index("seq")
    head_index = lax.axis_index("head")
    ndocs = doc_lengths.shape[0]
    ends = jnp.cumsum(doc_lengths)
    starts = ends - doc_lengths
    positions = seq_index * tok_dev + jnp.arange(tok_dev, dtype=jnp.int32)
    query_doc = doc_index(positions, ends)
    matches = query_doc[:, None] == jnp.arange(ndocs, dtype=jnp.int32)[None, :]
    own_start = jnp.sum(jnp.where(matches, starts[None, :], 0), axis=1)
    offset = (positions - own_start).astype(jnp.float32)
    half = head_dim // 2
    inverse = THETA ** (-2.0 * jnp.arange(half, dtype=jnp.float32) / head_dim)
    angles = offset[:, None] * inverse[None, :]
    cosine = jnp.cos(angles)
    sine = jnp.sin(angles)
    inputs = tokens.astype(jnp.float32)
    normed = rms_scale(inputs, norm_gain).astype(jnp.bfloat16)
    queries = jnp.dot(normed, w_query, preferred_element_type=jnp.float32)
    column = head_index * per_dev // (HEADS // KV_HEADS) * head_dim
    key_cols = lax.dynamic_slice_in_dim(w_key, column, head_dim, 1)
    value_cols = lax.dynamic_slice_in_dim(w_value, column, head_dim, 1)
    keys = rotate(
        rms_scale(jnp.dot(normed, key_cols, preferred_element_type=jnp.float32), key_gain),
        cosine,
        sine,
    ).astype(jnp.bfloat16)
    values = jnp.dot(normed, value_cols, preferred_element_type=jnp.float32).astype(jnp.bfloat16)
    stacked = jnp.stack([keys, values])
    pairs = n_seq // 2
    groups = [[2 * i + c for i in range(pairs)] for c in range(2)]
    spread = jnp.broadcast_to(stacked[None], (pairs,) + stacked.shape)
    same_core = lax.all_to_all(spread, "seq", 0, 0, tiled=True, axis_index_groups=groups)
    block = tok_dev
    low = own_start[0] // block
    high = positions[-1] // block + 1
    inner_low = jnp.clip(-(-own_start[-1] // block), low, high)
    inner_high = jnp.clip((positions[0] + 1) // block, inner_low, high)
    bounds = jnp.stack([low, inner_low, inner_high, high, seq_index % 2]).astype(jnp.int32)
    operands = (
        bounds,
        queries,
        jnp.concatenate([cosine, cosine], axis=-1),
        jnp.concatenate([-sine, sine], axis=-1),
        query_gain[None, :],
        jnp.tile(positions[:, None], (per_dev, 1)),
        jnp.tile(own_start[:, None], (per_dev, 1)),
    )
    operands, same_core = lax.optimization_barrier((operands, same_core))
    other_core = lax.ppermute(same_core, "seq", [(i, i ^ 1) for i in range(n_seq)])
    bounds, queries, cosine2, sine2, gain, qpos, qstart = operands
    terms = attend(bounds, queries, cosine2, sine2, gain, same_core, other_core, qpos, qstart, w_out)
    rows = tok_dev // n_head
    terms = lax.all_to_all(terms.reshape(n_head, rows, width), "head", 0, 0, tiled=True)
    attn_rows = jnp.sum(terms.astype(jnp.float32), axis=0)
    resid = lax.dynamic_slice_in_dim(tokens, head_index * rows, rows, 0).astype(jnp.float32) + attn_rows
    routed = rms_scale(resid, post_gain).astype(jnp.bfloat16)
    experts = n_seq * n_head * w_gate.shape[0]
    capacity = 2 * TOP * rows // experts
    chosen = expert_ids.reshape(-1)
    hits = (chosen[:, None] == jnp.arange(experts, dtype=jnp.int32)[None, :]).astype(jnp.int32)
    rank = jnp.sum((jnp.cumsum(hits, axis=0) - hits) * hits, axis=1)
    slot = rank * experts + chosen
    select = (slot[:, None] == jnp.arange(capacity * experts, dtype=jnp.int32)[None, :]).reshape(
        rows, TOP, capacity * experts
    )
    sources = jnp.transpose(jnp.any(select, axis=1)).astype(jnp.bfloat16)
    outgoing = jnp.dot(sources, routed, preferred_element_type=jnp.float32).astype(jnp.bfloat16)
    outgoing = outgoing.reshape(capacity, experts, width)
    block = lax.all_to_all(outgoing, ("seq", "head"), split_axis=1, concat_axis=1, tiled=True)
    flat = block.reshape(-1, width)
    gate = jnp.dot(flat, w_gate[0], preferred_element_type=jnp.float32)
    up = jnp.dot(flat, w_up[0], preferred_element_type=jnp.float32)
    gate, up = lax.optimization_barrier((gate, up))
    hidden = (jax.nn.silu(gate) * up).astype(jnp.bfloat16)
    returned = lax.all_to_all(
        jnp.dot(hidden, w_down[0], preferred_element_type=jnp.float32)
        .astype(jnp.bfloat16)
        .reshape(block.shape),
        ("seq", "head"),
        split_axis=1,
        concat_axis=1,
        tiled=True,
    ).reshape(-1, width)
    mixing = jnp.sum(jnp.where(select, route_weights[:, :, None], 0.0), axis=1)
    combined = jnp.dot(
        mixing, returned.astype(jnp.float32), precision=lax.Precision.HIGHEST,
        preferred_element_type=jnp.float32,
    )
    return (resid + combined).astype(jnp.bfloat16)


def solution(mesh):
    placed = (
        P("seq", None),
        P(),
        P(None, "head"),
        P(),
        P(),
        P(),
        P(),
        P("head", None),
        P(),
        P(),
        P(("seq", "head"), None),
        P(("seq", "head"), None),
        P(("seq", "head"), None, None),
        P(("seq", "head"), None, None),
        P(("seq", "head"), None, None),
    )
    return jax.shard_map(
        local, mesh=mesh, in_specs=placed, out_specs=P(("seq", "head"), None), check_vma=False
    )
```

```python
import functools
import math

import jax
import jax.numpy as jnp
from jax import lax
from jax.experimental import pallas as pl
from jax.experimental.pallas import tpu as pltpu
from jax.sharding import PartitionSpec as P

HEADS = 32
KV_HEADS = 4
TOP = 8


EPSILON = 1e-06
THETA = 1000000.0
FLOOR = -1e30


def rms_scale(values, gain):
    return values * lax.rsqrt(jnp.mean(values * values, axis=-1, keepdims=True) + EPSILON) * gain


def rotate(values, cosine, sine):
    half = values.shape[-1] // 2
    first = values[..., :half]
    second = values[..., half:]
    return jnp.concatenate(
        [first * cosine - second * sine, second * cosine + first * sine], axis=-1
    )


def doc_index(positions, ends):
    return jnp.sum((positions[:, None] >= ends[None, :]).astype(jnp.int32), axis=1)


def _attend_kernel(
    bounds_ref, q_ref, cos_ref, sin_ref, gain_ref, own_ref, other_ref, qpos_ref, qstart_ref, w_ref, o_ref, *, dim
):
    heads = q_ref.shape[1] // dim
    tok = q_ref.shape[0]
    block = 2 * own_ref.shape[2]
    parts = []
    for h in range(heads):
        part = q_ref[:, h * dim : (h + 1) * dim]
        part = part * lax.rsqrt(jnp.mean(part * part, axis=1, keepdims=True) + EPSILON) * gain_ref[...]
        part = part * cos_ref[...] + pltpu.roll(part, dim // 2, 1) * sin_ref[...]
        parts.append(part.astype(jnp.bfloat16))
    q = jnp.concatenate(parts, axis=0)
    qpos = qpos_ref[...]
    qstart = qstart_ref[...]
    scale = dim ** (-0.5)

    def step(j, carry, masked):
        high, total, accum = carry
        even = bounds_ref[4] == 0
        keys = jnp.concatenate(
            [jnp.where(even, own_ref[j, 0], other_ref[j, 0]), jnp.where(even, other_ref[j, 0], own_ref[j, 0])],
            axis=0,
        )
        values = jnp.concatenate(
            [jnp.where(even, own_ref[j, 1], other_ref[j, 1]), jnp.where(even, other_ref[j, 1], own_ref[j, 1])],
            axis=0,
        )
        scores = lax.dot_general(q, keys, (((1,), (1,)), ((), ())), preferred_element_type=jnp.float32) * scale
        if masked:
            key_pos = j * block + lax.broadcasted_iota(jnp.int32, (1, block), 1)
            allowed = (key_pos >= qstart) & (key_pos <= qpos)
            scores = jnp.where(allowed, scores, FLOOR)
        new_high = jnp.maximum(high, jnp.max(scores, axis=1, keepdims=True))
        weights = jnp.exp(scores - new_high)
        if masked:
            weights = jnp.where(allowed, weights, 0.0)
        factor = jnp.exp(high - new_high)
        total = total * factor + jnp.sum(weights, axis=1, keepdims=True)
        accum = accum * factor + jnp.dot(
            weights.astype(jnp.bfloat16), values, preferred_element_type=jnp.float32
        )
        return new_high, total, accum

    carry = (
        jnp.full((heads * tok, 1), FLOOR, jnp.float32),
        jnp.zeros((heads * tok, 1), jnp.float32),
        jnp.zeros((heads * tok, dim), jnp.float32),
    )
    carry = lax.fori_loop(bounds_ref[0], bounds_ref[1], lambda j, c: step(j, c, True), carry)
    carry = lax.fori_loop(bounds_ref[1], bounds_ref[2], lambda j, c: step(j, c, False), carry)
    carry = lax.fori_loop(bounds_ref[2], bounds_ref[3], lambda j, c: step(j, c, True), carry)
    high, total, accum = carry
    out = (accum / total).astype(jnp.bfloat16)
    terms = jnp.dot(out[:tok], w_ref[:dim, :], preferred_element_type=jnp.float32)
    for h in range(1, heads):
        terms = terms + jnp.dot(
            out[h * tok : (h + 1) * tok], w_ref[h * dim : (h + 1) * dim, :], preferred_element_type=jnp.float32
        )
    o_ref[...] = terms.astype(o_ref.dtype)


def attend(bounds, queries, cosine, sine, gain, own, other, qpos, qstart, w_out):
    tok, width = queries.shape
    dim = own.shape[-1]
    kernel = functools.partial(_attend_kernel, dim=dim)
    spec = pltpu.PrefetchScalarGridSpec(
        num_scalar_prefetch=1,
        grid=(1,),
        in_specs=[
            pl.BlockSpec((tok, width), lambda i, b: (0, 0)),
            pl.BlockSpec(cosine.shape, lambda i, b: (0, 0)),
            pl.BlockSpec(sine.shape, lambda i, b: (0, 0)),
            pl.BlockSpec(gain.shape, lambda i, b: (0, 0)),
            pl.BlockSpec(own.shape, lambda i, b: (0, 0, 0, 0)),
            pl.BlockSpec(other.shape, lambda i, b: (0, 0, 0, 0)),
            pl.BlockSpec(qpos.shape, lambda i, b: (0, 0)),
            pl.BlockSpec(qstart.shape, lambda i, b: (0, 0)),
            pl.BlockSpec(w_out.shape, lambda i, b: (0, 0)),
        ],
        out_specs=pl.BlockSpec((tok, w_out.shape[1]), lambda i, b: (0, 0)),
    )
    return pl.pallas_call(
        kernel, grid_spec=spec, out_shape=jax.ShapeDtypeStruct((tok, w_out.shape[1]), jnp.bfloat16)
    )(bounds, queries, cosine, sine, gain, own, other, qpos, qstart, w_out)


def local(
    tokens,
    norm_gain,
    w_query,
    w_key,
    w_value,
    query_gain,
    key_gain,
    w_out,
    post_gain,
    doc_lengths,
    expert_ids,
    route_weights,
    w_gate,
    w_up,
    w_down,
):
    tok_dev, width = tokens.shape
    head_dim = query_gain.shape[0]
    per_dev = w_query.shape[1] // head_dim
    n_seq = lax.axis_size("seq")
    n_head = lax.axis_size("head")
    seq_index = lax.axis_index("seq")
    head_index = lax.axis_index("head")
    ndocs = doc_lengths.shape[0]
    ends = jnp.cumsum(doc_lengths)
    starts = ends - doc_lengths
    positions = seq_index * tok_dev + jnp.arange(tok_dev, dtype=jnp.int32)
    query_doc = doc_index(positions, ends)
    matches = query_doc[:, None] == jnp.arange(ndocs, dtype=jnp.int32)[None, :]
    own_start = jnp.sum(jnp.where(matches, starts[None, :], 0), axis=1)
    offset = (positions - own_start).astype(jnp.float32)
    half = head_dim // 2
    inverse = THETA ** (-2.0 * jnp.arange(half, dtype=jnp.float32) / head_dim)
    angles = offset[:, None] * inverse[None, :]
    cosine = jnp.cos(angles)
    sine = jnp.sin(angles)
    inputs = tokens.astype(jnp.float32)
    normed = rms_scale(inputs, norm_gain).astype(jnp.bfloat16)
    queries = jnp.dot(normed, w_query, preferred_element_type=jnp.float32)
    column = head_index * per_dev // (HEADS // KV_HEADS) * head_dim
    key_cols = lax.dynamic_slice_in_dim(w_key, column, head_dim, 1)
    value_cols = lax.dynamic_slice_in_dim(w_value, column, head_dim, 1)
    keys = rotate(
        rms_scale(jnp.dot(normed, key_cols, preferred_element_type=jnp.float32), key_gain),
        cosine,
        sine,
    ).astype(jnp.bfloat16)
    values = jnp.dot(normed, value_cols, preferred_element_type=jnp.float32).astype(jnp.bfloat16)
    stacked = jnp.stack([keys, values])
    pairs = n_seq // 2
    groups = [[2 * i + c for i in range(pairs)] for c in range(2)]
    spread = jnp.broadcast_to(stacked[None], (pairs,) + stacked.shape)
    same_core = lax.all_to_all(spread, "seq", 0, 0, tiled=True, axis_index_groups=groups)
    block = 2 * tok_dev
    low = own_start[0] // block
    high = positions[-1] // block + 1
    inner_low = jnp.clip(-(-own_start[-1] // block), low, high)
    inner_high = jnp.clip((positions[0] + 1) // block, inner_low, high)
    bounds = jnp.stack([low, inner_low, inner_high, high, seq_index % 2]).astype(jnp.int32)
    operands = (
        bounds,
        queries,
        jnp.concatenate([cosine, cosine], axis=-1),
        jnp.concatenate([-sine, sine], axis=-1),
        query_gain[None, :],
        jnp.tile(positions[:, None], (per_dev, 1)),
        jnp.tile(own_start[:, None], (per_dev, 1)),
    )
    operands, same_core = lax.optimization_barrier((operands, same_core))
    other_core = lax.ppermute(same_core, "seq", [(i, i ^ 1) for i in range(n_seq)])
    bounds, queries, cosine2, sine2, gain, qpos, qstart = operands
    terms = attend(bounds, queries, cosine2, sine2, gain, same_core, other_core, qpos, qstart, w_out)
    rows = tok_dev // n_head
    terms = lax.all_to_all(terms.reshape(n_head, rows, width), "head", 0, 0, tiled=True)
    attn_rows = jnp.sum(terms.astype(jnp.float32), axis=0)
    resid = lax.dynamic_slice_in_dim(tokens, head_index * rows, rows, 0).astype(jnp.float32) + attn_rows
    routed = rms_scale(resid, post_gain).astype(jnp.bfloat16)
    experts = n_seq * n_head * w_gate.shape[0]
    capacity = 2 * TOP * rows // experts
    chosen = expert_ids.reshape(-1)
    hits = (chosen[:, None] == jnp.arange(experts, dtype=jnp.int32)[None, :]).astype(jnp.int32)
    rank = jnp.sum((jnp.cumsum(hits, axis=0) - hits) * hits, axis=1)
    slot = rank * experts + chosen
    select = (slot[:, None] == jnp.arange(capacity * experts, dtype=jnp.int32)[None, :]).reshape(
        rows, TOP, capacity * experts
    )
    sources = jnp.transpose(jnp.any(select, axis=1)).astype(jnp.bfloat16)
    outgoing = jnp.dot(sources, routed, preferred_element_type=jnp.float32).astype(jnp.bfloat16)
    outgoing = outgoing.reshape(capacity, experts, width)
    block = lax.all_to_all(outgoing, ("seq", "head"), split_axis=1, concat_axis=1, tiled=True)
    flat = block.reshape(-1, width)
    gate = jnp.dot(flat, w_gate[0], preferred_element_type=jnp.float32)
    up = jnp.dot(flat, w_up[0], preferred_element_type=jnp.float32)
    gate, up = lax.optimization_barrier((gate, up))
    hidden = (jax.nn.silu(gate) * up).astype(jnp.bfloat16)
    returned = lax.all_to_all(
        jnp.dot(hidden, w_down[0], preferred_element_type=jnp.float32)
        .astype(jnp.bfloat16)
        .reshape(block.shape),
        ("seq", "head"),
        split_axis=1,
        concat_axis=1,
        tiled=True,
    ).reshape(-1, width)
    mixing = jnp.sum(jnp.where(select, route_weights[:, :, None], 0.0), axis=1)
    combined = jnp.dot(
        mixing, returned.astype(jnp.float32), precision=lax.Precision.HIGHEST,
        preferred_element_type=jnp.float32,
    )
    return (resid + combined).astype(jnp.bfloat16)


def solution(mesh):
    placed = (
        P("seq", None),
        P(),
        P(None, "head"),
        P(),
        P(),
        P(),
        P(),
        P("head", None),
        P(),
        P(),
        P(("seq", "head"), None),
        P(("seq", "head"), None),
        P(("seq", "head"), None, None),
        P(("seq", "head"), None, None),
        P(("seq", "head"), None, None),
    )
    return jax.shard_map(
        local, mesh=mesh, in_specs=placed, out_specs=P(("seq", "head"), None), check_vma=False
    )
```

```python
import functools
import math

import jax
import jax.numpy as jnp
from jax import lax
from jax.experimental import pallas as pl
from jax.experimental.pallas import tpu as pltpu
from jax.sharding import PartitionSpec as P

HEADS = 32
KV_HEADS = 4
TOP = 8


EPSILON = 1e-06
THETA = 1000000.0
FLOOR = -1e30


def rms_scale(values, gain):
    return values * lax.rsqrt(jnp.mean(values * values, axis=-1, keepdims=True) + EPSILON) * gain


def rotate(values, cosine, sine):
    half = values.shape[-1] // 2
    first = values[..., :half]
    second = values[..., half:]
    return jnp.concatenate(
        [first * cosine - second * sine, second * cosine + first * sine], axis=-1
    )


def doc_index(positions, ends):
    return jnp.sum((positions[:, None] >= ends[None, :]).astype(jnp.int32), axis=1)


def _attend_kernel(
    bounds_ref, q_ref, cos_ref, sin_ref, gain_ref, own_ref, other_ref, qpos_ref, qstart_ref, w_ref, o_ref, *, dim
):
    heads = q_ref.shape[1] // dim
    tok = q_ref.shape[0]
    block = 2 * own_ref.shape[2]
    parts = []
    for h in range(heads):
        part = q_ref[:, h * dim : (h + 1) * dim]
        part = part * lax.rsqrt(jnp.mean(part * part, axis=1, keepdims=True) + EPSILON) * gain_ref[...]
        part = part * cos_ref[...] + pltpu.roll(part, dim // 2, 1) * sin_ref[...]
        parts.append(part.astype(jnp.bfloat16))
    q = jnp.concatenate(parts, axis=0)
    qpos = qpos_ref[...]
    qstart = qstart_ref[...]
    scale = dim ** (-0.5)

    def step(j, carry, masked):
        high, total, accum = carry
        even = bounds_ref[4] == 0
        keys = jnp.concatenate(
            [jnp.where(even, own_ref[j, 0], other_ref[j, 0]), jnp.where(even, other_ref[j, 0], own_ref[j, 0])],
            axis=0,
        )
        values = jnp.concatenate(
            [jnp.where(even, own_ref[j, 1], other_ref[j, 1]), jnp.where(even, other_ref[j, 1], own_ref[j, 1])],
            axis=0,
        )
        scores = lax.dot_general(q, keys, (((1,), (1,)), ((), ())), preferred_element_type=jnp.float32) * scale
        if masked:
            key_pos = j * block + lax.broadcasted_iota(jnp.int32, (1, block), 1)
            allowed = (key_pos >= qstart) & (key_pos <= qpos)
            scores = jnp.where(allowed, scores, FLOOR)
        new_high = jnp.maximum(high, jnp.max(scores, axis=1, keepdims=True))
        weights = jnp.exp(scores - new_high)
        if masked:
            weights = jnp.where(allowed, weights, 0.0)
        factor = jnp.exp(high - new_high)
        total = total * factor + jnp.sum(weights, axis=1, keepdims=True)
        accum = accum * factor + jnp.dot(
            weights.astype(jnp.bfloat16), values, preferred_element_type=jnp.float32
        )
        return new_high, total, accum

    carry = (
        jnp.full((heads * tok, 1), FLOOR, jnp.float32),
        jnp.zeros((heads * tok, 1), jnp.float32),
        jnp.zeros((heads * tok, dim), jnp.float32),
    )
    carry = lax.fori_loop(bounds_ref[0], bounds_ref[1], lambda j, c: step(j, c, True), carry)
    carry = lax.fori_loop(bounds_ref[1], bounds_ref[2], lambda j, c: step(j, c, False), carry)
    carry = lax.fori_loop(bounds_ref[2], bounds_ref[3], lambda j, c: step(j, c, True), carry)
    high, total, accum = carry
    out = (accum / total).astype(jnp.bfloat16)
    terms = jnp.dot(out[:tok], w_ref[:dim, :], preferred_element_type=jnp.float32)
    for h in range(1, heads):
        terms = terms + jnp.dot(
            out[h * tok : (h + 1) * tok], w_ref[h * dim : (h + 1) * dim, :], preferred_element_type=jnp.float32
        )
    o_ref[...] = terms.astype(o_ref.dtype)


def attend(bounds, queries, cosine, sine, gain, own, other, qpos, qstart, w_out):
    tok, width = queries.shape
    dim = own.shape[-1]
    kernel = functools.partial(_attend_kernel, dim=dim)
    spec = pltpu.PrefetchScalarGridSpec(
        num_scalar_prefetch=1,
        grid=(1,),
        in_specs=[
            pl.BlockSpec((tok, width), lambda i, b: (0, 0)),
            pl.BlockSpec(cosine.shape, lambda i, b: (0, 0)),
            pl.BlockSpec(sine.shape, lambda i, b: (0, 0)),
            pl.BlockSpec(gain.shape, lambda i, b: (0, 0)),
            pl.BlockSpec(own.shape, lambda i, b: (0, 0, 0, 0)),
            pl.BlockSpec(other.shape, lambda i, b: (0, 0, 0, 0)),
            pl.BlockSpec(qpos.shape, lambda i, b: (0, 0)),
            pl.BlockSpec(qstart.shape, lambda i, b: (0, 0)),
            pl.BlockSpec(w_out.shape, lambda i, b: (0, 0)),
        ],
        out_specs=pl.BlockSpec((tok, w_out.shape[1]), lambda i, b: (0, 0)),
    )
    return pl.pallas_call(
        kernel, grid_spec=spec, out_shape=jax.ShapeDtypeStruct((tok, w_out.shape[1]), jnp.bfloat16)
    )(bounds, queries, cosine, sine, gain, own, other, qpos, qstart, w_out)


def local(
    tokens,
    norm_gain,
    w_query,
    w_key,
    w_value,
    query_gain,
    key_gain,
    w_out,
    post_gain,
    doc_lengths,
    expert_ids,
    route_weights,
    w_gate,
    w_up,
    w_down,
):
    tok_dev, width = tokens.shape
    head_dim = query_gain.shape[0]
    per_dev = w_query.shape[1] // head_dim
    n_seq = lax.axis_size("seq")
    n_head = lax.axis_size("head")
    seq_index = lax.axis_index("seq")
    head_index = lax.axis_index("head")
    ndocs = doc_lengths.shape[0]
    ends = jnp.cumsum(doc_lengths)
    starts = ends - doc_lengths
    positions = seq_index * tok_dev + jnp.arange(tok_dev, dtype=jnp.int32)
    query_doc = doc_index(positions, ends)
    matches = query_doc[:, None] == jnp.arange(ndocs, dtype=jnp.int32)[None, :]
    own_start = jnp.sum(jnp.where(matches, starts[None, :], 0), axis=1)
    offset = (positions - own_start).astype(jnp.float32)
    half = head_dim // 2
    inverse = THETA ** (-2.0 * jnp.arange(half, dtype=jnp.float32) / head_dim)
    angles = offset[:, None] * inverse[None, :]
    cosine = jnp.cos(angles)
    sine = jnp.sin(angles)
    inputs = tokens.astype(jnp.float32)
    normed = rms_scale(inputs, norm_gain).astype(jnp.bfloat16)
    queries = jnp.dot(normed, w_query, preferred_element_type=jnp.float32)
    column = head_index * per_dev // (HEADS // KV_HEADS) * head_dim
    key_cols = lax.dynamic_slice_in_dim(w_key, column, head_dim, 1)
    value_cols = lax.dynamic_slice_in_dim(w_value, column, head_dim, 1)
    keys = rotate(
        rms_scale(jnp.dot(normed, key_cols, preferred_element_type=jnp.float32), key_gain),
        cosine,
        sine,
    ).astype(jnp.bfloat16)
    values = jnp.dot(normed, value_cols, preferred_element_type=jnp.float32).astype(jnp.bfloat16)
    stacked = jnp.stack([keys, values])
    pairs = n_seq // 2
    groups = [[2 * i + c for i in range(pairs)] for c in range(2)]
    spread = jnp.broadcast_to(stacked[None], (pairs,) + stacked.shape)
    same_core = lax.all_to_all(spread, "seq", 0, 0, tiled=True, axis_index_groups=groups)
    block = 2 * tok_dev
    low = own_start[0] // block
    high = positions[-1] // block + 1
    inner_low = jnp.clip(-(-own_start[-1] // block), low, high)
    inner_high = jnp.clip((positions[0] + 1) // block, inner_low, high)
    bounds = jnp.stack([low, inner_low, inner_high, high, seq_index % 2]).astype(jnp.int32)
    operands = (
        bounds,
        queries,
        jnp.concatenate([cosine, cosine], axis=-1),
        jnp.concatenate([-sine, sine], axis=-1),
        query_gain[None, :],
        jnp.tile(positions[:, None], (per_dev, 1)),
        jnp.tile(own_start[:, None], (per_dev, 1)),
    )
    operands, same_core = lax.optimization_barrier((operands, same_core))
    other_core = lax.ppermute(same_core, "seq", [(i, i ^ 1) for i in range(n_seq)])
    bounds, queries, cosine2, sine2, gain, qpos, qstart = operands
    terms = attend(bounds, queries, cosine2, sine2, gain, same_core, other_core, qpos, qstart, w_out)
    rows = tok_dev // n_head
    terms = lax.all_to_all(terms.reshape(n_head, rows, width), "head", 0, 0, tiled=True)
    attn_rows = jnp.sum(terms.astype(jnp.float32), axis=0)
    resid = lax.dynamic_slice_in_dim(tokens, head_index * rows, rows, 0).astype(jnp.float32) + attn_rows
    routed = rms_scale(resid, post_gain).astype(jnp.bfloat16)
    experts = n_seq * n_head * w_gate.shape[0]
    capacity = 2 * TOP * rows // experts
    chosen = expert_ids.reshape(-1)
    hits = (chosen[:, None] == jnp.arange(experts, dtype=jnp.int32)[None, :]).astype(jnp.int32)
    rank = jnp.sum((jnp.cumsum(hits, axis=0) - hits) * hits, axis=1)
    slot = chosen * capacity + rank
    select = (slot[:, None] == jnp.arange(experts * capacity, dtype=jnp.int32)[None, :]).reshape(
        rows, TOP, experts, capacity
    )
    sources = jnp.any(select, axis=1).astype(jnp.bfloat16)
    outgoing = lax.dot_general(
        sources, routed, (((0,), (0,)), ((), ())), preferred_element_type=jnp.float32
    ).astype(jnp.bfloat16)
    block = lax.all_to_all(outgoing, ("seq", "head"), split_axis=0, concat_axis=0, tiled=True)
    gate = jnp.einsum("scd,df->scf", block, w_gate[0], preferred_element_type=jnp.float32)
    up = jnp.einsum("scd,df->scf", block, w_up[0], preferred_element_type=jnp.float32)
    gate, up = lax.optimization_barrier((gate, up))
    hidden = (jax.nn.silu(gate) * up).astype(jnp.bfloat16)
    down = jnp.einsum("scf,fd->scd", hidden, w_down[0], preferred_element_type=jnp.float32)
    returned = lax.all_to_all(
        down.astype(jnp.bfloat16), ("seq", "head"), split_axis=0, concat_axis=0, tiled=True
    )
    mixing = jnp.sum(jnp.where(select, route_weights[:, :, None, None], 0.0), axis=1)
    combined = lax.dot_general(
        mixing,
        returned.astype(jnp.float32),
        (((1, 2), (0, 1)), ((), ())),
        precision=lax.Precision.HIGHEST,
        preferred_element_type=jnp.float32,
    )
    return (resid + combined).astype(jnp.bfloat16)


def solution(mesh):
    placed = (
        P("seq", None),
        P(),
        P(None, "head"),
        P(),
        P(),
        P(),
        P(),
        P("head", None),
        P(),
        P(),
        P(("seq", "head"), None),
        P(("seq", "head"), None),
        P(("seq", "head"), None, None),
        P(("seq", "head"), None, None),
        P(("seq", "head"), None, None),
    )
    return jax.shard_map(
        local, mesh=mesh, in_specs=placed, out_specs=P(("seq", "head"), None), check_vma=False
    )
```

```python
import functools
import math

import jax
import jax.numpy as jnp
from jax import lax
from jax.experimental import pallas as pl
from jax.experimental.pallas import tpu as pltpu
from jax.sharding import PartitionSpec as P

HEADS = 32
KV_HEADS = 4
TOP = 8


EPSILON = 1e-06
THETA = 1000000.0
FLOOR = -1e30


def rms_scale(values, gain):
    return values * lax.rsqrt(jnp.mean(values * values, axis=-1, keepdims=True) + EPSILON) * gain


def rotate(values, cosine, sine):
    half = values.shape[-1] // 2
    first = values[..., :half]
    second = values[..., half:]
    return jnp.concatenate(
        [first * cosine - second * sine, second * cosine + first * sine], axis=-1
    )


def doc_index(positions, ends):
    return jnp.sum((positions[:, None] >= ends[None, :]).astype(jnp.int32), axis=1)


def _attend_kernel(
    bounds_ref, q_ref, cos_ref, sin_ref, gain_ref, own_ref, other_ref, qpos_ref, qstart_ref, w_ref, o_ref, *, dim
):
    heads = q_ref.shape[1] // dim
    tok = q_ref.shape[0]
    block = 2 * own_ref.shape[2]
    parts = []
    for h in range(heads):
        part = q_ref[:, h * dim : (h + 1) * dim]
        part = part * lax.rsqrt(jnp.mean(part * part, axis=1, keepdims=True) + EPSILON) * gain_ref[...]
        part = part * cos_ref[...] + pltpu.roll(part, dim // 2, 1) * sin_ref[...]
        parts.append(part.astype(jnp.bfloat16))
    q = jnp.concatenate(parts, axis=0)
    qpos = qpos_ref[...]
    qstart = qstart_ref[...]
    scale = dim ** (-0.5)

    def step(j, carry, masked):
        high, total, accum = carry
        even = bounds_ref[4] == 0
        keys = jnp.concatenate(
            [jnp.where(even, own_ref[j, 0], other_ref[j, 0]), jnp.where(even, other_ref[j, 0], own_ref[j, 0])],
            axis=0,
        )
        values = jnp.concatenate(
            [jnp.where(even, own_ref[j, 1], other_ref[j, 1]), jnp.where(even, other_ref[j, 1], own_ref[j, 1])],
            axis=0,
        )
        scores = lax.dot_general(q, keys, (((1,), (1,)), ((), ())), preferred_element_type=jnp.float32) * scale
        if masked:
            key_pos = j * block + lax.broadcasted_iota(jnp.int32, (1, block), 1)
            allowed = (key_pos >= qstart) & (key_pos <= qpos)
            scores = jnp.where(allowed, scores, FLOOR)
        new_high = jnp.maximum(high, jnp.max(scores, axis=1, keepdims=True))
        weights = jnp.exp(scores - new_high)
        if masked:
            weights = jnp.where(allowed, weights, 0.0)
        factor = jnp.exp(high - new_high)
        total = total * factor + jnp.sum(weights, axis=1, keepdims=True)
        accum = accum * factor + jnp.dot(
            weights.astype(jnp.bfloat16), values, preferred_element_type=jnp.float32
        )
        return new_high, total, accum

    carry = (
        jnp.full((heads * tok, 1), FLOOR, jnp.float32),
        jnp.zeros((heads * tok, 1), jnp.float32),
        jnp.zeros((heads * tok, dim), jnp.float32),
    )
    carry = lax.fori_loop(bounds_ref[0], bounds_ref[1], lambda j, c: step(j, c, True), carry)
    carry = lax.fori_loop(bounds_ref[1], bounds_ref[2], lambda j, c: step(j, c, False), carry)
    carry = lax.fori_loop(bounds_ref[2], bounds_ref[3], lambda j, c: step(j, c, True), carry)
    high, total, accum = carry
    out = (accum / total).astype(jnp.bfloat16)
    terms = jnp.dot(out[:tok], w_ref[:dim, :], preferred_element_type=jnp.float32)
    for h in range(1, heads):
        terms = terms + jnp.dot(
            out[h * tok : (h + 1) * tok], w_ref[h * dim : (h + 1) * dim, :], preferred_element_type=jnp.float32
        )
    o_ref[...] = terms.astype(o_ref.dtype)


def attend(bounds, queries, cosine, sine, gain, own, other, qpos, qstart, w_out):
    tok, width = queries.shape
    dim = own.shape[-1]
    kernel = functools.partial(_attend_kernel, dim=dim)
    spec = pltpu.PrefetchScalarGridSpec(
        num_scalar_prefetch=1,
        grid=(1,),
        in_specs=[
            pl.BlockSpec((tok, width), lambda i, b: (0, 0)),
            pl.BlockSpec(cosine.shape, lambda i, b: (0, 0)),
            pl.BlockSpec(sine.shape, lambda i, b: (0, 0)),
            pl.BlockSpec(gain.shape, lambda i, b: (0, 0)),
            pl.BlockSpec(own.shape, lambda i, b: (0, 0, 0, 0)),
            pl.BlockSpec(other.shape, lambda i, b: (0, 0, 0, 0)),
            pl.BlockSpec(qpos.shape, lambda i, b: (0, 0)),
            pl.BlockSpec(qstart.shape, lambda i, b: (0, 0)),
            pl.BlockSpec(w_out.shape, lambda i, b: (0, 0)),
        ],
        out_specs=pl.BlockSpec((tok, w_out.shape[1]), lambda i, b: (0, 0)),
    )
    return pl.pallas_call(
        kernel, grid_spec=spec, out_shape=jax.ShapeDtypeStruct((tok, w_out.shape[1]), jnp.bfloat16)
    )(bounds, queries, cosine, sine, gain, own, other, qpos, qstart, w_out)


def _project_kernel(
    index_ref, x_ref, ngain_ref, wk_ref, wv_ref, kgain_ref, cos_ref, sin_ref, normed_ref, spread_ref
):
    x = x_ref[...].astype(jnp.float32)
    normed = (x * lax.rsqrt(jnp.mean(x * x, axis=1, keepdims=True) + EPSILON) * ngain_ref[...]).astype(
        jnp.bfloat16
    )
    normed_ref[...] = normed
    keys = jnp.dot(normed, wk_ref[...], preferred_element_type=jnp.float32)
    keys = keys * lax.rsqrt(jnp.mean(keys * keys, axis=1, keepdims=True) + EPSILON) * kgain_ref[...]
    keys = keys * cos_ref[...] + pltpu.roll(keys, keys.shape[1] // 2, 1) * sin_ref[...]
    keys = keys.astype(jnp.bfloat16)
    values = jnp.dot(normed, wv_ref[...], preferred_element_type=jnp.float32).astype(jnp.bfloat16)
    for i in range(spread_ref.shape[0]):
        spread_ref[i, 0] = keys
        spread_ref[i, 1] = values


def project(index, tokens, norm_gain, w_key, w_value, key_gain, cosine, sine, copies):
    tok, width = tokens.shape
    dim = key_gain.shape[0]
    spec = pltpu.PrefetchScalarGridSpec(
        num_scalar_prefetch=1,
        grid=(1,),
        in_specs=[
            pl.BlockSpec((tok, width), lambda i, b: (0, 0)),
            pl.BlockSpec((1, width), lambda i, b: (0, 0)),
            pl.BlockSpec((width, dim), lambda i, b: (0, b[0])),
            pl.BlockSpec((width, dim), lambda i, b: (0, b[0])),
            pl.BlockSpec((1, dim), lambda i, b: (0, 0)),
            pl.BlockSpec((tok, dim), lambda i, b: (0, 0)),
            pl.BlockSpec((tok, dim), lambda i, b: (0, 0)),
        ],
        out_specs=[
            pl.BlockSpec((tok, width), lambda i, b: (0, 0)),
            pl.BlockSpec((copies, 2, tok, dim), lambda i, b: (0, 0, 0, 0)),
        ],
    )
    return pl.pallas_call(
        _project_kernel,
        grid_spec=spec,
        out_shape=[
            jax.ShapeDtypeStruct((tok, width), jnp.bfloat16),
            jax.ShapeDtypeStruct((copies, 2, tok, dim), jnp.bfloat16),
        ],
    )(index, tokens, norm_gain[None, :], w_key, w_value, key_gain[None, :], cosine, sine)


def local(
    tokens,
    norm_gain,
    w_query,
    w_key,
    w_value,
    query_gain,
    key_gain,
    w_out,
    post_gain,
    doc_lengths,
    expert_ids,
    route_weights,
    w_gate,
    w_up,
    w_down,
):
    tok_dev, width = tokens.shape
    head_dim = query_gain.shape[0]
    per_dev = w_query.shape[1] // head_dim
    n_seq = lax.axis_size("seq")
    n_head = lax.axis_size("head")
    seq_index = lax.axis_index("seq")
    head_index = lax.axis_index("head")
    ndocs = doc_lengths.shape[0]
    ends = jnp.cumsum(doc_lengths)
    starts = ends - doc_lengths
    positions = seq_index * tok_dev + jnp.arange(tok_dev, dtype=jnp.int32)
    query_doc = doc_index(positions, ends)
    matches = query_doc[:, None] == jnp.arange(ndocs, dtype=jnp.int32)[None, :]
    own_start = jnp.sum(jnp.where(matches, starts[None, :], 0), axis=1)
    offset = (positions - own_start).astype(jnp.float32)
    half = head_dim // 2
    inverse = THETA ** (-2.0 * jnp.arange(half, dtype=jnp.float32) / head_dim)
    angles = offset[:, None] * inverse[None, :]
    cosine = jnp.cos(angles)
    sine = jnp.sin(angles)
    cosine2 = jnp.concatenate([cosine, cosine], axis=-1)
    sine2 = jnp.concatenate([-sine, sine], axis=-1)
    pairs = n_seq // 2
    groups = [[2 * i + c for i in range(pairs)] for c in range(2)]
    kv_head = jnp.reshape(head_index * per_dev // (HEADS // KV_HEADS), (1,)).astype(jnp.int32)
    normed, spread = project(kv_head, tokens, norm_gain, w_key, w_value, key_gain, cosine2, sine2, pairs)
    queries = jnp.dot(normed, w_query, preferred_element_type=jnp.float32)
    same_core = lax.all_to_all(spread, "seq", 0, 0, tiled=True, axis_index_groups=groups)
    block = 2 * tok_dev
    low = own_start[0] // block
    high = positions[-1] // block + 1
    inner_low = jnp.clip(-(-own_start[-1] // block), low, high)
    inner_high = jnp.clip((positions[0] + 1) // block, inner_low, high)
    bounds = jnp.stack([low, inner_low, inner_high, high, seq_index % 2]).astype(jnp.int32)
    operands = (
        bounds,
        queries,
        cosine2,
        sine2,
        query_gain[None, :],
        jnp.tile(positions[:, None], (per_dev, 1)),
        jnp.tile(own_start[:, None], (per_dev, 1)),
    )
    operands, same_core = lax.optimization_barrier((operands, same_core))
    other_core = lax.ppermute(same_core, "seq", [(i, i ^ 1) for i in range(n_seq)])
    bounds, queries, cosine2, sine2, gain, qpos, qstart = operands
    terms = attend(bounds, queries, cosine2, sine2, gain, same_core, other_core, qpos, qstart, w_out)
    rows = tok_dev // n_head
    terms = lax.all_to_all(terms.reshape(n_head, rows, width), "head", 0, 0, tiled=True)
    attn_rows = jnp.sum(terms.astype(jnp.float32), axis=0)
    resid = lax.dynamic_slice_in_dim(tokens, head_index * rows, rows, 0).astype(jnp.float32) + attn_rows
    routed = rms_scale(resid, post_gain).astype(jnp.bfloat16)
    experts = n_seq * n_head * w_gate.shape[0]
    capacity = 2 * TOP * rows // experts
    chosen = expert_ids.reshape(-1)
    hits = (chosen[:, None] == jnp.arange(experts, dtype=jnp.int32)[None, :]).astype(jnp.int32)
    rank = jnp.sum((jnp.cumsum(hits, axis=0) - hits) * hits, axis=1)
    slot = rank * experts + chosen
    select = (slot[:, None] == jnp.arange(capacity * experts, dtype=jnp.int32)[None, :]).reshape(
        rows, TOP, capacity * experts
    )
    sources = jnp.transpose(jnp.any(select, axis=1)).astype(jnp.bfloat16)
    outgoing = jnp.dot(sources, routed, preferred_element_type=jnp.float32).astype(jnp.bfloat16)
    outgoing = outgoing.reshape(capacity, experts, width)
    block = lax.all_to_all(outgoing, ("seq", "head"), split_axis=1, concat_axis=1, tiled=True)
    flat = block.reshape(-1, width)
    gate = jnp.dot(flat, w_gate[0], preferred_element_type=jnp.float32)
    up = jnp.dot(flat, w_up[0], preferred_element_type=jnp.float32)
    gate, up = lax.optimization_barrier((gate, up))
    hidden = (jax.nn.silu(gate) * up).astype(jnp.bfloat16)
    returned = lax.all_to_all(
        jnp.dot(hidden, w_down[0], preferred_element_type=jnp.float32)
        .astype(jnp.bfloat16)
        .reshape(block.shape),
        ("seq", "head"),
        split_axis=1,
        concat_axis=1,
        tiled=True,
    ).reshape(-1, width)
    mixing = jnp.sum(jnp.where(select, route_weights[:, :, None], 0.0), axis=1)
    combined = jnp.dot(
        mixing, returned.astype(jnp.float32), precision=lax.Precision.HIGHEST,
        preferred_element_type=jnp.float32,
    )
    return (resid + combined).astype(jnp.bfloat16)


def solution(mesh):
    placed = (
        P("seq", None),
        P(),
        P(None, "head"),
        P(),
        P(),
        P(),
        P(),
        P("head", None),
        P(),
        P(),
        P(("seq", "head"), None),
        P(("seq", "head"), None),
        P(("seq", "head"), None, None),
        P(("seq", "head"), None, None),
        P(("seq", "head"), None, None),
    )
    return jax.shard_map(
        local, mesh=mesh, in_specs=placed, out_specs=P(("seq", "head"), None), check_vma=False
    )
```

```python
import functools
import math

import jax
import jax.numpy as jnp
from jax import lax
from jax.experimental import pallas as pl
from jax.experimental.pallas import tpu as pltpu
from jax.sharding import PartitionSpec as P

HEADS = 32
KV_HEADS = 4
TOP = 8


EPSILON = 1e-06
THETA = 1000000.0
FLOOR = -1e30


def rms_scale(values, gain):
    return values * lax.rsqrt(jnp.mean(values * values, axis=-1, keepdims=True) + EPSILON) * gain


def rotate(values, cosine, sine):
    half = values.shape[-1] // 2
    first = values[..., :half]
    second = values[..., half:]
    return jnp.concatenate(
        [first * cosine - second * sine, second * cosine + first * sine], axis=-1
    )


def doc_index(positions, ends):
    return jnp.sum((positions[:, None] >= ends[None, :]).astype(jnp.int32), axis=1)


def _attend_kernel(
    bounds_ref, q_ref, cos_ref, sin_ref, gain_ref, own_ref, other_ref, qpos_ref, qstart_ref, w_hbm, o_ref,
    w_ref, w_sem, *, dim
):
    w_copy = pltpu.make_async_copy(w_hbm, w_ref, w_sem)
    w_copy.start()
    heads = q_ref.shape[1] // dim
    tok = q_ref.shape[0]
    block = 2 * own_ref.shape[2]
    parts = []
    for h in range(heads):
        part = q_ref[:, h * dim : (h + 1) * dim]
        part = part * lax.rsqrt(jnp.mean(part * part, axis=1, keepdims=True) + EPSILON) * gain_ref[...]
        part = part * cos_ref[...] + pltpu.roll(part, dim // 2, 1) * sin_ref[...]
        parts.append(part.astype(jnp.bfloat16))
    q = jnp.concatenate(parts, axis=0)
    qpos = qpos_ref[...]
    qstart = qstart_ref[...]
    scale = dim ** (-0.5)

    def step(j, carry, masked):
        high, total, accum = carry
        even = bounds_ref[4] == 0
        keys = jnp.concatenate(
            [jnp.where(even, own_ref[j, 0], other_ref[j, 0]), jnp.where(even, other_ref[j, 0], own_ref[j, 0])],
            axis=0,
        )
        values = jnp.concatenate(
            [jnp.where(even, own_ref[j, 1], other_ref[j, 1]), jnp.where(even, other_ref[j, 1], own_ref[j, 1])],
            axis=0,
        )
        scores = lax.dot_general(q, keys, (((1,), (1,)), ((), ())), preferred_element_type=jnp.float32) * scale
        if masked:
            key_pos = j * block + lax.broadcasted_iota(jnp.int32, (1, block), 1)
            allowed = (key_pos >= qstart) & (key_pos <= qpos)
            scores = jnp.where(allowed, scores, FLOOR)
        new_high = jnp.maximum(high, jnp.max(scores, axis=1, keepdims=True))
        weights = jnp.exp(scores - new_high)
        if masked:
            weights = jnp.where(allowed, weights, 0.0)
        factor = jnp.exp(high - new_high)
        total = total * factor + jnp.sum(weights, axis=1, keepdims=True)
        accum = accum * factor + jnp.dot(
            weights.astype(jnp.bfloat16), values, preferred_element_type=jnp.float32
        )
        return new_high, total, accum

    carry = (
        jnp.full((heads * tok, 1), FLOOR, jnp.float32),
        jnp.zeros((heads * tok, 1), jnp.float32),
        jnp.zeros((heads * tok, dim), jnp.float32),
    )
    carry = lax.fori_loop(bounds_ref[0], bounds_ref[1], lambda j, c: step(j, c, True), carry)
    carry = lax.fori_loop(bounds_ref[1], bounds_ref[2], lambda j, c: step(j, c, False), carry)
    carry = lax.fori_loop(bounds_ref[2], bounds_ref[3], lambda j, c: step(j, c, True), carry)
    high, total, accum = carry
    out = (accum / total).astype(jnp.bfloat16)
    w_copy.wait()
    terms = jnp.dot(out[:tok], w_ref[:dim, :], preferred_element_type=jnp.float32)
    for h in range(1, heads):
        terms = terms + jnp.dot(
            out[h * tok : (h + 1) * tok], w_ref[h * dim : (h + 1) * dim, :], preferred_element_type=jnp.float32
        )
    o_ref[...] = terms.astype(o_ref.dtype)


def attend(bounds, queries, cosine, sine, gain, own, other, qpos, qstart, w_out):
    tok, width = queries.shape
    dim = own.shape[-1]
    kernel = functools.partial(_attend_kernel, dim=dim)
    spec = pltpu.PrefetchScalarGridSpec(
        num_scalar_prefetch=1,
        grid=(1,),
        in_specs=[
            pl.BlockSpec((tok, width), lambda i, b: (0, 0)),
            pl.BlockSpec(cosine.shape, lambda i, b: (0, 0)),
            pl.BlockSpec(sine.shape, lambda i, b: (0, 0)),
            pl.BlockSpec(gain.shape, lambda i, b: (0, 0)),
            pl.BlockSpec(own.shape, lambda i, b: (0, 0, 0, 0)),
            pl.BlockSpec(other.shape, lambda i, b: (0, 0, 0, 0)),
            pl.BlockSpec(qpos.shape, lambda i, b: (0, 0)),
            pl.BlockSpec(qstart.shape, lambda i, b: (0, 0)),
            pl.BlockSpec(memory_space=pl.ANY),
        ],
        out_specs=pl.BlockSpec((tok, w_out.shape[1]), lambda i, b: (0, 0)),
        scratch_shapes=[pltpu.VMEM(w_out.shape, w_out.dtype), pltpu.SemaphoreType.DMA],
    )
    return pl.pallas_call(
        kernel, grid_spec=spec, out_shape=jax.ShapeDtypeStruct((tok, w_out.shape[1]), jnp.bfloat16)
    )(bounds, queries, cosine, sine, gain, own, other, qpos, qstart, w_out)


def _project_kernel(
    index_ref, x_ref, ngain_ref, wk_ref, wv_ref, kgain_ref, cos_ref, sin_ref, normed_ref, spread_ref
):
    x = x_ref[...].astype(jnp.float32)
    normed = (x * lax.rsqrt(jnp.mean(x * x, axis=1, keepdims=True) + EPSILON) * ngain_ref[...]).astype(
        jnp.bfloat16
    )
    normed_ref[...] = normed
    keys = jnp.dot(normed, wk_ref[...], preferred_element_type=jnp.float32)
    keys = keys * lax.rsqrt(jnp.mean(keys * keys, axis=1, keepdims=True) + EPSILON) * kgain_ref[...]
    keys = keys * cos_ref[...] + pltpu.roll(keys, keys.shape[1] // 2, 1) * sin_ref[...]
    keys = keys.astype(jnp.bfloat16)
    values = jnp.dot(normed, wv_ref[...], preferred_element_type=jnp.float32).astype(jnp.bfloat16)
    for i in range(spread_ref.shape[0]):
        spread_ref[i, 0] = keys
        spread_ref[i, 1] = values


def project(index, tokens, norm_gain, w_key, w_value, key_gain, cosine, sine, copies):
    tok, width = tokens.shape
    dim = key_gain.shape[0]
    spec = pltpu.PrefetchScalarGridSpec(
        num_scalar_prefetch=1,
        grid=(1,),
        in_specs=[
            pl.BlockSpec((tok, width), lambda i, b: (0, 0)),
            pl.BlockSpec((1, width), lambda i, b: (0, 0)),
            pl.BlockSpec((width, dim), lambda i, b: (0, b[0])),
            pl.BlockSpec((width, dim), lambda i, b: (0, b[0])),
            pl.BlockSpec((1, dim), lambda i, b: (0, 0)),
            pl.BlockSpec((tok, dim), lambda i, b: (0, 0)),
            pl.BlockSpec((tok, dim), lambda i, b: (0, 0)),
        ],
        out_specs=[
            pl.BlockSpec((tok, width), lambda i, b: (0, 0)),
            pl.BlockSpec((copies, 2, tok, dim), lambda i, b: (0, 0, 0, 0)),
        ],
    )
    return pl.pallas_call(
        _project_kernel,
        grid_spec=spec,
        out_shape=[
            jax.ShapeDtypeStruct((tok, width), jnp.bfloat16),
            jax.ShapeDtypeStruct((copies, 2, tok, dim), jnp.bfloat16),
        ],
    )(index, tokens, norm_gain[None, :], w_key, w_value, key_gain[None, :], cosine, sine)


def local(
    tokens,
    norm_gain,
    w_query,
    w_key,
    w_value,
    query_gain,
    key_gain,
    w_out,
    post_gain,
    doc_lengths,
    expert_ids,
    route_weights,
    w_gate,
    w_up,
    w_down,
):
    tok_dev, width = tokens.shape
    head_dim = query_gain.shape[0]
    per_dev = w_query.shape[1] // head_dim
    n_seq = lax.axis_size("seq")
    n_head = lax.axis_size("head")
    seq_index = lax.axis_index("seq")
    head_index = lax.axis_index("head")
    ndocs = doc_lengths.shape[0]
    ends = jnp.cumsum(doc_lengths)
    starts = ends - doc_lengths
    positions = seq_index * tok_dev + jnp.arange(tok_dev, dtype=jnp.int32)
    query_doc = doc_index(positions, ends)
    matches = query_doc[:, None] == jnp.arange(ndocs, dtype=jnp.int32)[None, :]
    own_start = jnp.sum(jnp.where(matches, starts[None, :], 0), axis=1)
    offset = (positions - own_start).astype(jnp.float32)
    half = head_dim // 2
    inverse = THETA ** (-2.0 * jnp.arange(half, dtype=jnp.float32) / head_dim)
    angles = offset[:, None] * inverse[None, :]
    cosine = jnp.cos(angles)
    sine = jnp.sin(angles)
    cosine2 = jnp.concatenate([cosine, cosine], axis=-1)
    sine2 = jnp.concatenate([-sine, sine], axis=-1)
    pairs = n_seq // 2
    groups = [[2 * i + c for i in range(pairs)] for c in range(2)]
    kv_head = jnp.reshape(head_index * per_dev // (HEADS // KV_HEADS), (1,)).astype(jnp.int32)
    normed, spread = project(kv_head, tokens, norm_gain, w_key, w_value, key_gain, cosine2, sine2, pairs)
    queries = jnp.dot(normed, w_query, preferred_element_type=jnp.float32)
    same_core = lax.all_to_all(spread, "seq", 0, 0, tiled=True, axis_index_groups=groups)
    block = 2 * tok_dev
    low = own_start[0] // block
    high = positions[-1] // block + 1
    inner_low = jnp.clip(-(-own_start[-1] // block), low, high)
    inner_high = jnp.clip((positions[0] + 1) // block, inner_low, high)
    bounds = jnp.stack([low, inner_low, inner_high, high, seq_index % 2]).astype(jnp.int32)
    operands = (
        bounds,
        queries,
        cosine2,
        sine2,
        query_gain[None, :],
        jnp.tile(positions[:, None], (per_dev, 1)),
        jnp.tile(own_start[:, None], (per_dev, 1)),
    )
    operands, same_core = lax.optimization_barrier((operands, same_core))
    other_core = lax.ppermute(same_core, "seq", [(i, i ^ 1) for i in range(n_seq)])
    bounds, queries, cosine2, sine2, gain, qpos, qstart = operands
    terms = attend(bounds, queries, cosine2, sine2, gain, same_core, other_core, qpos, qstart, w_out)
    rows = tok_dev // n_head
    terms = lax.all_to_all(terms.reshape(n_head, rows, width), "head", 0, 0, tiled=True)
    attn_rows = jnp.sum(terms.astype(jnp.float32), axis=0)
    resid = lax.dynamic_slice_in_dim(tokens, head_index * rows, rows, 0).astype(jnp.float32) + attn_rows
    routed = rms_scale(resid, post_gain).astype(jnp.bfloat16)
    experts = n_seq * n_head * w_gate.shape[0]
    capacity = 2 * TOP * rows // experts
    chosen = expert_ids.reshape(-1)
    hits = (chosen[:, None] == jnp.arange(experts, dtype=jnp.int32)[None, :]).astype(jnp.int32)
    rank = jnp.sum((jnp.cumsum(hits, axis=0) - hits) * hits, axis=1)
    slot = rank * experts + chosen
    select = (slot[:, None] == jnp.arange(capacity * experts, dtype=jnp.int32)[None, :]).reshape(
        rows, TOP, capacity * experts
    )
    sources = jnp.transpose(jnp.any(select, axis=1)).astype(jnp.bfloat16)
    outgoing = jnp.dot(sources, routed, preferred_element_type=jnp.float32).astype(jnp.bfloat16)
    outgoing = outgoing.reshape(capacity, experts, width)
    block = lax.all_to_all(outgoing, ("seq", "head"), split_axis=1, concat_axis=1, tiled=True)
    flat = block.reshape(-1, width)
    gate = jnp.dot(flat, w_gate[0], preferred_element_type=jnp.float32)
    up = jnp.dot(flat, w_up[0], preferred_element_type=jnp.float32)
    gate, up = lax.optimization_barrier((gate, up))
    hidden = (jax.nn.silu(gate) * up).astype(jnp.bfloat16)
    returned = lax.all_to_all(
        jnp.dot(hidden, w_down[0], preferred_element_type=jnp.float32)
        .astype(jnp.bfloat16)
        .reshape(block.shape),
        ("seq", "head"),
        split_axis=1,
        concat_axis=1,
        tiled=True,
    ).reshape(-1, width)
    mixing = jnp.sum(jnp.where(select, route_weights[:, :, None], 0.0), axis=1)
    combined = jnp.dot(
        mixing, returned.astype(jnp.float32), precision=lax.Precision.HIGHEST,
        preferred_element_type=jnp.float32,
    )
    return (resid + combined).astype(jnp.bfloat16)


def solution(mesh):
    placed = (
        P("seq", None),
        P(),
        P(None, "head"),
        P(),
        P(),
        P(),
        P(),
        P("head", None),
        P(),
        P(),
        P(("seq", "head"), None),
        P(("seq", "head"), None),
        P(("seq", "head"), None, None),
        P(("seq", "head"), None, None),
        P(("seq", "head"), None, None),
    )
    return jax.shard_map(
        local, mesh=mesh, in_specs=placed, out_specs=P(("seq", "head"), None), check_vma=False
    )
```

```python
import functools
import math

import jax
import jax.numpy as jnp
from jax import lax
from jax.experimental import pallas as pl
from jax.experimental.pallas import tpu as pltpu
from jax.sharding import PartitionSpec as P

HEADS = 32
KV_HEADS = 4
TOP = 8


EPSILON = 1e-06
THETA = 1000000.0
FLOOR = -1e30


def rms_scale(values, gain):
    return values * lax.rsqrt(jnp.mean(values * values, axis=-1, keepdims=True) + EPSILON) * gain


def rotate(values, cosine, sine):
    half = values.shape[-1] // 2
    first = values[..., :half]
    second = values[..., half:]
    return jnp.concatenate(
        [first * cosine - second * sine, second * cosine + first * sine], axis=-1
    )


def doc_index(positions, ends):
    return jnp.sum((positions[:, None] >= ends[None, :]).astype(jnp.int32), axis=1)


def _attend_kernel(
    bounds_ref, q_ref, cos_ref, sin_ref, gain_ref, own_ref, other_ref, qpos_ref, qstart_ref, w_ref, o_ref, *, dim
):
    heads = q_ref.shape[1] // dim
    tok = q_ref.shape[0]
    block = 2 * own_ref.shape[2]
    parts = []
    for h in range(heads):
        part = q_ref[:, h * dim : (h + 1) * dim]
        part = part * lax.rsqrt(jnp.mean(part * part, axis=1, keepdims=True) + EPSILON) * gain_ref[...]
        part = part * cos_ref[...] + pltpu.roll(part, dim // 2, 1) * sin_ref[...]
        parts.append(part.astype(jnp.bfloat16))
    q = jnp.concatenate(parts, axis=0)
    qpos = qpos_ref[...]
    qstart = qstart_ref[...]
    scale = dim ** (-0.5)

    def step(j, carry, masked):
        high, total, accum = carry
        even = bounds_ref[4] == 0
        keys = jnp.concatenate(
            [jnp.where(even, own_ref[j, 0], other_ref[j, 0]), jnp.where(even, other_ref[j, 0], own_ref[j, 0])],
            axis=0,
        )
        values = jnp.concatenate(
            [jnp.where(even, own_ref[j, 1], other_ref[j, 1]), jnp.where(even, other_ref[j, 1], own_ref[j, 1])],
            axis=0,
        )
        scores = lax.dot_general(q, keys, (((1,), (1,)), ((), ())), preferred_element_type=jnp.float32) * scale
        if masked:
            key_pos = j * block + lax.broadcasted_iota(jnp.int32, (1, block), 1)
            allowed = (key_pos >= qstart) & (key_pos <= qpos)
            scores = jnp.where(allowed, scores, FLOOR)
        new_high = jnp.maximum(high, jnp.max(scores, axis=1, keepdims=True))
        weights = jnp.exp(scores - new_high)
        if masked:
            weights = jnp.where(allowed, weights, 0.0)
        factor = jnp.exp(high - new_high)
        total = total * factor + jnp.sum(weights, axis=1, keepdims=True)
        accum = accum * factor + jnp.dot(
            weights.astype(jnp.bfloat16), values, preferred_element_type=jnp.float32
        )
        return new_high, total, accum

    carry = (
        jnp.full((heads * tok, 1), FLOOR, jnp.float32),
        jnp.zeros((heads * tok, 1), jnp.float32),
        jnp.zeros((heads * tok, dim), jnp.float32),
    )
    carry = lax.fori_loop(bounds_ref[0], bounds_ref[1], lambda j, c: step(j, c, True), carry)
    carry = lax.fori_loop(bounds_ref[1], bounds_ref[2], lambda j, c: step(j, c, False), carry)
    carry = lax.fori_loop(bounds_ref[2], bounds_ref[3], lambda j, c: step(j, c, True), carry)
    high, total, accum = carry
    out = (accum / total).astype(jnp.bfloat16)
    terms = jnp.dot(out[:tok], w_ref[:dim, :], preferred_element_type=jnp.float32)
    for h in range(1, heads):
        terms = terms + jnp.dot(
            out[h * tok : (h + 1) * tok], w_ref[h * dim : (h + 1) * dim, :], preferred_element_type=jnp.float32
        )
    o_ref[...] = terms.astype(o_ref.dtype)


def attend(bounds, queries, cosine, sine, gain, own, other, qpos, qstart, w_out):
    tok, width = queries.shape
    dim = own.shape[-1]
    kernel = functools.partial(_attend_kernel, dim=dim)
    spec = pltpu.PrefetchScalarGridSpec(
        num_scalar_prefetch=1,
        grid=(1,),
        in_specs=[
            pl.BlockSpec((tok, width), lambda i, b: (0, 0)),
            pl.BlockSpec(cosine.shape, lambda i, b: (0, 0)),
            pl.BlockSpec(sine.shape, lambda i, b: (0, 0)),
            pl.BlockSpec(gain.shape, lambda i, b: (0, 0)),
            pl.BlockSpec(own.shape, lambda i, b: (0, 0, 0, 0)),
            pl.BlockSpec(other.shape, lambda i, b: (0, 0, 0, 0)),
            pl.BlockSpec(qpos.shape, lambda i, b: (0, 0)),
            pl.BlockSpec(qstart.shape, lambda i, b: (0, 0)),
            pl.BlockSpec(w_out.shape, lambda i, b: (0, 0)),
        ],
        out_specs=pl.BlockSpec((tok, w_out.shape[1]), lambda i, b: (0, 0)),
    )
    return pl.pallas_call(
        kernel, grid_spec=spec, out_shape=jax.ShapeDtypeStruct((tok, w_out.shape[1]), jnp.bfloat16)
    )(bounds, queries, cosine, sine, gain, own, other, qpos, qstart, w_out)


def _project_kernel(
    index_ref, x_ref, ngain_ref, wk_ref, wv_ref, kgain_ref, cos_ref, sin_ref, normed_ref, spread_ref
):
    x = x_ref[...].astype(jnp.float32)
    normed = (x * lax.rsqrt(jnp.mean(x * x, axis=1, keepdims=True) + EPSILON) * ngain_ref[...]).astype(
        jnp.bfloat16
    )
    normed_ref[...] = normed
    keys = jnp.dot(normed, wk_ref[...], preferred_element_type=jnp.float32)
    keys = keys * lax.rsqrt(jnp.mean(keys * keys, axis=1, keepdims=True) + EPSILON) * kgain_ref[...]
    keys = keys * cos_ref[...] + pltpu.roll(keys, keys.shape[1] // 2, 1) * sin_ref[...]
    keys = keys.astype(jnp.bfloat16)
    values = jnp.dot(normed, wv_ref[...], preferred_element_type=jnp.float32).astype(jnp.bfloat16)
    for i in range(spread_ref.shape[0]):
        spread_ref[i, 0] = keys
        spread_ref[i, 1] = values


def project(index, tokens, norm_gain, w_key, w_value, key_gain, cosine, sine, copies):
    tok, width = tokens.shape
    dim = key_gain.shape[0]
    spec = pltpu.PrefetchScalarGridSpec(
        num_scalar_prefetch=1,
        grid=(1,),
        in_specs=[
            pl.BlockSpec((tok, width), lambda i, b: (0, 0)),
            pl.BlockSpec((1, width), lambda i, b: (0, 0)),
            pl.BlockSpec((width, dim), lambda i, b: (0, b[0])),
            pl.BlockSpec((width, dim), lambda i, b: (0, b[0])),
            pl.BlockSpec((1, dim), lambda i, b: (0, 0)),
            pl.BlockSpec((tok, dim), lambda i, b: (0, 0)),
            pl.BlockSpec((tok, dim), lambda i, b: (0, 0)),
        ],
        out_specs=[
            pl.BlockSpec((tok, width), lambda i, b: (0, 0)),
            pl.BlockSpec((copies, 2, tok, dim), lambda i, b: (0, 0, 0, 0)),
        ],
    )
    return pl.pallas_call(
        _project_kernel,
        grid_spec=spec,
        out_shape=[
            jax.ShapeDtypeStruct((tok, width), jnp.bfloat16),
            jax.ShapeDtypeStruct((copies, 2, tok, dim), jnp.bfloat16),
        ],
    )(index, tokens, norm_gain[None, :], w_key, w_value, key_gain[None, :], cosine, sine)


def local(
    tokens,
    norm_gain,
    w_query,
    w_key,
    w_value,
    query_gain,
    key_gain,
    w_out,
    post_gain,
    doc_lengths,
    expert_ids,
    route_weights,
    w_gate,
    w_up,
    w_down,
):
    tok_dev, width = tokens.shape
    head_dim = query_gain.shape[0]
    per_dev = w_query.shape[1] // head_dim
    n_seq = lax.axis_size("seq")
    n_head = lax.axis_size("head")
    seq_index = lax.axis_index("seq")
    head_index = lax.axis_index("head")
    ndocs = doc_lengths.shape[0]
    order = jnp.arange(ndocs, dtype=jnp.int32)
    ends = jnp.sum(jnp.where(order[None, :] <= order[:, None], doc_lengths[None, :], 0), axis=1)
    starts = ends - doc_lengths
    positions = seq_index * tok_dev + jnp.arange(tok_dev, dtype=jnp.int32)
    query_doc = doc_index(positions, ends)
    matches = query_doc[:, None] == jnp.arange(ndocs, dtype=jnp.int32)[None, :]
    own_start = jnp.sum(jnp.where(matches, starts[None, :], 0), axis=1)
    offset = (positions - own_start).astype(jnp.float32)
    half = head_dim // 2
    inverse = THETA ** (-2.0 * jnp.arange(half, dtype=jnp.float32) / head_dim)
    angles = offset[:, None] * jnp.concatenate([inverse, inverse])[None, :]
    cosine2 = jnp.cos(angles)
    sign = jnp.where(jnp.arange(head_dim) < half, -1.0, 1.0).astype(jnp.float32)
    sine2 = jnp.sin(angles) * sign[None, :]
    pairs = n_seq // 2
    groups = [[2 * i + c for i in range(pairs)] for c in range(2)]
    kv_head = jnp.reshape(head_index * per_dev // (HEADS // KV_HEADS), (1,)).astype(jnp.int32)
    normed, spread = project(kv_head, tokens, norm_gain, w_key, w_value, key_gain, cosine2, sine2, pairs)
    queries = jnp.dot(normed, w_query, preferred_element_type=jnp.float32)
    same_core = lax.all_to_all(spread, "seq", 0, 0, tiled=True, axis_index_groups=groups)
    block = 2 * tok_dev
    low = own_start[0] // block
    high = positions[-1] // block + 1
    inner_low = jnp.clip(-(-own_start[-1] // block), low, high)
    inner_high = jnp.clip((positions[0] + 1) // block, inner_low, high)
    bounds = jnp.stack([low, inner_low, inner_high, high, seq_index % 2]).astype(jnp.int32)
    operands = (
        bounds,
        queries,
        cosine2,
        sine2,
        query_gain[None, :],
        jnp.tile(positions[:, None], (per_dev, 1)),
        jnp.tile(own_start[:, None], (per_dev, 1)),
    )
    operands, same_core = lax.optimization_barrier((operands, same_core))
    other_core = lax.ppermute(same_core, "seq", [(i, i ^ 1) for i in range(n_seq)])
    bounds, queries, cosine2, sine2, gain, qpos, qstart = operands
    terms = attend(bounds, queries, cosine2, sine2, gain, same_core, other_core, qpos, qstart, w_out)
    rows = tok_dev // n_head
    terms = lax.all_to_all(terms.reshape(n_head, rows, width), "head", 0, 0, tiled=True)
    attn_rows = jnp.sum(terms.astype(jnp.float32), axis=0)
    resid = lax.dynamic_slice_in_dim(tokens, head_index * rows, rows, 0).astype(jnp.float32) + attn_rows
    routed = rms_scale(resid, post_gain).astype(jnp.bfloat16)
    experts = n_seq * n_head * w_gate.shape[0]
    capacity = 2 * TOP * rows // experts
    chosen = expert_ids.reshape(-1)
    hits = (chosen[:, None] == jnp.arange(experts, dtype=jnp.int32)[None, :]).astype(jnp.int32)
    rank = jnp.sum((jnp.cumsum(hits, axis=0) - hits) * hits, axis=1)
    slot = rank * experts + chosen
    select = (slot[:, None] == jnp.arange(capacity * experts, dtype=jnp.int32)[None, :]).reshape(
        rows, TOP, capacity * experts
    )
    sources = jnp.transpose(jnp.any(select, axis=1)).astype(jnp.bfloat16)
    outgoing = jnp.dot(sources, routed, preferred_element_type=jnp.float32).astype(jnp.bfloat16)
    outgoing = outgoing.reshape(capacity, experts, width)
    block = lax.all_to_all(outgoing, ("seq", "head"), split_axis=1, concat_axis=1, tiled=True)
    flat = block.reshape(-1, width)
    gate = jnp.dot(flat, w_gate[0], preferred_element_type=jnp.float32)
    up = jnp.dot(flat, w_up[0], preferred_element_type=jnp.float32)
    gate, up = lax.optimization_barrier((gate, up))
    hidden = (jax.nn.silu(gate) * up).astype(jnp.bfloat16)
    returned = lax.all_to_all(
        jnp.dot(hidden, w_down[0], preferred_element_type=jnp.float32)
        .astype(jnp.bfloat16)
        .reshape(block.shape),
        ("seq", "head"),
        split_axis=1,
        concat_axis=1,
        tiled=True,
    ).reshape(-1, width)
    mixing = jnp.sum(jnp.where(select, route_weights[:, :, None], 0.0), axis=1)
    combined = jnp.dot(
        mixing, returned.astype(jnp.float32), precision=lax.Precision.HIGHEST,
        preferred_element_type=jnp.float32,
    )
    return (resid + combined).astype(jnp.bfloat16)


def solution(mesh):
    placed = (
        P("seq", None),
        P(),
        P(None, "head"),
        P(),
        P(),
        P(),
        P(),
        P("head", None),
        P(),
        P(),
        P(("seq", "head"), None),
        P(("seq", "head"), None),
        P(("seq", "head"), None, None),
        P(("seq", "head"), None, None),
        P(("seq", "head"), None, None),
    )
    return jax.shard_map(
        local, mesh=mesh, in_specs=placed, out_specs=P(("seq", "head"), None), check_vma=False
    )
```

```python
import functools
import math

import jax
import jax.numpy as jnp
from jax import lax
from jax.experimental import pallas as pl
from jax.experimental.pallas import tpu as pltpu
from jax.sharding import PartitionSpec as P

HEADS = 32
KV_HEADS = 4
TOP = 8


EPSILON = 1e-06
THETA = 1000000.0
FLOOR = -1e30


def rms_scale(values, gain):
    return values * lax.rsqrt(jnp.mean(values * values, axis=-1, keepdims=True) + EPSILON) * gain


def rotate(values, cosine, sine):
    half = values.shape[-1] // 2
    first = values[..., :half]
    second = values[..., half:]
    return jnp.concatenate(
        [first * cosine - second * sine, second * cosine + first * sine], axis=-1
    )


def doc_index(positions, ends):
    return jnp.sum((positions[:, None] >= ends[None, :]).astype(jnp.int32), axis=1)


def _attend_kernel(
    bounds_ref, q_ref, cos_ref, sin_ref, gain_ref, own_ref, other_ref, qpos_ref, qstart_ref, w_ref, o_ref, *, dim
):
    heads = q_ref.shape[1] // dim
    tok = q_ref.shape[0]
    block = 2 * own_ref.shape[2]
    parts = []
    for h in range(heads):
        part = q_ref[:, h * dim : (h + 1) * dim]
        part = part * lax.rsqrt(jnp.mean(part * part, axis=1, keepdims=True) + EPSILON) * gain_ref[...]
        part = part * cos_ref[...] + pltpu.roll(part, dim // 2, 1) * sin_ref[...]
        parts.append(part.astype(jnp.bfloat16))
    q = jnp.concatenate(parts, axis=0)
    qpos = qpos_ref[...]
    qstart = qstart_ref[...]
    scale = dim ** (-0.5)

    def step(j, carry, masked):
        high, total, accum = carry
        even = bounds_ref[4] == 0
        keys = jnp.concatenate(
            [jnp.where(even, own_ref[j, 0], other_ref[j, 0]), jnp.where(even, other_ref[j, 0], own_ref[j, 0])],
            axis=0,
        )
        values = jnp.concatenate(
            [jnp.where(even, own_ref[j, 1], other_ref[j, 1]), jnp.where(even, other_ref[j, 1], own_ref[j, 1])],
            axis=0,
        )
        scores = lax.dot_general(q, keys, (((1,), (1,)), ((), ())), preferred_element_type=jnp.float32) * scale
        if masked:
            key_pos = j * block + lax.broadcasted_iota(jnp.int32, (1, block), 1)
            allowed = (key_pos >= qstart) & (key_pos <= qpos)
            scores = jnp.where(allowed, scores, FLOOR)
        new_high = jnp.maximum(high, jnp.max(scores, axis=1, keepdims=True))
        weights = jnp.exp(scores - new_high)
        if masked:
            weights = jnp.where(allowed, weights, 0.0)
        factor = jnp.exp(high - new_high)
        total = total * factor + jnp.sum(weights, axis=1, keepdims=True)
        accum = accum * factor + jnp.dot(
            weights.astype(jnp.bfloat16), values, preferred_element_type=jnp.float32
        )
        return new_high, total, accum

    carry = (
        jnp.full((heads * tok, 1), FLOOR, jnp.float32),
        jnp.zeros((heads * tok, 1), jnp.float32),
        jnp.zeros((heads * tok, dim), jnp.float32),
    )
    carry = lax.fori_loop(bounds_ref[0], bounds_ref[1], lambda j, c: step(j, c, True), carry)
    carry = lax.fori_loop(bounds_ref[1], bounds_ref[2], lambda j, c: step(j, c, False), carry)
    carry = lax.fori_loop(bounds_ref[2], bounds_ref[3], lambda j, c: step(j, c, True), carry)
    high, total, accum = carry
    out = (accum / total).astype(jnp.bfloat16)
    terms = jnp.dot(out[:tok], w_ref[:dim, :], preferred_element_type=jnp.float32)
    for h in range(1, heads):
        terms = terms + jnp.dot(
            out[h * tok : (h + 1) * tok], w_ref[h * dim : (h + 1) * dim, :], preferred_element_type=jnp.float32
        )
    o_ref[...] = terms.astype(o_ref.dtype)


def attend(bounds, queries, cosine, sine, gain, own, other, qpos, qstart, w_out):
    tok, width = queries.shape
    dim = own.shape[-1]
    kernel = functools.partial(_attend_kernel, dim=dim)
    spec = pltpu.PrefetchScalarGridSpec(
        num_scalar_prefetch=1,
        grid=(1,),
        in_specs=[
            pl.BlockSpec((tok, width), lambda i, b: (0, 0)),
            pl.BlockSpec(cosine.shape, lambda i, b: (0, 0)),
            pl.BlockSpec(sine.shape, lambda i, b: (0, 0)),
            pl.BlockSpec(gain.shape, lambda i, b: (0, 0)),
            pl.BlockSpec(own.shape, lambda i, b: (0, 0, 0, 0)),
            pl.BlockSpec(other.shape, lambda i, b: (0, 0, 0, 0)),
            pl.BlockSpec(qpos.shape, lambda i, b: (0, 0)),
            pl.BlockSpec(qstart.shape, lambda i, b: (0, 0)),
            pl.BlockSpec(w_out.shape, lambda i, b: (0, 0)),
        ],
        out_specs=pl.BlockSpec((tok, w_out.shape[1]), lambda i, b: (0, 0)),
    )
    return pl.pallas_call(
        kernel, grid_spec=spec, out_shape=jax.ShapeDtypeStruct((tok, w_out.shape[1]), jnp.bfloat16)
    )(bounds, queries, cosine, sine, gain, own, other, qpos, qstart, w_out)


def _project_kernel(
    index_ref, x_ref, ngain_ref, wk_ref, wv_ref, kgain_ref, cos_ref, sin_ref, normed_ref, spread_ref
):
    x = x_ref[...].astype(jnp.float32)
    normed = (x * lax.rsqrt(jnp.mean(x * x, axis=1, keepdims=True) + EPSILON) * ngain_ref[...]).astype(
        jnp.bfloat16
    )
    normed_ref[...] = normed
    keys = jnp.dot(normed, wk_ref[...], preferred_element_type=jnp.float32)
    keys = keys * lax.rsqrt(jnp.mean(keys * keys, axis=1, keepdims=True) + EPSILON) * kgain_ref[...]
    keys = keys * cos_ref[...] + pltpu.roll(keys, keys.shape[1] // 2, 1) * sin_ref[...]
    keys = keys.astype(jnp.bfloat16)
    values = jnp.dot(normed, wv_ref[...], preferred_element_type=jnp.float32).astype(jnp.bfloat16)
    for i in range(spread_ref.shape[0]):
        spread_ref[i, 0] = keys
        spread_ref[i, 1] = values


def project(index, tokens, norm_gain, w_key, w_value, key_gain, cosine, sine, copies):
    tok, width = tokens.shape
    dim = key_gain.shape[0]
    spec = pltpu.PrefetchScalarGridSpec(
        num_scalar_prefetch=1,
        grid=(1,),
        in_specs=[
            pl.BlockSpec((tok, width), lambda i, b: (0, 0)),
            pl.BlockSpec((1, width), lambda i, b: (0, 0)),
            pl.BlockSpec((width, dim), lambda i, b: (0, b[0])),
            pl.BlockSpec((width, dim), lambda i, b: (0, b[0])),
            pl.BlockSpec((1, dim), lambda i, b: (0, 0)),
            pl.BlockSpec((tok, dim), lambda i, b: (0, 0)),
            pl.BlockSpec((tok, dim), lambda i, b: (0, 0)),
        ],
        out_specs=[
            pl.BlockSpec((tok, width), lambda i, b: (0, 0)),
            pl.BlockSpec((copies, 2, tok, dim), lambda i, b: (0, 0, 0, 0)),
        ],
    )
    return pl.pallas_call(
        _project_kernel,
        grid_spec=spec,
        out_shape=[
            jax.ShapeDtypeStruct((tok, width), jnp.bfloat16),
            jax.ShapeDtypeStruct((copies, 2, tok, dim), jnp.bfloat16),
        ],
    )(index, tokens, norm_gain[None, :], w_key, w_value, key_gain[None, :], cosine, sine)


def _route_kernel(index_ref, terms_ref, tok_ref, gain_ref, src_ref, resid_ref, out_ref):
    attn = terms_ref[0].astype(jnp.float32)
    for i in range(1, terms_ref.shape[0]):
        attn = attn + terms_ref[i].astype(jnp.float32)
    resid = tok_ref[...].astype(jnp.float32) + attn
    resid_ref[...] = resid
    routed = (
        resid * lax.rsqrt(jnp.mean(resid * resid, axis=1, keepdims=True) + EPSILON) * gain_ref[...]
    ).astype(jnp.bfloat16)
    out_ref[...] = jnp.dot(src_ref[...], routed, preferred_element_type=jnp.float32).astype(out_ref.dtype)


def route(index, terms, tokens, gain, sources):
    parts, rows, width = terms.shape
    slots = sources.shape[0]
    spec = pltpu.PrefetchScalarGridSpec(
        num_scalar_prefetch=1,
        grid=(1,),
        in_specs=[
            pl.BlockSpec((parts, rows, width), lambda i, b: (0, 0, 0)),
            pl.BlockSpec((rows, width), lambda i, b: (b[0], 0)),
            pl.BlockSpec((1, width), lambda i, b: (0, 0)),
            pl.BlockSpec((slots, rows), lambda i, b: (0, 0)),
        ],
        out_specs=[
            pl.BlockSpec((rows, width), lambda i, b: (0, 0)),
            pl.BlockSpec((slots, width), lambda i, b: (0, 0)),
        ],
    )
    return pl.pallas_call(
        _route_kernel,
        grid_spec=spec,
        out_shape=[
            jax.ShapeDtypeStruct((rows, width), jnp.float32),
            jax.ShapeDtypeStruct((slots, width), jnp.bfloat16),
        ],
    )(index, terms, tokens, gain[None, :], sources)


def local(
    tokens,
    norm_gain,
    w_query,
    w_key,
    w_value,
    query_gain,
    key_gain,
    w_out,
    post_gain,
    doc_lengths,
    expert_ids,
    route_weights,
    w_gate,
    w_up,
    w_down,
):
    tok_dev, width = tokens.shape
    head_dim = query_gain.shape[0]
    per_dev = w_query.shape[1] // head_dim
    n_seq = lax.axis_size("seq")
    n_head = lax.axis_size("head")
    seq_index = lax.axis_index("seq")
    head_index = lax.axis_index("head")
    ndocs = doc_lengths.shape[0]
    ends = jnp.cumsum(doc_lengths)
    starts = ends - doc_lengths
    positions = seq_index * tok_dev + jnp.arange(tok_dev, dtype=jnp.int32)
    query_doc = doc_index(positions, ends)
    matches = query_doc[:, None] == jnp.arange(ndocs, dtype=jnp.int32)[None, :]
    own_start = jnp.sum(jnp.where(matches, starts[None, :], 0), axis=1)
    offset = (positions - own_start).astype(jnp.float32)
    half = head_dim // 2
    inverse = THETA ** (-2.0 * jnp.arange(half, dtype=jnp.float32) / head_dim)
    angles = offset[:, None] * inverse[None, :]
    cosine = jnp.cos(angles)
    sine = jnp.sin(angles)
    cosine2 = jnp.concatenate([cosine, cosine], axis=-1)
    sine2 = jnp.concatenate([-sine, sine], axis=-1)
    pairs = n_seq // 2
    groups = [[2 * i + c for i in range(pairs)] for c in range(2)]
    kv_head = jnp.reshape(head_index * per_dev // (HEADS // KV_HEADS), (1,)).astype(jnp.int32)
    normed, spread = project(kv_head, tokens, norm_gain, w_key, w_value, key_gain, cosine2, sine2, pairs)
    queries = jnp.dot(normed, w_query, preferred_element_type=jnp.float32)
    same_core = lax.all_to_all(spread, "seq", 0, 0, tiled=True, axis_index_groups=groups)
    block = 2 * tok_dev
    low = own_start[0] // block
    high = positions[-1] // block + 1
    inner_low = jnp.clip(-(-own_start[-1] // block), low, high)
    inner_high = jnp.clip((positions[0] + 1) // block, inner_low, high)
    bounds = jnp.stack([low, inner_low, inner_high, high, seq_index % 2]).astype(jnp.int32)
    operands = (
        bounds,
        queries,
        cosine2,
        sine2,
        query_gain[None, :],
        jnp.tile(positions[:, None], (per_dev, 1)),
        jnp.tile(own_start[:, None], (per_dev, 1)),
    )
    operands, same_core = lax.optimization_barrier((operands, same_core))
    other_core = lax.ppermute(same_core, "seq", [(i, i ^ 1) for i in range(n_seq)])
    bounds, queries, cosine2, sine2, gain, qpos, qstart = operands
    terms = attend(bounds, queries, cosine2, sine2, gain, same_core, other_core, qpos, qstart, w_out)
    rows = tok_dev // n_head
    terms = lax.all_to_all(terms.reshape(n_head, rows, width), "head", 0, 0, tiled=True)
    experts = n_seq * n_head * w_gate.shape[0]
    capacity = 2 * TOP * rows // experts
    chosen = expert_ids.reshape(-1)
    hits = (chosen[:, None] == jnp.arange(experts, dtype=jnp.int32)[None, :]).astype(jnp.int32)
    rank = jnp.sum((jnp.cumsum(hits, axis=0) - hits) * hits, axis=1)
    slot = rank * experts + chosen
    select = (slot[:, None] == jnp.arange(capacity * experts, dtype=jnp.int32)[None, :]).reshape(
        rows, TOP, capacity * experts
    )
    sources = jnp.transpose(jnp.any(select, axis=1)).astype(jnp.bfloat16)
    resid, outgoing = route(jnp.reshape(head_index, (1,)).astype(jnp.int32), terms, tokens, post_gain, sources)
    outgoing = outgoing.reshape(capacity, experts, width)
    block = lax.all_to_all(outgoing, ("seq", "head"), split_axis=1, concat_axis=1, tiled=True)
    flat = block.reshape(-1, width)
    gate = jnp.dot(flat, w_gate[0], preferred_element_type=jnp.float32)
    up = jnp.dot(flat, w_up[0], preferred_element_type=jnp.float32)
    gate, up = lax.optimization_barrier((gate, up))
    hidden = (jax.nn.silu(gate) * up).astype(jnp.bfloat16)
    returned = lax.all_to_all(
        jnp.dot(hidden, w_down[0], preferred_element_type=jnp.float32)
        .astype(jnp.bfloat16)
        .reshape(block.shape),
        ("seq", "head"),
        split_axis=1,
        concat_axis=1,
        tiled=True,
    ).reshape(-1, width)
    mixing = jnp.sum(jnp.where(select, route_weights[:, :, None], 0.0), axis=1)
    combined = jnp.dot(
        mixing, returned.astype(jnp.float32), precision=lax.Precision.HIGHEST,
        preferred_element_type=jnp.float32,
    )
    return (resid + combined).astype(jnp.bfloat16)


def solution(mesh):
    placed = (
        P("seq", None),
        P(),
        P(None, "head"),
        P(),
        P(),
        P(),
        P(),
        P("head", None),
        P(),
        P(),
        P(("seq", "head"), None),
        P(("seq", "head"), None),
        P(("seq", "head"), None, None),
        P(("seq", "head"), None, None),
        P(("seq", "head"), None, None),
    )
    return jax.shard_map(
        local, mesh=mesh, in_specs=placed, out_specs=P(("seq", "head"), None), check_vma=False
    )
```

```python
import functools
import math

import jax
import jax.numpy as jnp
from jax import lax
from jax.experimental import pallas as pl
from jax.experimental.pallas import tpu as pltpu
from jax.sharding import PartitionSpec as P

HEADS = 32
KV_HEADS = 4
TOP = 8


EPSILON = 1e-06
THETA = 1000000.0
FLOOR = -1e30


def rms_scale(values, gain):
    return values * lax.rsqrt(jnp.mean(values * values, axis=-1, keepdims=True) + EPSILON) * gain


def rotate(values, cosine, sine):
    half = values.shape[-1] // 2
    first = values[..., :half]
    second = values[..., half:]
    return jnp.concatenate(
        [first * cosine - second * sine, second * cosine + first * sine], axis=-1
    )


def doc_index(positions, ends):
    return jnp.sum((positions[:, None] >= ends[None, :]).astype(jnp.int32), axis=1)


def _attend_kernel(
    bounds_ref, q_ref, cos_ref, sin_ref, gain_ref, own_ref, other_ref, w_ref, o_ref, *, dim
):
    heads = q_ref.shape[1] // dim
    tok = q_ref.shape[0]
    block = 2 * own_ref.shape[2]
    parts = []
    for h in range(heads):
        part = q_ref[:, h * dim : (h + 1) * dim]
        part = part * lax.rsqrt(jnp.mean(part * part, axis=1, keepdims=True) + EPSILON) * gain_ref[...]
        part = part * cos_ref[...] + pltpu.roll(part, dim // 2, 1) * sin_ref[...]
        parts.append(part.astype(jnp.bfloat16))
    q = jnp.concatenate(parts, axis=0)
    row = lax.broadcasted_iota(jnp.int32, (heads * tok, 1), 0)
    qpos = bounds_ref[5] + row % tok
    qstart = jnp.zeros_like(qpos)
    for d in range(6, bounds_ref.shape[0]):
        qstart = jnp.maximum(qstart, jnp.where(bounds_ref[d] <= qpos, bounds_ref[d], 0))
    scale = dim ** (-0.5)

    def step(j, carry, masked):
        high, total, accum = carry
        even = bounds_ref[4] == 0
        keys = jnp.concatenate(
            [jnp.where(even, own_ref[j, 0], other_ref[j, 0]), jnp.where(even, other_ref[j, 0], own_ref[j, 0])],
            axis=0,
        )
        values = jnp.concatenate(
            [jnp.where(even, own_ref[j, 1], other_ref[j, 1]), jnp.where(even, other_ref[j, 1], own_ref[j, 1])],
            axis=0,
        )
        scores = lax.dot_general(q, keys, (((1,), (1,)), ((), ())), preferred_element_type=jnp.float32) * scale
        if masked:
            key_pos = j * block + lax.broadcasted_iota(jnp.int32, (1, block), 1)
            allowed = (key_pos >= qstart) & (key_pos <= qpos)
            scores = jnp.where(allowed, scores, FLOOR)
        new_high = jnp.maximum(high, jnp.max(scores, axis=1, keepdims=True))
        weights = jnp.exp(scores - new_high)
        if masked:
            weights = jnp.where(allowed, weights, 0.0)
        factor = jnp.exp(high - new_high)
        total = total * factor + jnp.sum(weights, axis=1, keepdims=True)
        accum = accum * factor + jnp.dot(
            weights.astype(jnp.bfloat16), values, preferred_element_type=jnp.float32
        )
        return new_high, total, accum

    carry = (
        jnp.full((heads * tok, 1), FLOOR, jnp.float32),
        jnp.zeros((heads * tok, 1), jnp.float32),
        jnp.zeros((heads * tok, dim), jnp.float32),
    )
    carry = lax.fori_loop(bounds_ref[0], bounds_ref[1], lambda j, c: step(j, c, True), carry)
    carry = lax.fori_loop(bounds_ref[1], bounds_ref[2], lambda j, c: step(j, c, False), carry)
    carry = lax.fori_loop(bounds_ref[2], bounds_ref[3], lambda j, c: step(j, c, True), carry)
    high, total, accum = carry
    out = (accum / total).astype(jnp.bfloat16)
    terms = jnp.dot(out[:tok], w_ref[:dim, :], preferred_element_type=jnp.float32)
    for h in range(1, heads):
        terms = terms + jnp.dot(
            out[h * tok : (h + 1) * tok], w_ref[h * dim : (h + 1) * dim, :], preferred_element_type=jnp.float32
        )
    o_ref[...] = terms.astype(o_ref.dtype)


def attend(bounds, queries, cosine, sine, gain, own, other, w_out):
    tok, width = queries.shape
    dim = own.shape[-1]
    kernel = functools.partial(_attend_kernel, dim=dim)
    spec = pltpu.PrefetchScalarGridSpec(
        num_scalar_prefetch=1,
        grid=(1,),
        in_specs=[
            pl.BlockSpec((tok, width), lambda i, b: (0, 0)),
            pl.BlockSpec(cosine.shape, lambda i, b: (0, 0)),
            pl.BlockSpec(sine.shape, lambda i, b: (0, 0)),
            pl.BlockSpec(gain.shape, lambda i, b: (0, 0)),
            pl.BlockSpec(own.shape, lambda i, b: (0, 0, 0, 0)),
            pl.BlockSpec(other.shape, lambda i, b: (0, 0, 0, 0)),
            pl.BlockSpec(w_out.shape, lambda i, b: (0, 0)),
        ],
        out_specs=pl.BlockSpec((tok, w_out.shape[1]), lambda i, b: (0, 0)),
    )
    return pl.pallas_call(
        kernel, grid_spec=spec, out_shape=jax.ShapeDtypeStruct((tok, w_out.shape[1]), jnp.bfloat16)
    )(bounds, queries, cosine, sine, gain, own, other, w_out)


def _project_kernel(
    index_ref, x_ref, ngain_ref, wk_ref, wv_ref, kgain_ref, cos_ref, sin_ref, normed_ref, spread_ref
):
    x = x_ref[...].astype(jnp.float32)
    normed = (x * lax.rsqrt(jnp.mean(x * x, axis=1, keepdims=True) + EPSILON) * ngain_ref[...]).astype(
        jnp.bfloat16
    )
    normed_ref[...] = normed
    keys = jnp.dot(normed, wk_ref[...], preferred_element_type=jnp.float32)
    keys = keys * lax.rsqrt(jnp.mean(keys * keys, axis=1, keepdims=True) + EPSILON) * kgain_ref[...]
    keys = keys * cos_ref[...] + pltpu.roll(keys, keys.shape[1] // 2, 1) * sin_ref[...]
    keys = keys.astype(jnp.bfloat16)
    values = jnp.dot(normed, wv_ref[...], preferred_element_type=jnp.float32).astype(jnp.bfloat16)
    for i in range(spread_ref.shape[0]):
        spread_ref[i, 0] = keys
        spread_ref[i, 1] = values


def project(index, tokens, norm_gain, w_key, w_value, key_gain, cosine, sine, copies):
    tok, width = tokens.shape
    dim = key_gain.shape[0]
    spec = pltpu.PrefetchScalarGridSpec(
        num_scalar_prefetch=1,
        grid=(1,),
        in_specs=[
            pl.BlockSpec((tok, width), lambda i, b: (0, 0)),
            pl.BlockSpec((1, width), lambda i, b: (0, 0)),
            pl.BlockSpec((width, dim), lambda i, b: (0, b[0])),
            pl.BlockSpec((width, dim), lambda i, b: (0, b[0])),
            pl.BlockSpec((1, dim), lambda i, b: (0, 0)),
            pl.BlockSpec((tok, dim), lambda i, b: (0, 0)),
            pl.BlockSpec((tok, dim), lambda i, b: (0, 0)),
        ],
        out_specs=[
            pl.BlockSpec((tok, width), lambda i, b: (0, 0)),
            pl.BlockSpec((copies, 2, tok, dim), lambda i, b: (0, 0, 0, 0)),
        ],
    )
    return pl.pallas_call(
        _project_kernel,
        grid_spec=spec,
        out_shape=[
            jax.ShapeDtypeStruct((tok, width), jnp.bfloat16),
            jax.ShapeDtypeStruct((copies, 2, tok, dim), jnp.bfloat16),
        ],
    )(index, tokens, norm_gain[None, :], w_key, w_value, key_gain[None, :], cosine, sine)


def local(
    tokens,
    norm_gain,
    w_query,
    w_key,
    w_value,
    query_gain,
    key_gain,
    w_out,
    post_gain,
    doc_lengths,
    expert_ids,
    route_weights,
    w_gate,
    w_up,
    w_down,
):
    tok_dev, width = tokens.shape
    head_dim = query_gain.shape[0]
    per_dev = w_query.shape[1] // head_dim
    n_seq = lax.axis_size("seq")
    n_head = lax.axis_size("head")
    seq_index = lax.axis_index("seq")
    head_index = lax.axis_index("head")
    ndocs = doc_lengths.shape[0]
    ends = jnp.cumsum(doc_lengths)
    starts = ends - doc_lengths
    positions = seq_index * tok_dev + jnp.arange(tok_dev, dtype=jnp.int32)
    query_doc = doc_index(positions, ends)
    matches = query_doc[:, None] == jnp.arange(ndocs, dtype=jnp.int32)[None, :]
    own_start = jnp.sum(jnp.where(matches, starts[None, :], 0), axis=1)
    offset = (positions - own_start).astype(jnp.float32)
    half = head_dim // 2
    inverse = THETA ** (-2.0 * jnp.arange(half, dtype=jnp.float32) / head_dim)
    angles = offset[:, None] * inverse[None, :]
    cosine = jnp.cos(angles)
    sine = jnp.sin(angles)
    cosine2 = jnp.concatenate([cosine, cosine], axis=-1)
    sine2 = jnp.concatenate([-sine, sine], axis=-1)
    pairs = n_seq // 2
    groups = [[2 * i + c for i in range(pairs)] for c in range(2)]
    kv_head = jnp.reshape(head_index * per_dev // (HEADS // KV_HEADS), (1,)).astype(jnp.int32)
    normed, spread = project(kv_head, tokens, norm_gain, w_key, w_value, key_gain, cosine2, sine2, pairs)
    queries = jnp.dot(normed, w_query, preferred_element_type=jnp.float32)
    same_core = lax.all_to_all(spread, "seq", 0, 0, tiled=True, axis_index_groups=groups)
    block = 2 * tok_dev
    low = own_start[0] // block
    high = positions[-1] // block + 1
    inner_low = jnp.clip(-(-own_start[-1] // block), low, high)
    inner_high = jnp.clip((positions[0] + 1) // block, inner_low, high)
    bounds = jnp.concatenate(
        [jnp.stack([low, inner_low, inner_high, high, seq_index % 2, positions[0]]), starts]
    ).astype(jnp.int32)
    operands = (
        bounds,
        queries,
        cosine2,
        sine2,
        query_gain[None, :],
    )
    operands, same_core = lax.optimization_barrier((operands, same_core))
    other_core = lax.ppermute(same_core, "seq", [(i, i ^ 1) for i in range(n_seq)])
    bounds, queries, cosine2, sine2, gain = operands
    terms = attend(bounds, queries, cosine2, sine2, gain, same_core, other_core, w_out)
    rows = tok_dev // n_head
    terms = lax.all_to_all(terms.reshape(n_head, rows, width), "head", 0, 0, tiled=True)
    attn_rows = jnp.sum(terms.astype(jnp.float32), axis=0)
    resid = lax.dynamic_slice_in_dim(tokens, head_index * rows, rows, 0).astype(jnp.float32) + attn_rows
    routed = rms_scale(resid, post_gain).astype(jnp.bfloat16)
    experts = n_seq * n_head * w_gate.shape[0]
    capacity = 2 * TOP * rows // experts
    chosen = expert_ids.reshape(-1)
    hits = (chosen[:, None] == jnp.arange(experts, dtype=jnp.int32)[None, :]).astype(jnp.int32)
    rank = jnp.sum((jnp.cumsum(hits, axis=0) - hits) * hits, axis=1)
    slot = rank * experts + chosen
    select = (slot[:, None] == jnp.arange(capacity * experts, dtype=jnp.int32)[None, :]).reshape(
        rows, TOP, capacity * experts
    )
    sources = jnp.transpose(jnp.any(select, axis=1)).astype(jnp.bfloat16)
    outgoing = jnp.dot(sources, routed, preferred_element_type=jnp.float32).astype(jnp.bfloat16)
    outgoing = outgoing.reshape(capacity, experts, width)
    block = lax.all_to_all(outgoing, ("seq", "head"), split_axis=1, concat_axis=1, tiled=True)
    flat = block.reshape(-1, width)
    gate = jnp.dot(flat, w_gate[0], preferred_element_type=jnp.float32)
    up = jnp.dot(flat, w_up[0], preferred_element_type=jnp.float32)
    gate, up = lax.optimization_barrier((gate, up))
    hidden = (jax.nn.silu(gate) * up).astype(jnp.bfloat16)
    returned = lax.all_to_all(
        jnp.dot(hidden, w_down[0], preferred_element_type=jnp.float32)
        .astype(jnp.bfloat16)
        .reshape(block.shape),
        ("seq", "head"),
        split_axis=1,
        concat_axis=1,
        tiled=True,
    ).reshape(-1, width)
    mixing = jnp.sum(jnp.where(select, route_weights[:, :, None], 0.0), axis=1)
    combined = jnp.dot(
        mixing, returned.astype(jnp.float32), precision=lax.Precision.HIGHEST,
        preferred_element_type=jnp.float32,
    )
    return (resid + combined).astype(jnp.bfloat16)


def solution(mesh):
    placed = (
        P("seq", None),
        P(),
        P(None, "head"),
        P(),
        P(),
        P(),
        P(),
        P("head", None),
        P(),
        P(),
        P(("seq", "head"), None),
        P(("seq", "head"), None),
        P(("seq", "head"), None, None),
        P(("seq", "head"), None, None),
        P(("seq", "head"), None, None),
    )
    return jax.shard_map(
        local, mesh=mesh, in_specs=placed, out_specs=P(("seq", "head"), None), check_vma=False
    )
```
